32 devices in a mesh: seq: 8 (over y, x, core), head: 4 (over z).
Axes of the slice: x: 2, y: 2, z: 4, core: 2. Of those that a mesh axis runs over, the one named last changes fastest.
Arguments:
- inner_rows: bfloat16 [2048, 4096], P('seq', 'head'), may hold values from -6 to 6
- gate_rows: bfloat16 [2048, 4096], P('seq', 'head'), may hold values from -6 to 6
- input_proj: bfloat16 [2048, 512], P('seq'), may hold values from -6 to 6
- step_raw: float32 [2048, 64], P('seq', 'head'), may hold values from -8 to 8
- decay_rate: float32 [64], P('head'), may hold values from 1e-05 to 0.08
- skip_gain: float32 [64], P('head'), may hold values from 0.5 to 1.5
- conv_inner: float32 [4, 4096], P(None, 'head'), may hold values from -3 to 3
- conv_proj: float32 [4, 512], replicated, may hold values from -0.25 to 0.25
- norm_gain: float32 [4096], P('head'), may hold values from 0.1 to 1.9
Outputs:
- mixed_out: bfloat16 [2048, 4096], P('seq', 'head')
The draws below stay inside these ranges and needn't reach their ends.
All inputs are finite; a program needn't handle non-finite values.
Results may differ from the reference program's by a relative error of at most 0.0062.
Values may be sent and summed in bfloat16 or wider, within the bound.
No kernel may reach another device: no remote copies, remote signals or barrier semaphores. Data moves between devices by JAX's collectives and lax.ppermute only.
A program may use at most 64 MiB of HBM per device.

```python
import math
import jax
import jax.numpy as jnp
from jax import lax

HEAD_SIZE = 64
STATE = 128
GROUP_HEADS = 32
KERNEL = 4
TOK_DEV = 256
BLK = 128
TOKENS = 2048
HEADS = 64
GROUPS = 2
XCH = 4096
BCH = 512
N_SEQ = 8


def draw_step_raw(key, part):
    first_key, second_key, third_key, fourth_key = jax.random.split(key, 4)
    base = jax.random.normal(first_key, (TOKENS, HEADS), jnp.float32)
    offset = jax.random.uniform(second_key, (TOKENS // BLK, 1, HEADS), jnp.float32, -4.0, 3.0)
    rows_idx = jnp.arange(TOKENS, dtype=jnp.int32)
    device = rows_idx // TOK_DEV
    within = rows_idx % TOK_DEV
    block = jnp.where(within < BLK, device, 2 * (TOKENS // TOK_DEV) - 1 - device)
    position = (block * BLK + within % BLK).astype(jnp.float32)
    amplitude = jax.random.uniform(third_key, (1, HEADS), jnp.float32, 1.5, 2.5)
    phase = jax.random.uniform(fourth_key, (1, HEADS), jnp.float32, 0.0, 2.0 * math.pi)
    trend = amplitude * jnp.sin(2.0 * math.pi * position[:, None] / TOKENS + phase)
    value = (base.reshape(TOKENS // BLK, BLK, HEADS) + offset).reshape(TOKENS, HEADS) + trend
    return jnp.clip(value, -8.0, 8.0)


def draw_decay_rate(key, part):
    first_key, second_key, third_key = jax.random.split(key, 3)
    slow_heads = jax.random.bernoulli(first_key, 0.5, (HEADS,))
    slow_rate = jnp.exp(jax.random.uniform(second_key, (HEADS,), jnp.float32, math.log(1e-05), math.log(8e-05)))
    other_rate = jnp.exp(jax.random.uniform(third_key, (HEADS,), jnp.float32, math.log(0.0002), math.log(0.08)))
    return jnp.where(slow_heads, slow_rate, other_rate)


def level_of(stream_key, dims, cuts, smallest, high):
    loudness, own = 1.0, jax.random.fold_in(stream_key, 6)
    for axis_at, blocks in cuts:
        heights = jnp.exp(jax.random.uniform(jax.random.fold_in(own, axis_at), (blocks,), jnp.float32, smallest / len(cuts), high / len(cuts)))
        loudness = loudness * jnp.repeat(heights, dims[axis_at] // blocks).reshape([-1 if axis == axis_at else 1 for axis in range(len(dims))])
    return loudness


def scatter_about(stream_key, dims, scale, bound, cuts=(), kind=jnp.bfloat16):
    entries = scale * jax.random.normal(stream_key, dims, jnp.float32)
    if cuts:
        entries = entries * level_of(stream_key, dims, cuts, -0.22, 0.18)
    return jnp.clip(entries, -bound, bound).astype(kind)


def setup_inputs(seed: int = 0) -> dict:
    seeds = jax.random.split(jax.random.key(seed), 10)
    return {
        "inner_rows": scatter_about(seeds[0], (TOKENS, XCH), 1.0, 6.0, ((0, 8), (1, 4))),
        "gate_rows": scatter_about(seeds[1], (TOKENS, XCH), 1.0, 6.0, ((0, 8), (1, 4))),
        "input_proj": scatter_about(seeds[2], (TOKENS, BCH), 1.0, 6.0, ((0, 8),)),
        "step_raw": draw_step_raw(jax.random.fold_in(seeds[9], 71), 0),
        "decay_rate": draw_decay_rate(jax.random.fold_in(seeds[9], 71), 0),
        "skip_gain": jnp.clip(0.5 + 1.0 * jax.random.uniform(seeds[5], (HEADS,), jnp.float32) ** level_of(seeds[5], (HEADS,), ((0, 4),), -0.2, 0.2), 0.5, 1.5),
        "conv_inner": scatter_about(seeds[6], (KERNEL, XCH), KERNEL ** -0.5, 3.0, ((1, 4),), jnp.float32),
        "conv_proj": scatter_about(seeds[7], (KERNEL, BCH), (KERNEL * STATE) ** -0.5, 0.25, (), jnp.float32),
        "norm_gain": jnp.clip(1.0 + 0.18 * jax.random.normal(seeds[8], (XCH,), jnp.float32), 0.1, 1.9),
    }


def reference(inner_rows, gate_rows, input_proj, step_raw, decay_rate, skip_gain, conv_inner, conv_proj, norm_gain):
    rows_idx = jnp.arange(TOKENS, dtype=jnp.int32)
    device = rows_idx // TOK_DEV
    within = rows_idx % TOK_DEV
    block = jnp.where(within < BLK, device, 2 * N_SEQ - 1 - device)
    position = (block * BLK + within % BLK).astype(jnp.int32)
    order = jnp.zeros((TOKENS,), jnp.int32).at[position].set(rows_idx)
    count = 2 * N_SEQ
    joined = jnp.concatenate([inner_rows, input_proj], axis=1)[order].reshape(count, BLK, XCH + BCH)
    gates = gate_rows[order].reshape(count, BLK, XCH)
    steps_dt = jax.nn.softplus(step_raw[order]).reshape(count, BLK, HEADS)
    conv_taps = jnp.concatenate([conv_inner, conv_proj], axis=1)
    causal = jnp.arange(BLK)[:, None] >= jnp.arange(BLK)[None, :]

    def advance(carry, inputs):
        lead_rows, carry_state = carry
        rows_in, gate_block, step_size = inputs
        padded = jnp.concatenate([lead_rows, rows_in], axis=0).astype(jnp.float32)
        conv_sum = jnp.zeros((BLK, XCH + BCH), jnp.float32)
        for offset in range(KERNEL):
            conv_sum = conv_sum + conv_taps[offset][None, :] * padded[offset:offset + BLK]
        conv_out = jax.nn.silu(conv_sum).astype(jnp.bfloat16)
        inner_conv = conv_out[:, :XCH].reshape(BLK, HEADS, HEAD_SIZE)
        b_rows = conv_out[:, XCH:XCH + GROUPS * STATE].reshape(BLK, GROUPS, STATE)
        c_rows = conv_out[:, XCH + GROUPS * STATE:].reshape(BLK, GROUPS, STATE)
        log_step = -step_size * decay_rate[None, :]
        log_cum = jnp.cumsum(log_step, axis=0)
        score_grid = jnp.einsum('tgn,sgn->gts', c_rows.astype(jnp.float32), b_rows.astype(jnp.float32))
        score_heads = jnp.repeat(score_grid, GROUP_HEADS, axis=0)
        log_gap = log_cum.T[:, :, None] - log_cum.T[:, None, :]
        decay_grid = jnp.where(causal[None], jnp.exp(jnp.where(causal[None], log_gap, 0.0)), 0.0)
        weights = (score_heads * decay_grid * step_size.T[:, None, :]).astype(jnp.bfloat16)
        intra_out = jnp.einsum('hts,shp->thp', weights.astype(jnp.float32), inner_conv.astype(jnp.float32))
        tail_decay = jnp.exp(log_cum[-1][None, :] - log_cum) * step_size
        x_weighted = (inner_conv.astype(jnp.float32) * tail_decay[:, :, None]).astype(jnp.bfloat16)
        b_heads = jnp.repeat(b_rows, GROUP_HEADS, axis=1).astype(jnp.float32)
        c_heads = jnp.repeat(c_rows, GROUP_HEADS, axis=1).astype(jnp.float32)
        local_state = jnp.einsum('shp,shn->hpn', x_weighted.astype(jnp.float32), b_heads)
        inter_out = jnp.exp(log_cum)[:, :, None] * jnp.einsum('thn,hpn->thp', c_heads, carry_state, precision=lax.Precision.HIGHEST)
        ssm_out = intra_out + inter_out + skip_gain[None, :, None] * inner_conv.astype(jnp.float32)
        new_state = jnp.exp(log_cum[-1])[:, None, None] * carry_state + local_state
        gated = ssm_out.reshape(BLK, XCH) * jax.nn.silu(gate_block.astype(jnp.float32))
        grouped = gated.reshape(BLK, GROUPS, GROUP_HEADS * HEAD_SIZE)
        mean_sq = lax.optimization_barrier(jnp.mean(grouped * grouped, axis=-1, keepdims=True))
        normed = (grouped * lax.rsqrt(mean_sq + 1e-05)).reshape(BLK, XCH) * norm_gain[None, :]
        return ((rows_in[BLK - (KERNEL - 1):], new_state), normed.astype(jnp.bfloat16))
    init = (jnp.zeros((KERNEL - 1, XCH + BCH), jnp.bfloat16), jnp.zeros((HEADS, HEAD_SIZE, STATE), jnp.float32))
    _, outputs = lax.scan(advance, init, (joined, gates, steps_dt))
    return outputs.reshape(TOKENS, XCH)[position]
```

```python
import jax
import jax.numpy as jnp
from jax import lax
from jax.sharding import PartitionSpec as P

HEAD_SIZE = 64
STATE = 128
GROUP_HEADS = 32
KERNEL = 4


def extended_2(block, sides, width):
    for axis, dim in sides:
        count = lax.axis_size(axis)
        forward = [(i, i + 1) for i in range(count - 1)]
        backward = [(target, source) for source, target in forward]
        low = lax.ppermute(
            lax.slice_in_dim(block, block.shape[dim] - width, None, axis=dim), axis, forward
        )
        high = lax.ppermute(lax.slice_in_dim(block, 0, width, axis=dim), axis, backward)
        block = jnp.concatenate([low, block, high], axis=dim)
    return block


def partner(array, axis, stride):
    return lax.ppermute(array, axis, [(i, i ^ 1 << stride) for i in range(lax.axis_size(axis))])


def butterfly_states(first_loc, second_loc, first_log, second_log, seq_pos, seq_count):
    levels = seq_count.bit_length() - 1
    assert 1 << levels == seq_count
    heads = first_loc.shape[0]
    both = lax.all_gather(jnp.stack([first_log, second_log]), "seq")
    block_log = jnp.concatenate([both[:, 0], both[::-1, 1]], axis=0)
    block_ids = jnp.arange(2 * seq_count)[:, None]

    def span(lo, hi):
        inside = (block_ids >= lo) & (block_ids < hi)
        return jnp.exp(jnp.sum(jnp.where(inside, block_log, 0.0), axis=0))[:, None, None]

    def pick(cond, yes, no):
        return jnp.where(cond, yes, no)

    last = 2 * seq_count
    prefix = jnp.zeros_like(first_loc)
    above = jnp.zeros_like(first_loc)
    sub_f, sub_g = first_loc, second_loc
    one = jnp.ones((heads, 1, 1), jnp.float32)
    zero = jnp.zeros((heads, 1, 1), jnp.float32)
    for level in range(levels):
        size = 1 << level
        lo = seq_pos - seq_pos % size
        hi = lo + size
        lower = (seq_pos // size) % 2 == 0
        part_lo = jnp.where(lower, hi, lo - size)
        part_hi = part_lo + size
        pairs = [(i, i ^ size) for i in range(seq_count)]
        e_prefix = span(lo, seq_pos)
        e_above = span(last - hi, last - 1 - seq_pos)
        e_f = span(lo, hi)
        e_g = span(last - hi, last - lo)
        if level < levels - 1:
            got_f, got_g = lax.ppermute((sub_f, sub_g), "seq", pairs)
            e_pf = span(part_lo, part_hi)
            e_pg = span(last - part_hi, last - part_lo)
            new_f = pick(lower, e_pf, one) * sub_f + pick(lower, one, e_f) * got_f
            new_g = pick(lower, one, e_pg) * sub_g + pick(lower, e_g, one) * got_g
            above = above + pick(lower, e_above, zero) * got_g
            prefix = prefix + pick(lower, zero, e_prefix) * got_f
            sub_f, sub_g = new_f, new_g
        else:
            message = pick(lower, one, e_g) * sub_f + pick(lower, zero, one) * sub_g
            got = lax.ppermute(message, "seq", pairs)
            e_pw = span(part_lo, part_hi) * span(last - part_hi, last - part_lo)
            first_in = prefix + pick(lower, zero, e_prefix) * got
            second_in = (
                above
                + pick(lower, e_above * e_pw, e_above) * sub_f
                + pick(lower, e_above, e_above * e_f) * got
            )
    return first_in, second_in


def on_device(
    inner_rows,
    gate_rows,
    input_proj,
    step_raw,
    decay_rate,
    skip_gain,
    conv_inner,
    conv_proj,
    norm_gain,
):
    tokens = inner_rows.shape[0]
    half_rows = tokens // 2
    head_count = step_raw.shape[1]
    inner_width = inner_rows.shape[1]
    group_count = input_proj.shape[1] // (2 * STATE)
    rim_rows = KERNEL - 1
    seq_count = lax.axis_size("seq")
    seq_pos = lax.axis_index("seq")
    is_last = seq_pos == seq_count - 1
    my_group = lax.axis_index("head") * head_count // GROUP_HEADS
    joined = jnp.concatenate([inner_rows, input_proj], axis=1)
    edge_rows = jnp.concatenate(
        [joined[tokens - rim_rows :], joined[half_rows - rim_rows : half_rows]], axis=0
    )
    extended = extended_2(edge_rows, (("seq", 0),), rim_rows)
    lead_first = extended[:rim_rows]
    lead_second = jnp.where(
        is_last, joined[half_rows - rim_rows : half_rows], extended[3 * rim_rows :]
    )
    conv_taps = jnp.concatenate([conv_inner, conv_proj], axis=1)
    step_size = jax.nn.softplus(step_raw)
    causal = jnp.arange(half_rows)[:, None] >= jnp.arange(half_rows)[None, :]

    def local_block(lead_rows, rows_in, block_step):
        padded = jnp.concatenate([lead_rows, rows_in], axis=0).astype(jnp.float32)
        conv_sum = jnp.zeros((half_rows, joined.shape[1]), jnp.float32)
        for offset in range(KERNEL):
            conv_sum = conv_sum + conv_taps[offset][None, :] * padded[offset : offset + half_rows]
        conv_out = jax.nn.silu(conv_sum).astype(jnp.bfloat16)
        inner_conv = conv_out[:, :inner_width].reshape(half_rows, head_count, HEAD_SIZE)
        b_rows = lax.dynamic_slice_in_dim(conv_out, inner_width + my_group * STATE, STATE, 1)
        c_rows = lax.dynamic_slice_in_dim(
            conv_out, inner_width + (group_count + my_group) * STATE, STATE, 1
        )
        log_cum = jnp.cumsum(-block_step * decay_rate[None, :], axis=0)
        score_grid = jnp.dot(c_rows, b_rows.T, preferred_element_type=jnp.float32)
        log_gap = log_cum.T[:, :, None] - log_cum.T[:, None, :]
        decay_grid = jnp.where(causal[None], jnp.exp(jnp.where(causal[None], log_gap, 0.0)), 0.0)
        weights = (score_grid[None] * decay_grid * block_step.T[:, None, :]).astype(jnp.bfloat16)
        intra_out = jnp.einsum(
            "hts,shp->thp", weights, inner_conv, preferred_element_type=jnp.float32
        )
        tail_decay = jnp.exp(log_cum[-1][None, :] - log_cum) * block_step
        x_weighted = (inner_conv.astype(jnp.float32) * tail_decay[:, :, None]).astype(jnp.bfloat16)
        local_state = jnp.einsum(
            "shp,sn->hpn", x_weighted, b_rows, preferred_element_type=jnp.float32
        )
        partial_out = intra_out + skip_gain[None, :, None] * inner_conv.astype(jnp.float32)
        return (partial_out, log_cum, c_rows, (jnp.exp(log_cum[-1]), local_state))

    def finish_block(partial_out, log_cum, c_rows, state_in):
        inter_out = jnp.einsum(
            "tn,hpn->thp", c_rows.astype(jnp.float32), state_in, precision=lax.Precision.HIGHEST
        )
        total_out = partial_out + jnp.exp(log_cum)[:, :, None] * inter_out
        return total_out.reshape(half_rows, inner_width)

    first_out, first_cum, first_c, first_elem = local_block(
        lead_first, joined[:half_rows], step_size[:half_rows]
    )
    second_out, second_cum, second_c, second_elem = local_block(
        lead_second, joined[half_rows:], step_size[half_rows:]
    )
    first_in, second_in = butterfly_states(
        first_elem[1], second_elem[1], first_cum[-1], second_cum[-1], seq_pos, seq_count
    )
    ssm_out = jnp.concatenate(
        [
            finish_block(first_out, first_cum, first_c, first_in),
            finish_block(second_out, second_cum, second_c, second_in),
        ],
        axis=0,
    )
    gated = ssm_out * jax.nn.silu(gate_rows.astype(jnp.float32))
    partial_sq = jnp.sum(gated * gated, axis=1)
    other_sq = partner(partial_sq, "head", 0)
    mean_sq = (partial_sq + other_sq) / (GROUP_HEADS * HEAD_SIZE)
    normed = gated * lax.rsqrt(mean_sq + 1e-05)[:, None] * norm_gain[None, :]
    return normed.astype(jnp.bfloat16)


def solution(mesh):
    in_specs = (
        P("seq", "head"),
        P("seq", "head"),
        P("seq", None),
        P("seq", "head"),
        P("head"),
        P("head"),
        P(None, "head"),
        P(),
        P("head"),
    )
    out_specs = P("seq", "head")
    return jax.shard_map(
        on_device, mesh=mesh, in_specs=in_specs, out_specs=out_specs, check_vma=False
    )
```

```python
import jax
import jax.numpy as jnp
from jax import lax
from jax.sharding import PartitionSpec as P

HEAD_SIZE = 64
STATE = 128
GROUP_HEADS = 32
KERNEL = 4


def extended_2(block, sides, width):
    for axis, dim in sides:
        count = lax.axis_size(axis)
        forward = [(i, i + 1) for i in range(count - 1)]
        backward = [(target, source) for source, target in forward]
        tail, head = lax.optimization_barrier(
            (
                lax.slice_in_dim(block, block.shape[dim] - width, None, axis=dim),
                lax.slice_in_dim(block, 0, width, axis=dim),
            )
        )
        low = lax.ppermute(tail, axis, forward)
        high = lax.ppermute(head, axis, backward)
        block = jnp.concatenate([low, block, high], axis=dim)
    return block


def partner(array, axis, stride):
    return lax.ppermute(array, axis, [(i, i ^ 1 << stride) for i in range(lax.axis_size(axis))])


LINK = jnp.float32


def pack(maps, decays):
    flat = [m.reshape(-1, m.shape[-1]) for m in maps]
    lanes = flat[0].shape[1]
    rows = jnp.stack(decays)
    high = rows.astype(LINK)
    low = (rows - high.astype(jnp.float32)).astype(LINK)
    tail = jnp.concatenate([high, low], axis=0)
    tail = jnp.pad(tail, ((0, 8 - tail.shape[0]), (0, lanes - tail.shape[1])))
    return jnp.concatenate([f.astype(LINK) for f in flat] + [tail], axis=0)


def unpack(message, count, shape):
    rows = shape[0] * shape[1]
    maps = [
        message[i * rows : (i + 1) * rows].astype(jnp.float32).reshape(shape) for i in range(count)
    ]
    tail = message[count * rows :].astype(jnp.float32)
    decays = [tail[i, : shape[0]] + tail[count + i, : shape[0]] for i in range(count)]
    return maps, decays


def butterfly_states(first_loc, second_loc, first_log, second_log, seq_pos, seq_count):
    levels = seq_count.bit_length() - 1
    assert 1 << levels == seq_count
    shape = first_loc.shape
    if levels == 0:
        return jnp.zeros_like(first_loc), first_loc

    def col(v):
        return v[:, None, None]

    ones = jnp.ones((shape[0],), jnp.float32)
    zeros = jnp.zeros((shape[0],), jnp.float32)
    prefix = jnp.zeros_like(first_loc)
    above = jnp.zeros_like(first_loc)
    e_pre, e_abv = ones, ones
    sub_f, sub_g = first_loc, second_loc
    e_f, e_g = jnp.exp(first_log), jnp.exp(second_log)
    for level in range(levels):
        size = 1 << level
        lower = (seq_pos // size) % 2 == 0
        pairs = [(i, i ^ size) for i in range(seq_count)]
        if level < levels - 1:
            got = lax.ppermute(pack((sub_f, sub_g), (e_f, e_g)), "seq", pairs)
            (got_f, got_g), (p_f, p_g) = unpack(got, 2, shape)
            new_f = col(jnp.where(lower, p_f, ones)) * sub_f + col(jnp.where(lower, ones, e_f)) * got_f
            new_g = col(jnp.where(lower, ones, p_g)) * sub_g + col(jnp.where(lower, e_g, ones)) * got_g
            above = above + col(jnp.where(lower, e_abv, zeros)) * got_g
            prefix = prefix + col(jnp.where(lower, zeros, e_pre)) * got_f
            e_abv = jnp.where(lower, e_abv * p_g, e_abv)
            e_pre = jnp.where(lower, e_pre, e_pre * p_f)
            sub_f, sub_g = new_f, new_g
            e_f, e_g = e_f * p_f, e_g * p_g
        else:
            sent = col(jnp.where(lower, ones, e_g)) * sub_f + col(jnp.where(lower, zeros, ones)) * sub_g
            sent_e = jnp.where(lower, e_f, e_f * e_g)
            got = lax.ppermute(pack((sent,), (sent_e,)), "seq", pairs)
            (got_w,), (p_w,) = unpack(got, 1, shape)
            first_in = prefix + col(jnp.where(lower, zeros, e_pre)) * got_w
            second_in = (
                above
                + col(jnp.where(lower, e_abv * p_w, e_abv)) * sub_f
                + col(jnp.where(lower, e_abv, e_abv * e_f)) * got_w
            )
    return first_in, second_in


def on_device(
    inner_rows,
    gate_rows,
    input_proj,
    step_raw,
    decay_rate,
    skip_gain,
    conv_inner,
    conv_proj,
    norm_gain,
):
    tokens = inner_rows.shape[0]
    half_rows = tokens // 2
    head_count = step_raw.shape[1]
    inner_width = inner_rows.shape[1]
    group_count = input_proj.shape[1] // (2 * STATE)
    rim_rows = KERNEL - 1
    seq_count = lax.axis_size("seq")
    seq_pos = lax.axis_index("seq")
    is_last = seq_pos == seq_count - 1
    my_group = lax.axis_index("head") * head_count // GROUP_HEADS
    joined = jnp.concatenate([inner_rows, input_proj], axis=1)
    edge_rows = jnp.concatenate(
        [joined[tokens - rim_rows :], joined[half_rows - rim_rows : half_rows]], axis=0
    )
    extended = extended_2(edge_rows, (("seq", 0),), rim_rows)
    lead_first = extended[:rim_rows]
    lead_second = jnp.where(
        is_last, joined[half_rows - rim_rows : half_rows], extended[3 * rim_rows :]
    )
    conv_taps = jnp.concatenate([conv_inner, conv_proj], axis=1)
    step_size = jax.nn.softplus(step_raw)
    causal = jnp.arange(half_rows)[:, None] >= jnp.arange(half_rows)[None, :]

    def local_block(lead_rows, rows_in, block_step):
        padded = jnp.concatenate([lead_rows, rows_in], axis=0).astype(jnp.float32)
        conv_sum = jnp.zeros((half_rows, joined.shape[1]), jnp.float32)
        for offset in range(KERNEL):
            conv_sum = conv_sum + conv_taps[offset][None, :] * padded[offset : offset + half_rows]
        conv_out = jax.nn.silu(conv_sum).astype(jnp.bfloat16)
        inner_conv = conv_out[:, :inner_width].reshape(half_rows, head_count, HEAD_SIZE)
        b_rows = lax.dynamic_slice_in_dim(conv_out, inner_width + my_group * STATE, STATE, 1)
        c_rows = lax.dynamic_slice_in_dim(
            conv_out, inner_width + (group_count + my_group) * STATE, STATE, 1
        )
        log_cum = jnp.cumsum(-block_step * decay_rate[None, :], axis=0)
        score_grid = jnp.dot(c_rows, b_rows.T, preferred_element_type=jnp.float32)
        log_gap = log_cum.T[:, :, None] - log_cum.T[:, None, :]
        decay_grid = jnp.where(causal[None], jnp.exp(jnp.where(causal[None], log_gap, 0.0)), 0.0)
        weights = (score_grid[None] * decay_grid * block_step.T[:, None, :]).astype(jnp.bfloat16)
        intra_out = jnp.einsum(
            "hts,shp->thp", weights, inner_conv, preferred_element_type=jnp.float32
        )
        tail_decay = jnp.exp(log_cum[-1][None, :] - log_cum) * block_step
        x_weighted = (inner_conv.astype(jnp.float32) * tail_decay[:, :, None]).astype(jnp.bfloat16)
        local_state = jnp.einsum(
            "shp,sn->hpn", x_weighted, b_rows, preferred_element_type=jnp.float32
        )
        partial_out = intra_out + skip_gain[None, :, None] * inner_conv.astype(jnp.float32)
        return (partial_out, log_cum, c_rows, (jnp.exp(log_cum[-1]), local_state))

    def finish_block(partial_out, log_cum, c_rows, state_in):
        inter_out = jnp.einsum(
            "tn,hpn->thp", c_rows.astype(jnp.float32), state_in, precision=lax.Precision.HIGHEST
        )
        total_out = partial_out + jnp.exp(log_cum)[:, :, None] * inter_out
        return total_out.reshape(half_rows, inner_width)

    first_out, first_cum, first_c, first_elem = local_block(
        lead_first, joined[:half_rows], step_size[:half_rows]
    )
    second_out, second_cum, second_c, second_elem = local_block(
        lead_second, joined[half_rows:], step_size[half_rows:]
    )
    first_in, second_in = butterfly_states(
        first_elem[1], second_elem[1], first_cum[-1], second_cum[-1], seq_pos, seq_count
    )
    ssm_out = jnp.concatenate(
        [
            finish_block(first_out, first_cum, first_c, first_in),
            finish_block(second_out, second_cum, second_c, second_in),
        ],
        axis=0,
    )
    gated = ssm_out * jax.nn.silu(gate_rows.astype(jnp.float32))
    partial_sq = jnp.sum(gated * gated, axis=1)
    other_sq = partner(partial_sq, "head", 0)
    mean_sq = (partial_sq + other_sq) / (GROUP_HEADS * HEAD_SIZE)
    normed = gated * lax.rsqrt(mean_sq + 1e-05)[:, None] * norm_gain[None, :]
    return normed.astype(jnp.bfloat16)


def solution(mesh):
    in_specs = (
        P("seq", "head"),
        P("seq", "head"),
        P("seq", None),
        P("seq", "head"),
        P("head"),
        P("head"),
        P(None, "head"),
        P(),
        P("head"),
    )
    out_specs = P("seq", "head")
    return jax.shard_map(
        on_device, mesh=mesh, in_specs=in_specs, out_specs=out_specs, check_vma=False
    )
```

```python
import jax
import jax.numpy as jnp
from jax import lax
from jax.sharding import PartitionSpec as P

HEAD_SIZE = 64
STATE = 128
GROUP_HEADS = 32
KERNEL = 4


def extended_2(block, sides, width):
    for axis, dim in sides:
        count = lax.axis_size(axis)
        forward = [(i, i + 1) for i in range(count - 1)]
        backward = [(target, source) for source, target in forward]
        tail, head = lax.optimization_barrier(
            (
                lax.slice_in_dim(block, block.shape[dim] - width, None, axis=dim),
                lax.slice_in_dim(block, 0, width, axis=dim),
            )
        )
        low = lax.ppermute(tail, axis, forward)
        high = lax.ppermute(head, axis, backward)
        block = jnp.concatenate([low, block, high], axis=dim)
    return block


def partner(array, axis, stride):
    return lax.ppermute(array, axis, [(i, i ^ 1 << stride) for i in range(lax.axis_size(axis))])


LINK = jnp.bfloat16


def pack(maps, decays):
    flat = [m.reshape(-1, m.shape[-1]) for m in maps]
    lanes = flat[0].shape[1]
    rows = jnp.stack(decays)
    high = rows.astype(LINK)
    low = (rows - high.astype(jnp.float32)).astype(LINK)
    tail = jnp.concatenate([high, low], axis=0)
    tail = jnp.pad(tail, ((0, 8 - tail.shape[0]), (0, lanes - tail.shape[1])))
    return jnp.concatenate([f.astype(LINK) for f in flat] + [tail], axis=0)


def unpack(message, count, shape):
    rows = shape[0] * shape[1]
    maps = [
        message[i * rows : (i + 1) * rows].astype(jnp.float32).reshape(shape) for i in range(count)
    ]
    tail = message[count * rows :].astype(jnp.float32)
    decays = [tail[i, : shape[0]] + tail[count + i, : shape[0]] for i in range(count)]
    return maps, decays


def butterfly_states(first_loc, second_loc, first_log, second_log, seq_pos, seq_count):
    levels = seq_count.bit_length() - 1
    assert 1 << levels == seq_count
    shape = first_loc.shape
    if levels == 0:
        return jnp.zeros_like(first_loc), first_loc

    def col(v):
        return v[:, None, None]

    ones = jnp.ones((shape[0],), jnp.float32)
    zeros = jnp.zeros((shape[0],), jnp.float32)
    prefix = jnp.zeros_like(first_loc)
    above = jnp.zeros_like(first_loc)
    e_pre, e_abv = ones, ones
    sub_f, sub_g = first_loc, second_loc
    e_f, e_g = jnp.exp(first_log), jnp.exp(second_log)
    for level in range(levels):
        size = 1 << level
        lower = (seq_pos // size) % 2 == 0
        pairs = [(i, i ^ size) for i in range(seq_count)]
        if level < levels - 1:
            got = lax.ppermute(pack((sub_f, sub_g), (e_f, e_g)), "seq", pairs)
            (got_f, got_g), (p_f, p_g) = unpack(got, 2, shape)
            new_f = col(jnp.where(lower, p_f, ones)) * sub_f + col(jnp.where(lower, ones, e_f)) * got_f
            new_g = col(jnp.where(lower, ones, p_g)) * sub_g + col(jnp.where(lower, e_g, ones)) * got_g
            above = above + col(jnp.where(lower, e_abv, zeros)) * got_g
            prefix = prefix + col(jnp.where(lower, zeros, e_pre)) * got_f
            e_abv = jnp.where(lower, e_abv * p_g, e_abv)
            e_pre = jnp.where(lower, e_pre, e_pre * p_f)
            sub_f, sub_g = new_f, new_g
            e_f, e_g = e_f * p_f, e_g * p_g
        else:
            sent = col(jnp.where(lower, ones, e_g)) * sub_f + col(jnp.where(lower, zeros, ones)) * sub_g
            sent_e = jnp.where(lower, e_f, e_f * e_g)
            got = lax.ppermute(pack((sent,), (sent_e,)), "seq", pairs)
            (got_w,), (p_w,) = unpack(got, 1, shape)
            first_in = prefix + col(jnp.where(lower, zeros, e_pre)) * got_w
            second_in = (
                above
                + col(jnp.where(lower, e_abv * p_w, e_abv)) * sub_f
                + col(jnp.where(lower, e_abv, e_abv * e_f)) * got_w
            )
    return first_in, second_in


def on_device(
    inner_rows,
    gate_rows,
    input_proj,
    step_raw,
    decay_rate,
    skip_gain,
    conv_inner,
    conv_proj,
    norm_gain,
):
    tokens = inner_rows.shape[0]
    half_rows = tokens // 2
    head_count = step_raw.shape[1]
    inner_width = inner_rows.shape[1]
    group_count = input_proj.shape[1] // (2 * STATE)
    rim_rows = KERNEL - 1
    seq_count = lax.axis_size("seq")
    seq_pos = lax.axis_index("seq")
    is_last = seq_pos == seq_count - 1
    my_group = lax.axis_index("head") * head_count // GROUP_HEADS
    joined = jnp.concatenate([inner_rows, input_proj], axis=1)
    edge_rows = jnp.concatenate(
        [joined[tokens - rim_rows :], joined[half_rows - rim_rows : half_rows]], axis=0
    )
    extended = extended_2(edge_rows, (("seq", 0),), rim_rows)
    lead_first = extended[:rim_rows]
    lead_second = jnp.where(
        is_last, joined[half_rows - rim_rows : half_rows], extended[3 * rim_rows :]
    )
    conv_taps = jnp.concatenate([conv_inner, conv_proj], axis=1)
    step_size = jax.nn.softplus(step_raw)
    causal = jnp.arange(half_rows)[:, None] >= jnp.arange(half_rows)[None, :]

    def local_block(lead_rows, rows_in, block_step):
        padded = jnp.concatenate([lead_rows, rows_in], axis=0).astype(jnp.float32)
        conv_sum = jnp.zeros((half_rows, joined.shape[1]), jnp.float32)
        for offset in range(KERNEL):
            conv_sum = conv_sum + conv_taps[offset][None, :] * padded[offset : offset + half_rows]
        conv_out = jax.nn.silu(conv_sum).astype(jnp.bfloat16)
        inner_conv = conv_out[:, :inner_width].reshape(half_rows, head_count, HEAD_SIZE)
        b_rows = lax.dynamic_slice_in_dim(conv_out, inner_width + my_group * STATE, STATE, 1)
        c_rows = lax.dynamic_slice_in_dim(
            conv_out, inner_width + (group_count + my_group) * STATE, STATE, 1
        )
        log_cum = jnp.cumsum(-block_step * decay_rate[None, :], axis=0)
        score_grid = jnp.dot(c_rows, b_rows.T, preferred_element_type=jnp.float32)
        log_gap = log_cum.T[:, :, None] - log_cum.T[:, None, :]
        decay_grid = jnp.where(causal[None], jnp.exp(jnp.where(causal[None], log_gap, 0.0)), 0.0)
        weights = (score_grid[None] * decay_grid * block_step.T[:, None, :]).astype(jnp.bfloat16)
        intra_out = jnp.einsum(
            "hts,shp->thp", weights, inner_conv, preferred_element_type=jnp.float32
        )
        tail_decay = jnp.exp(log_cum[-1][None, :] - log_cum) * block_step
        x_weighted = (inner_conv.astype(jnp.float32) * tail_decay[:, :, None]).astype(jnp.bfloat16)
        local_state = jnp.einsum(
            "shp,sn->hpn", x_weighted, b_rows, preferred_element_type=jnp.float32
        )
        partial_out = intra_out + skip_gain[None, :, None] * inner_conv.astype(jnp.float32)
        return (partial_out, log_cum, c_rows, (jnp.exp(log_cum[-1]), local_state))

    def finish_block(partial_out, log_cum, c_rows, state_in):
        inter_out = jnp.einsum(
            "tn,hpn->thp", c_rows.astype(jnp.float32), state_in, precision=lax.Precision.HIGHEST
        )
        total_out = partial_out + jnp.exp(log_cum)[:, :, None] * inter_out
        return total_out.reshape(half_rows, inner_width)

    first_out, first_cum, first_c, first_elem = local_block(
        lead_first, joined[:half_rows], step_size[:half_rows]
    )
    second_out, second_cum, second_c, second_elem = local_block(
        lead_second, joined[half_rows:], step_size[half_rows:]
    )
    first_in, second_in = butterfly_states(
        first_elem[1], second_elem[1], first_cum[-1], second_cum[-1], seq_pos, seq_count
    )
    ssm_out = jnp.concatenate(
        [
            finish_block(first_out, first_cum, first_c, first_in),
            finish_block(second_out, second_cum, second_c, second_in),
        ],
        axis=0,
    )
    gated = ssm_out * jax.nn.silu(gate_rows.astype(jnp.float32))
    partial_sq = jnp.sum(gated * gated, axis=1)
    other_sq = partner(partial_sq, "head", 0)
    mean_sq = (partial_sq + other_sq) / (GROUP_HEADS * HEAD_SIZE)
    normed = gated * lax.rsqrt(mean_sq + 1e-05)[:, None] * norm_gain[None, :]
    return normed.astype(jnp.bfloat16)


def solution(mesh):
    in_specs = (
        P("seq", "head"),
        P("seq", "head"),
        P("seq", None),
        P("seq", "head"),
        P("head"),
        P("head"),
        P(None, "head"),
        P(),
        P("head"),
    )
    out_specs = P("seq", "head")
    return jax.shard_map(
        on_device, mesh=mesh, in_specs=in_specs, out_specs=out_specs, check_vma=False
    )
```

```python
import jax
import jax.numpy as jnp
from jax import lax
from jax.sharding import PartitionSpec as P

HEAD_SIZE = 64
STATE = 128
GROUP_HEADS = 32
KERNEL = 4


def extended_2(block, sides, width):
    for axis, dim in sides:
        count = lax.axis_size(axis)
        forward = [(i, i + 1) for i in range(count - 1)]
        backward = [(target, source) for source, target in forward]
        tail, head = lax.optimization_barrier(
            (
                lax.slice_in_dim(block, block.shape[dim] - width, None, axis=dim),
                lax.slice_in_dim(block, 0, width, axis=dim),
            )
        )
        low = lax.ppermute(tail, axis, forward)
        high = lax.ppermute(head, axis, backward)
        block = jnp.concatenate([low, block, high], axis=dim)
    return block


def partner(array, axis, stride):
    return lax.ppermute(array, axis, [(i, i ^ 1 << stride) for i in range(lax.axis_size(axis))])


LINK = jnp.bfloat16


def pack(maps, decays, kind):
    flat = [m.reshape(-1, m.shape[-1]) for m in maps]
    lanes = flat[0].shape[1]
    rows = jnp.stack(decays)
    high = rows.astype(kind)
    low = (rows - high.astype(jnp.float32)).astype(kind)
    tail = jnp.concatenate([high, low], axis=0)
    tail = jnp.pad(tail, ((0, 8 - tail.shape[0]), (0, lanes - tail.shape[1])))
    return jnp.concatenate([f.astype(kind) for f in flat] + [tail], axis=0)


def unpack(message, count, shape):
    rows = shape[0] * shape[1]
    maps = [
        message[i * rows : (i + 1) * rows].astype(jnp.float32).reshape(shape) for i in range(count)
    ]
    tail = message[count * rows :].astype(jnp.float32)
    decays = [tail[i, : shape[0]] + tail[count + i, : shape[0]] for i in range(count)]
    return maps, decays


def col(v):
    return v[:, None, None]


def butterfly_states(sub_f, sub_g, e_f, e_g, index, count, stride, seq_count):
    levels = count.bit_length() - 1
    assert 1 << levels == count
    shape = sub_f.shape
    if levels == 0:
        return jnp.zeros_like(sub_f), sub_f
    ones = jnp.ones((shape[0],), jnp.float32)
    zeros = jnp.zeros((shape[0],), jnp.float32)
    prefix = jnp.zeros_like(sub_f)
    above = jnp.zeros_like(sub_f)
    e_pre, e_abv = ones, ones
    for level in range(levels):
        size = 1 << level
        lower = (index // size) % 2 == 0
        pairs = [(i, i ^ (size * stride)) for i in range(seq_count)]
        if level < levels - 1:
            got = lax.ppermute(pack((sub_f, sub_g), (e_f, e_g), LINK), "seq", pairs)
            (got_f, got_g), (p_f, p_g) = unpack(got, 2, shape)
            new_f = col(jnp.where(lower, p_f, ones)) * sub_f + col(jnp.where(lower, ones, e_f)) * got_f
            new_g = col(jnp.where(lower, ones, p_g)) * sub_g + col(jnp.where(lower, e_g, ones)) * got_g
            above = above + col(jnp.where(lower, e_abv, zeros)) * got_g
            prefix = prefix + col(jnp.where(lower, zeros, e_pre)) * got_f
            e_abv = jnp.where(lower, e_abv * p_g, e_abv)
            e_pre = jnp.where(lower, e_pre, e_pre * p_f)
            sub_f, sub_g = new_f, new_g
            e_f, e_g = e_f * p_f, e_g * p_g
        else:
            sent = col(jnp.where(lower, ones, e_g)) * sub_f + col(jnp.where(lower, zeros, ones)) * sub_g
            sent_e = jnp.where(lower, e_f, e_f * e_g)
            got = lax.ppermute(pack((sent,), (sent_e,), LINK), "seq", pairs)
            (got_w,), (p_w,) = unpack(got, 1, shape)
            first_in = prefix + col(jnp.where(lower, zeros, e_pre)) * got_w
            second_in = (
                above
                + col(jnp.where(lower, e_abv * p_w, e_abv)) * sub_f
                + col(jnp.where(lower, e_abv, e_abv * e_f)) * got_w
            )
    return first_in, second_in


def block_states(first_loc, second_loc, first_log, second_log, seq_pos, seq_count):
    heads = first_loc.shape[0]
    e1, e2 = jnp.exp(first_log), jnp.exp(second_log)
    if seq_count % 2 or heads % 2:
        return butterfly_states(first_loc, second_loc, e1, e2, seq_pos, seq_count, 1, seq_count)
    half = heads // 2
    core = seq_pos % 2
    upper = core == 1
    pairs = [(i, i ^ 1) for i in range(seq_count)]
    got = lax.ppermute(pack((first_loc, second_loc), (e1, e2), jnp.float32), "seq", pairs)
    (p1, p2), (q1, q2) = unpack(got, 2, first_loc.shape)
    ones = jnp.ones((heads,), jnp.float32)
    pair_f = col(jnp.where(upper, ones, q1)) * first_loc + col(jnp.where(upper, e1, ones)) * p1
    pair_g = col(jnp.where(upper, q2, ones)) * second_loc + col(jnp.where(upper, ones, e2)) * p2
    low_f = jnp.where(upper, p1, first_loc)
    low_fe = jnp.where(upper, q1, e1)
    high_g = jnp.where(upper, second_loc, p2)
    high_ge = jnp.where(upper, e2, q2)

    def mine(x):
        return lax.dynamic_slice_in_dim(x, core * half, half, 0)

    prefix, wrapped = butterfly_states(
        mine(pair_f),
        mine(pair_g),
        mine(e1 * q1),
        mine(e2 * q2),
        seq_pos // 2,
        seq_count // 2,
        2,
        seq_count,
    )
    after_low = col(mine(low_fe)) * prefix + mine(low_f)
    before_high = col(mine(high_ge)) * wrapped + mine(high_g)
    own = (jnp.where(upper, after_low, prefix), jnp.where(upper, wrapped, before_high))
    other = (jnp.where(upper, prefix, after_low), jnp.where(upper, before_high, wrapped))
    got_1, got_2 = lax.ppermute(other, "seq", pairs)

    def whole(own_half, got_half):
        return jnp.where(
            upper,
            jnp.concatenate([got_half, own_half], axis=0),
            jnp.concatenate([own_half, got_half], axis=0),
        )

    return whole(own[0], got_1), whole(own[1], got_2)


def on_device(
    inner_rows,
    gate_rows,
    input_proj,
    step_raw,
    decay_rate,
    skip_gain,
    conv_inner,
    conv_proj,
    norm_gain,
):
    tokens = inner_rows.shape[0]
    half_rows = tokens // 2
    head_count = step_raw.shape[1]
    inner_width = inner_rows.shape[1]
    group_count = input_proj.shape[1] // (2 * STATE)
    rim_rows = KERNEL - 1
    seq_count = lax.axis_size("seq")
    seq_pos = lax.axis_index("seq")
    is_last = seq_pos == seq_count - 1
    my_group = lax.axis_index("head") * head_count // GROUP_HEADS
    joined = jnp.concatenate([inner_rows, input_proj], axis=1)
    edge_rows = jnp.concatenate(
        [joined[tokens - rim_rows :], joined[half_rows - rim_rows : half_rows]], axis=0
    )
    extended = extended_2(edge_rows, (("seq", 0),), rim_rows)
    lead_first = extended[:rim_rows]
    lead_second = jnp.where(
        is_last, joined[half_rows - rim_rows : half_rows], extended[3 * rim_rows :]
    )
    conv_taps = jnp.concatenate([conv_inner, conv_proj], axis=1)
    step_size = jax.nn.softplus(step_raw)
    causal = jnp.arange(half_rows)[:, None] >= jnp.arange(half_rows)[None, :]

    def local_block(lead_rows, rows_in, block_step):
        padded = jnp.concatenate([lead_rows, rows_in], axis=0).astype(jnp.float32)
        conv_sum = jnp.zeros((half_rows, joined.shape[1]), jnp.float32)
        for offset in range(KERNEL):
            conv_sum = conv_sum + conv_taps[offset][None, :] * padded[offset : offset + half_rows]
        conv_out = jax.nn.silu(conv_sum).astype(jnp.bfloat16)
        inner_conv = conv_out[:, :inner_width].reshape(half_rows, head_count, HEAD_SIZE)
        b_rows = lax.dynamic_slice_in_dim(conv_out, inner_width + my_group * STATE, STATE, 1)
        c_rows = lax.dynamic_slice_in_dim(
            conv_out, inner_width + (group_count + my_group) * STATE, STATE, 1
        )
        log_cum = jnp.cumsum(-block_step * decay_rate[None, :], axis=0)
        score_grid = jnp.dot(c_rows, b_rows.T, preferred_element_type=jnp.float32)
        log_gap = log_cum.T[:, :, None] - log_cum.T[:, None, :]
        decay_grid = jnp.where(causal[None], jnp.exp(jnp.where(causal[None], log_gap, 0.0)), 0.0)
        weights = (score_grid[None] * decay_grid * block_step.T[:, None, :]).astype(jnp.bfloat16)
        intra_out = jnp.einsum(
            "hts,shp->thp", weights, inner_conv, preferred_element_type=jnp.float32
        )
        tail_decay = jnp.exp(log_cum[-1][None, :] - log_cum) * block_step
        x_weighted = (inner_conv.astype(jnp.float32) * tail_decay[:, :, None]).astype(jnp.bfloat16)
        local_state = jnp.einsum(
            "shp,sn->hpn", x_weighted, b_rows, preferred_element_type=jnp.float32
        )
        partial_out = intra_out + skip_gain[None, :, None] * inner_conv.astype(jnp.float32)
        return (partial_out, log_cum, c_rows, (jnp.exp(log_cum[-1]), local_state))

    def finish_block(partial_out, log_cum, c_rows, state_in):
        inter_out = jnp.einsum(
            "tn,hpn->thp", c_rows.astype(jnp.float32), state_in, precision=lax.Precision.HIGHEST
        )
        total_out = partial_out + jnp.exp(log_cum)[:, :, None] * inter_out
        return total_out.reshape(half_rows, inner_width)

    first_out, first_cum, first_c, first_elem = local_block(
        lead_first, joined[:half_rows], step_size[:half_rows]
    )
    second_out, second_cum, second_c, second_elem = local_block(
        lead_second, joined[half_rows:], step_size[half_rows:]
    )
    first_in, second_in = block_states(
        first_elem[1], second_elem[1], first_cum[-1], second_cum[-1], seq_pos, seq_count
    )
    ssm_out = jnp.concatenate(
        [
            finish_block(first_out, first_cum, first_c, first_in),
            finish_block(second_out, second_cum, second_c, second_in),
        ],
        axis=0,
    )
    gated = ssm_out * jax.nn.silu(gate_rows.astype(jnp.float32))
    partial_sq = jnp.sum(gated * gated, axis=1)
    other_sq = partner(partial_sq, "head", 0)
    mean_sq = (partial_sq + other_sq) / (GROUP_HEADS * HEAD_SIZE)
    normed = gated * lax.rsqrt(mean_sq + 1e-05)[:, None] * norm_gain[None, :]
    return normed.astype(jnp.bfloat16)


def solution(mesh):
    in_specs = (
        P("seq", "head"),
        P("seq", "head"),
        P("seq", None),
        P("seq", "head"),
        P("head"),
        P("head"),
        P(None, "head"),
        P(),
        P("head"),
    )
    out_specs = P("seq", "head")
    return jax.shard_map(
        on_device, mesh=mesh, in_specs=in_specs, out_specs=out_specs, check_vma=False
    )
```

```python
import jax
import jax.numpy as jnp
from jax import lax
from jax.experimental import pallas as pl
from jax.experimental.pallas import tpu as pltpu
from jax.sharding import PartitionSpec as P

HEAD_SIZE = 64
STATE = 128
GROUP_HEADS = 32
KERNEL = 4


def extended_2(block, sides, width):
    for axis, dim in sides:
        count = lax.axis_size(axis)
        forward = [(i, i + 1) for i in range(count - 1)]
        backward = [(target, source) for source, target in forward]
        tail, head = lax.optimization_barrier(
            (
                lax.slice_in_dim(block, block.shape[dim] - width, None, axis=dim),
                lax.slice_in_dim(block, 0, width, axis=dim),
            )
        )
        low = lax.ppermute(tail, axis, forward)
        high = lax.ppermute(head, axis, backward)
        block = jnp.concatenate([low, block, high], axis=dim)
    return block


def partner(array, axis, stride):
    return lax.ppermute(array, axis, [(i, i ^ 1 << stride) for i in range(lax.axis_size(axis))])


LINK = jnp.bfloat16


def pack(maps, decays, kind):
    flat = [m.reshape(-1, m.shape[-1]) for m in maps]
    lanes = flat[0].shape[1]
    rows = jnp.stack(decays)
    high = rows.astype(kind)
    low = (rows - high.astype(jnp.float32)).astype(kind)
    tail = jnp.concatenate([high, low], axis=0)
    tail = jnp.pad(tail, ((0, 8 - tail.shape[0]), (0, lanes - tail.shape[1])))
    return jnp.concatenate([f.astype(kind) for f in flat] + [tail], axis=0)


def unpack(message, count, shape):
    rows = shape[0] * shape[1]
    maps = [
        message[i * rows : (i + 1) * rows].astype(jnp.float32).reshape(shape) for i in range(count)
    ]
    tail = message[count * rows :].astype(jnp.float32)
    decays = [tail[i, : shape[0]] + tail[count + i, : shape[0]] for i in range(count)]
    return maps, decays


def col(v):
    return v[:, None, None]


def butterfly_states(sub_f, sub_g, e_f, e_g, index, count, stride, seq_count):
    levels = count.bit_length() - 1
    assert 1 << levels == count
    shape = sub_f.shape
    if levels == 0:
        return jnp.zeros_like(sub_f), sub_f
    ones = jnp.ones((shape[0],), jnp.float32)
    zeros = jnp.zeros((shape[0],), jnp.float32)
    prefix = jnp.zeros_like(sub_f)
    above = jnp.zeros_like(sub_f)
    e_pre, e_abv = ones, ones
    for level in range(levels):
        size = 1 << level
        lower = (index // size) % 2 == 0
        pairs = [(i, i ^ (size * stride)) for i in range(seq_count)]
        if level < levels - 1:
            got = lax.ppermute(pack((sub_f, sub_g), (e_f, e_g), LINK), "seq", pairs)
            (got_f, got_g), (p_f, p_g) = unpack(got, 2, shape)
            new_f = col(jnp.where(lower, p_f, ones)) * sub_f + col(jnp.where(lower, ones, e_f)) * got_f
            new_g = col(jnp.where(lower, ones, p_g)) * sub_g + col(jnp.where(lower, e_g, ones)) * got_g
            above = above + col(jnp.where(lower, e_abv, zeros)) * got_g
            prefix = prefix + col(jnp.where(lower, zeros, e_pre)) * got_f
            e_abv = jnp.where(lower, e_abv * p_g, e_abv)
            e_pre = jnp.where(lower, e_pre, e_pre * p_f)
            sub_f, sub_g = new_f, new_g
            e_f, e_g = e_f * p_f, e_g * p_g
        else:
            sent = col(jnp.where(lower, ones, e_g)) * sub_f + col(jnp.where(lower, zeros, ones)) * sub_g
            sent_e = jnp.where(lower, e_f, e_f * e_g)
            got = lax.ppermute(pack((sent,), (sent_e,), LINK), "seq", pairs)
            (got_w,), (p_w,) = unpack(got, 1, shape)
            first_in = prefix + col(jnp.where(lower, zeros, e_pre)) * got_w
            second_in = (
                above
                + col(jnp.where(lower, e_abv * p_w, e_abv)) * sub_f
                + col(jnp.where(lower, e_abv, e_abv * e_f)) * got_w
            )
    return first_in, second_in


def block_states(first_loc, second_loc, first_log, second_log, seq_pos, seq_count):
    heads = first_loc.shape[0]
    e1, e2 = jnp.exp(first_log), jnp.exp(second_log)
    if seq_count % 2 or heads % 2:
        return butterfly_states(first_loc, second_loc, e1, e2, seq_pos, seq_count, 1, seq_count)
    half = heads // 2
    core = seq_pos % 2
    upper = core == 1
    pairs = [(i, i ^ 1) for i in range(seq_count)]
    got = lax.ppermute(pack((first_loc, second_loc), (e1, e2), jnp.float32), "seq", pairs)
    (p1, p2), (q1, q2) = unpack(got, 2, first_loc.shape)
    ones = jnp.ones((heads,), jnp.float32)
    pair_f = col(jnp.where(upper, ones, q1)) * first_loc + col(jnp.where(upper, e1, ones)) * p1
    pair_g = col(jnp.where(upper, q2, ones)) * second_loc + col(jnp.where(upper, ones, e2)) * p2
    low_f = jnp.where(upper, p1, first_loc)
    low_fe = jnp.where(upper, q1, e1)
    high_g = jnp.where(upper, second_loc, p2)
    high_ge = jnp.where(upper, e2, q2)

    def mine(x):
        return lax.dynamic_slice_in_dim(x, core * half, half, 0)

    prefix, wrapped = butterfly_states(
        mine(pair_f),
        mine(pair_g),
        mine(e1 * q1),
        mine(e2 * q2),
        seq_pos // 2,
        seq_count // 2,
        2,
        seq_count,
    )
    after_low = col(mine(low_fe)) * prefix + mine(low_f)
    before_high = col(mine(high_ge)) * wrapped + mine(high_g)
    own = (jnp.where(upper, after_low, prefix), jnp.where(upper, wrapped, before_high))
    other = (jnp.where(upper, prefix, after_low), jnp.where(upper, before_high, wrapped))
    got_1, got_2 = lax.ppermute(other, "seq", pairs)

    def whole(own_half, got_half):
        return jnp.where(
            upper,
            jnp.concatenate([got_half, own_half], axis=0),
            jnp.concatenate([own_half, got_half], axis=0),
        )

    return whole(own[0], got_1), whole(own[1], got_2)


class Mix:
    def __init__(self, heads):
        self.heads = heads
        self.arrays = []
        self.views = []

    def view(self, array, offset):
        for index, known in enumerate(self.arrays):
            if known is array:
                break
        else:
            self.arrays.append(array)
            index = len(self.arrays) - 1
        self.views.append((index, offset))
        return [(len(self.views) - 1, jnp.ones((self.heads,), jnp.float32))]

    def run(self, logical, out_arrays):
        heads = self.heads
        coefs, layout = [], []
        for terms, dests in logical:
            rows = []
            for view, coef in terms:
                rows.append((view, len(coefs)))
                coefs.append(coef)
            layout.append((rows, dests))
        table = jnp.stack(coefs).reshape(-1)
        offsets = jnp.stack([jnp.asarray(off, jnp.int32) for _, off in self.views])
        inner = self.arrays[0].shape[1:]
        views = self.views
        count = len(self.arrays)

        def kernel(table_ref, off_ref, *refs):
            ins, outs = refs[:count], refs[count:]
            for h in range(heads):
                cache = {}
                for rows, dests in layout:
                    acc = None
                    for view, row in rows:
                        if view not in cache:
                            array, _ = views[view]
                            cache[view] = ins[array][off_ref[view] + h].astype(jnp.float32)
                        term = table_ref[row * heads + h] * cache[view]
                        acc = term if acc is None else acc + term
                    for out, block in dests:
                        outs[out][block * heads + h] = acc.astype(outs[out].dtype)

        slab = heads * inner[0] * inner[1]
        moved = sum(a.size * a.dtype.itemsize for a in self.arrays)
        moved += sum(b * slab * jnp.dtype(d).itemsize for d, b in out_arrays)
        smem = pl.BlockSpec(memory_space=pltpu.SMEM)
        vmem = pl.BlockSpec(memory_space=pltpu.VMEM)
        return pl.pallas_call(
            kernel,
            out_shape=[jax.ShapeDtypeStruct((b * heads, *inner), d) for d, b in out_arrays],
            in_specs=[smem, smem] + [vmem] * count,
            out_specs=[vmem] * len(out_arrays),
            cost_estimate=pl.CostEstimate(
                flops=2 * len(coefs) * slab, bytes_accessed=moved, transcendentals=0
            ),
        )(table, offsets, *self.arrays)


def scale(terms, coef):
    return [(view, c * coef) for view, c in terms]


def next_message(f_terms, g_terms, e_f, e_g, lower, last):
    if not last:
        return [f_terms, g_terms], jnp.stack([e_f, e_g])
    one = jnp.ones_like(e_f)
    sent = scale(f_terms, jnp.where(lower, one, e_g)) + scale(g_terms, jnp.where(lower, 0.0 * one, one))
    return [sent], jnp.stack([jnp.where(lower, e_f, e_f * e_g)])


def kernel_states(first_loc, second_loc, first_log, second_log, seq_pos, seq_count):
    heads = first_loc.shape[0]
    half = heads // 2
    units = seq_count // 2
    levels = max(units, 1).bit_length() - 1
    if seq_count % 2 or heads % 2 or levels < 1 or (1 << levels) != units:
        return block_states(first_loc, second_loc, first_log, second_log, seq_pos, seq_count)
    f32 = jnp.float32
    e1, e2 = jnp.exp(first_log), jnp.exp(second_log)
    core = seq_pos % 2
    upper = core == 1
    up = upper.astype(f32)
    unit = seq_pos // 2
    one = jnp.ones((half,), f32)
    pairs = [(i, i ^ 1) for i in range(seq_count)]
    p1, p2, got_e = lax.ppermute((first_loc, second_loc, jnp.stack([e1, e2])), "seq", pairs)

    def mine(v):
        return lax.dynamic_slice_in_dim(v, core * half, half)

    e1h, e2h, q1h, q2h = mine(e1), mine(e2), mine(got_e[0]), mine(got_e[1])
    mix = Mix(half)
    v_p1, v_p2 = mix.view(p1, core * half), mix.view(p2, core * half)
    v_l1, v_l2 = mix.view(first_loc, core * half), mix.view(second_loc, core * half)
    f_terms = scale(v_l1, jnp.where(upper, one, q1h)) + scale(v_p1, jnp.where(upper, e1h, one))
    g_terms = scale(v_l2, jnp.where(upper, q2h, one)) + scale(v_p2, jnp.where(upper, one, e2h))
    low_terms = scale(v_p1, up * one) + scale(v_l1, (1 - up) * one)
    high_terms = scale(v_l2, up * one) + scale(v_p2, (1 - up) * one)
    e_f, e_g = e1h * q1h, e2h * q2h
    low_fe = jnp.where(upper, q1h, e1h)
    high_ge = jnp.where(upper, e2h, q2h)
    lower = unit % 2 == 0
    msg_terms, msg_e = next_message(f_terms, g_terms, e_f, e_g, lower, levels == 1)
    logical = [(f_terms, [(0, 0)]), (g_terms, [(0, 1)]), (low_terms, [(1, 0)]), (high_terms, [(1, 1)])]
    logical += [(t, [(2, b)]) for b, t in enumerate(msg_terms)]
    state, edges, msg = mix.run(logical, [(f32, 2), (f32, 2), (LINK, len(msg_terms))])
    zero_h = jnp.zeros((half,), f32)
    e_pre, e_abv = one, one
    have_acc = False
    for level in range(levels):
        size = 1 << level
        lower = (unit // size) % 2 == 0
        last = level == levels - 1
        pairs = [(i, i ^ (2 * size)) for i in range(seq_count)]
        got, got_e = lax.ppermute((msg, msg_e), "seq", pairs)
        mix = Mix(half)
        v_f, v_g = mix.view(state, 0), mix.view(state, half)
        if have_acc:
            v_pre, v_abv = mix.view(acc, 0), mix.view(acc, half)
        else:
            v_pre, v_abv = [], []
        if not last:
            p_f, p_g = got_e[0], got_e[1]
            w_f, w_g = mix.view(got, 0), mix.view(got, half)
            f_terms = scale(v_f, jnp.where(lower, p_f, one)) + scale(w_f, jnp.where(lower, one, e_f))
            g_terms = scale(v_g, jnp.where(lower, one, p_g)) + scale(w_g, jnp.where(lower, e_g, one))
            abv_terms = v_abv + scale(w_g, jnp.where(lower, e_abv, zero_h))
            pre_terms = v_pre + scale(w_f, jnp.where(lower, zero_h, e_pre))
            e_abv = jnp.where(lower, e_abv * p_g, e_abv)
            e_pre = jnp.where(lower, e_pre, e_pre * p_f)
            e_f, e_g = e_f * p_f, e_g * p_g
            next_lower = (unit // (2 * size)) % 2 == 0
            msg_terms, msg_e = next_message(f_terms, g_terms, e_f, e_g, next_lower, level + 1 == levels - 1)
            logical = [(f_terms, [(0, 0)]), (g_terms, [(0, 1)])]
            logical += [(pre_terms, [(1, 0)]), (abv_terms, [(1, 1)])]
            logical += [(t, [(2, b)]) for b, t in enumerate(msg_terms)]
            state, acc, msg = mix.run(logical, [(f32, 2), (f32, 2), (LINK, len(msg_terms))])
            have_acc = True
        else:
            p_w = got_e[0]
            w = mix.view(got, 0)
            v_low, v_high = mix.view(edges, 0), mix.view(edges, half)
            first_terms = v_pre + scale(w, jnp.where(lower, zero_h, e_pre))
            second_terms = (
                v_abv
                + scale(v_f, jnp.where(lower, e_abv * p_w, e_abv))
                + scale(w, jnp.where(lower, e_abv, e_abv * e_f))
            )
            own_first = scale(first_terms, jnp.where(upper, low_fe, one)) + scale(v_low, up * one)
            own_second = scale(second_terms, jnp.where(upper, one, high_ge)) + scale(v_high, (1 - up) * one)
            other_first = scale(first_terms, jnp.where(upper, one, low_fe)) + scale(v_low, (1 - up) * one)
            other_second = scale(second_terms, jnp.where(upper, high_ge, one)) + scale(v_high, up * one)
            logical = [(own_first, [(0, 0)]), (own_second, [(0, 1)])]
            logical += [(other_first, [(1, 0)]), (other_second, [(1, 1)])]
            own, other = mix.run(logical, [(f32, 2), (f32, 2)])
    swapped = lax.ppermute(other, "seq", [(i, i ^ 1) for i in range(seq_count)])

    def whole(own_half, got_half):
        return jnp.where(
            upper,
            jnp.concatenate([got_half, own_half], axis=0),
            jnp.concatenate([own_half, got_half], axis=0),
        )

    return whole(own[:half], swapped[:half]), whole(own[half:], swapped[half:])


def on_device(
    inner_rows,
    gate_rows,
    input_proj,
    step_raw,
    decay_rate,
    skip_gain,
    conv_inner,
    conv_proj,
    norm_gain,
):
    tokens = inner_rows.shape[0]
    half_rows = tokens // 2
    head_count = step_raw.shape[1]
    inner_width = inner_rows.shape[1]
    group_count = input_proj.shape[1] // (2 * STATE)
    rim_rows = KERNEL - 1
    seq_count = lax.axis_size("seq")
    seq_pos = lax.axis_index("seq")
    is_last = seq_pos == seq_count - 1
    my_group = lax.axis_index("head") * head_count // GROUP_HEADS
    joined = jnp.concatenate([inner_rows, input_proj], axis=1)
    edge_rows = jnp.concatenate(
        [joined[tokens - rim_rows :], joined[half_rows - rim_rows : half_rows]], axis=0
    )
    extended = extended_2(edge_rows, (("seq", 0),), rim_rows)
    lead_first = extended[:rim_rows]
    lead_second = jnp.where(
        is_last, joined[half_rows - rim_rows : half_rows], extended[3 * rim_rows :]
    )
    conv_taps = jnp.concatenate([conv_inner, conv_proj], axis=1)
    step_size = jax.nn.softplus(step_raw)
    causal = jnp.arange(half_rows)[:, None] >= jnp.arange(half_rows)[None, :]

    def local_block(lead_rows, rows_in, block_step):
        padded = jnp.concatenate([lead_rows, rows_in], axis=0).astype(jnp.float32)
        conv_sum = jnp.zeros((half_rows, joined.shape[1]), jnp.float32)
        for offset in range(KERNEL):
            conv_sum = conv_sum + conv_taps[offset][None, :] * padded[offset : offset + half_rows]
        conv_out = jax.nn.silu(conv_sum).astype(jnp.bfloat16)
        inner_conv = conv_out[:, :inner_width].reshape(half_rows, head_count, HEAD_SIZE)
        b_rows = lax.dynamic_slice_in_dim(conv_out, inner_width + my_group * STATE, STATE, 1)
        c_rows = lax.dynamic_slice_in_dim(
            conv_out, inner_width + (group_count + my_group) * STATE, STATE, 1
        )
        log_cum = jnp.cumsum(-block_step * decay_rate[None, :], axis=0)
        score_grid = jnp.dot(c_rows, b_rows.T, preferred_element_type=jnp.float32)
        log_gap = log_cum.T[:, :, None] - log_cum.T[:, None, :]
        decay_grid = jnp.where(causal[None], jnp.exp(jnp.where(causal[None], log_gap, 0.0)), 0.0)
        weights = (score_grid[None] * decay_grid * block_step.T[:, None, :]).astype(jnp.bfloat16)
        intra_out = jnp.einsum(
            "hts,shp->thp", weights, inner_conv, preferred_element_type=jnp.float32
        )
        tail_decay = jnp.exp(log_cum[-1][None, :] - log_cum) * block_step
        x_weighted = (inner_conv.astype(jnp.float32) * tail_decay[:, :, None]).astype(jnp.bfloat16)
        local_state = jnp.einsum(
            "shp,sn->hpn", x_weighted, b_rows, preferred_element_type=jnp.float32
        )
        partial_out = intra_out + skip_gain[None, :, None] * inner_conv.astype(jnp.float32)
        return (partial_out, log_cum, c_rows, (jnp.exp(log_cum[-1]), local_state))

    def finish_block(partial_out, log_cum, c_rows, state_in):
        inter_out = jnp.einsum(
            "tn,hpn->thp", c_rows.astype(jnp.float32), state_in, precision=lax.Precision.HIGHEST
        )
        total_out = partial_out + jnp.exp(log_cum)[:, :, None] * inter_out
        return total_out.reshape(half_rows, inner_width)

    first_out, first_cum, first_c, first_elem = local_block(
        lead_first, joined[:half_rows], step_size[:half_rows]
    )
    second_out, second_cum, second_c, second_elem = local_block(
        lead_second, joined[half_rows:], step_size[half_rows:]
    )
    first_in, second_in = kernel_states(
        first_elem[1], second_elem[1], first_cum[-1], second_cum[-1], seq_pos, seq_count
    )
    ssm_out = jnp.concatenate(
        [
            finish_block(first_out, first_cum, first_c, first_in),
            finish_block(second_out, second_cum, second_c, second_in),
        ],
        axis=0,
    )
    gated = ssm_out * jax.nn.silu(gate_rows.astype(jnp.float32))
    partial_sq = jnp.sum(gated * gated, axis=1)
    other_sq = partner(partial_sq, "head", 0)
    mean_sq = (partial_sq + other_sq) / (GROUP_HEADS * HEAD_SIZE)
    normed = gated * lax.rsqrt(mean_sq + 1e-05)[:, None] * norm_gain[None, :]
    return normed.astype(jnp.bfloat16)


def solution(mesh):
    in_specs = (
        P("seq", "head"),
        P("seq", "head"),
        P("seq", None),
        P("seq", "head"),
        P("head"),
        P("head"),
        P(None, "head"),
        P(),
        P("head"),
    )
    out_specs = P("seq", "head")
    return jax.shard_map(
        on_device, mesh=mesh, in_specs=in_specs, out_specs=out_specs, check_vma=False
    )
```

```python
import jax
import jax.numpy as jnp
from jax import lax
from jax.experimental import pallas as pl
from jax.experimental.pallas import tpu as pltpu
from jax.sharding import PartitionSpec as P

HEAD_SIZE = 64
STATE = 128
GROUP_HEADS = 32
KERNEL = 4


def extended_2(block, sides, width):
    for axis, dim in sides:
        count = lax.axis_size(axis)
        forward = [(i, i + 1) for i in range(count - 1)]
        backward = [(target, source) for source, target in forward]
        tail, head = lax.optimization_barrier(
            (
                lax.slice_in_dim(block, block.shape[dim] - width, None, axis=dim),
                lax.slice_in_dim(block, 0, width, axis=dim),
            )
        )
        low = lax.ppermute(tail, axis, forward)
        high = lax.ppermute(head, axis, backward)
        block = jnp.concatenate([low, block, high], axis=dim)
    return block


def partner(array, axis, stride):
    return lax.ppermute(array, axis, [(i, i ^ 1 << stride) for i in range(lax.axis_size(axis))])


LINK = jnp.bfloat16


def pack(maps, decays, kind):
    flat = [m.reshape(-1, m.shape[-1]) for m in maps]
    lanes = flat[0].shape[1]
    rows = jnp.stack(decays)
    high = rows.astype(kind)
    low = (rows - high.astype(jnp.float32)).astype(kind)
    tail = jnp.concatenate([high, low], axis=0)
    tail = jnp.pad(tail, ((0, 8 - tail.shape[0]), (0, lanes - tail.shape[1])))
    return jnp.concatenate([f.astype(kind) for f in flat] + [tail], axis=0)


def unpack(message, count, shape):
    rows = shape[0] * shape[1]
    maps = [
        message[i * rows : (i + 1) * rows].astype(jnp.float32).reshape(shape) for i in range(count)
    ]
    tail = message[count * rows :].astype(jnp.float32)
    decays = [tail[i, : shape[0]] + tail[count + i, : shape[0]] for i in range(count)]
    return maps, decays


def col(v):
    return v[:, None, None]


def butterfly_states(sub_f, sub_g, e_f, e_g, index, count, stride, seq_count):
    levels = count.bit_length() - 1
    assert 1 << levels == count
    shape = sub_f.shape
    if levels == 0:
        return jnp.zeros_like(sub_f), sub_f
    ones = jnp.ones((shape[0],), jnp.float32)
    zeros = jnp.zeros((shape[0],), jnp.float32)
    prefix = jnp.zeros_like(sub_f)
    above = jnp.zeros_like(sub_f)
    e_pre, e_abv = ones, ones
    for level in range(levels):
        size = 1 << level
        lower = (index // size) % 2 == 0
        pairs = [(i, i ^ (size * stride)) for i in range(seq_count)]
        if level < levels - 1:
            got = lax.ppermute(pack((sub_f, sub_g), (e_f, e_g), LINK), "seq", pairs)
            (got_f, got_g), (p_f, p_g) = unpack(got, 2, shape)
            new_f = col(jnp.where(lower, p_f, ones)) * sub_f + col(jnp.where(lower, ones, e_f)) * got_f
            new_g = col(jnp.where(lower, ones, p_g)) * sub_g + col(jnp.where(lower, e_g, ones)) * got_g
            above = above + col(jnp.where(lower, e_abv, zeros)) * got_g
            prefix = prefix + col(jnp.where(lower, zeros, e_pre)) * got_f
            e_abv = jnp.where(lower, e_abv * p_g, e_abv)
            e_pre = jnp.where(lower, e_pre, e_pre * p_f)
            sub_f, sub_g = new_f, new_g
            e_f, e_g = e_f * p_f, e_g * p_g
        else:
            sent = col(jnp.where(lower, ones, e_g)) * sub_f + col(jnp.where(lower, zeros, ones)) * sub_g
            sent_e = jnp.where(lower, e_f, e_f * e_g)
            got = lax.ppermute(pack((sent,), (sent_e,), LINK), "seq", pairs)
            (got_w,), (p_w,) = unpack(got, 1, shape)
            first_in = prefix + col(jnp.where(lower, zeros, e_pre)) * got_w
            second_in = (
                above
                + col(jnp.where(lower, e_abv * p_w, e_abv)) * sub_f
                + col(jnp.where(lower, e_abv, e_abv * e_f)) * got_w
            )
    return first_in, second_in


def block_states(first_loc, second_loc, first_log, second_log, seq_pos, seq_count):
    heads = first_loc.shape[0]
    e1, e2 = jnp.exp(first_log), jnp.exp(second_log)
    if seq_count % 2 or heads % 2:
        return butterfly_states(first_loc, second_loc, e1, e2, seq_pos, seq_count, 1, seq_count)
    half = heads // 2
    core = seq_pos % 2
    upper = core == 1
    pairs = [(i, i ^ 1) for i in range(seq_count)]
    got = lax.ppermute(pack((first_loc, second_loc), (e1, e2), jnp.float32), "seq", pairs)
    (p1, p2), (q1, q2) = unpack(got, 2, first_loc.shape)
    ones = jnp.ones((heads,), jnp.float32)
    pair_f = col(jnp.where(upper, ones, q1)) * first_loc + col(jnp.where(upper, e1, ones)) * p1
    pair_g = col(jnp.where(upper, q2, ones)) * second_loc + col(jnp.where(upper, ones, e2)) * p2
    low_f = jnp.where(upper, p1, first_loc)
    low_fe = jnp.where(upper, q1, e1)
    high_g = jnp.where(upper, second_loc, p2)
    high_ge = jnp.where(upper, e2, q2)

    def mine(x):
        return lax.dynamic_slice_in_dim(x, core * half, half, 0)

    prefix, wrapped = butterfly_states(
        mine(pair_f),
        mine(pair_g),
        mine(e1 * q1),
        mine(e2 * q2),
        seq_pos // 2,
        seq_count // 2,
        2,
        seq_count,
    )
    after_low = col(mine(low_fe)) * prefix + mine(low_f)
    before_high = col(mine(high_ge)) * wrapped + mine(high_g)
    own = (jnp.where(upper, after_low, prefix), jnp.where(upper, wrapped, before_high))
    other = (jnp.where(upper, prefix, after_low), jnp.where(upper, before_high, wrapped))
    got_1, got_2 = lax.ppermute(other, "seq", pairs)

    def whole(own_half, got_half):
        return jnp.where(
            upper,
            jnp.concatenate([got_half, own_half], axis=0),
            jnp.concatenate([own_half, got_half], axis=0),
        )

    return whole(own[0], got_1), whole(own[1], got_2)


class Mix:
    def __init__(self, heads):
        self.heads = heads
        self.arrays = []
        self.views = []

    def view(self, array, offset):
        for index, known in enumerate(self.arrays):
            if known is array:
                break
        else:
            self.arrays.append(array)
            index = len(self.arrays) - 1
        self.views.append((index, offset))
        return [(len(self.views) - 1, jnp.ones((self.heads,), jnp.float32))]

    def run(self, logical, out_arrays, tails=()):
        heads = self.heads
        coefs, layout = [], []
        for terms, dests in logical:
            rows = []
            for view, coef in terms:
                rows.append((view, len(coefs)))
                coefs.append(coef)
            layout.append((rows, dests))
        table = jnp.stack(coefs).reshape(-1)
        offsets = jnp.stack([jnp.asarray(off, jnp.int32) for _, off in self.views])
        inner = self.arrays[0].shape[1:]
        views = self.views
        count = len(self.arrays) + len(tails)
        tail_outs = [(len(self.arrays) + i, out) for i, (_, out) in enumerate(tails)]
        extra = [0] * len(out_arrays)
        for _, out in tails:
            extra[out] = 1

        def kernel(table_ref, off_ref, *refs):
            ins, outs = refs[:count], refs[count:]
            for source, out in tail_outs:
                outs[out][outs[out].shape[0] - 1] = ins[source][0]
            for h in range(heads):
                cache = {}
                for rows, dests in layout:
                    acc = None
                    for view, row in rows:
                        if view not in cache:
                            array, _ = views[view]
                            cache[view] = ins[array][off_ref[view] + h].astype(jnp.float32)
                        term = table_ref[row * heads + h] * cache[view]
                        acc = term if acc is None else acc + term
                    for out, block in dests:
                        outs[out][block * heads + h] = acc.astype(outs[out].dtype)

        slab = heads * inner[0] * inner[1]
        moved = sum(a.size * a.dtype.itemsize for a in self.arrays)
        moved += sum(b * slab * jnp.dtype(d).itemsize for d, b in out_arrays)
        arrays = list(self.arrays) + [t for t, _ in tails]
        smem = pl.BlockSpec(memory_space=pltpu.SMEM)
        vmem = pl.BlockSpec(memory_space=pltpu.VMEM)
        return pl.pallas_call(
            kernel,
            out_shape=[
                jax.ShapeDtypeStruct((b * heads + x, *inner), d)
                for (d, b), x in zip(out_arrays, extra)
            ],
            in_specs=[smem, smem] + [vmem] * count,
            out_specs=[vmem] * len(out_arrays),
            cost_estimate=pl.CostEstimate(
                flops=2 * len(coefs) * slab, bytes_accessed=moved, transcendentals=0
            ),
        )(table, offsets, *arrays)


def tail_slot(decays, inner, kind):
    rows = jnp.stack(decays)
    high = rows.astype(kind)
    low = (rows - high.astype(jnp.float32)).astype(kind)
    both = jnp.concatenate([high, low], axis=0)
    return jnp.pad(both, ((0, inner[0] - both.shape[0]), (0, inner[1] - both.shape[1])))[None]


def read_tail(message, count, heads):
    tail = message[-1].astype(jnp.float32)
    return [tail[i, :heads] + tail[count + i, :heads] for i in range(count)]


def scale(terms, coef):
    return [(view, c * coef) for view, c in terms]


def next_message(f_terms, g_terms, e_f, e_g, lower, last):
    if not last:
        return [f_terms, g_terms], jnp.stack([e_f, e_g])
    one = jnp.ones_like(e_f)
    sent = scale(f_terms, jnp.where(lower, one, e_g)) + scale(g_terms, jnp.where(lower, 0.0 * one, one))
    return [sent], jnp.stack([jnp.where(lower, e_f, e_f * e_g)])


def kernel_states(first_loc, second_loc, first_log, second_log, seq_pos, seq_count):
    heads = first_loc.shape[0]
    half = heads // 2
    units = seq_count // 2
    levels = max(units, 1).bit_length() - 1
    if seq_count % 2 or heads % 2 or levels < 1 or (1 << levels) != units:
        return block_states(first_loc, second_loc, first_log, second_log, seq_pos, seq_count)
    f32 = jnp.float32
    e1, e2 = jnp.exp(first_log), jnp.exp(second_log)
    core = seq_pos % 2
    upper = core == 1
    up = upper.astype(f32)
    unit = seq_pos // 2
    one = jnp.ones((half,), f32)
    pairs = [(i, i ^ 1) for i in range(seq_count)]
    inner = first_loc.shape[1:]
    sent = jnp.concatenate([first_loc, second_loc, tail_slot((e1, e2), inner, f32)], axis=0)
    got = lax.ppermute(sent, "seq", pairs)
    q1, q2 = read_tail(got, 2, heads)

    def mine(v):
        return lax.dynamic_slice_in_dim(v, core * half, half)

    e1h, e2h, q1h, q2h = mine(e1), mine(e2), mine(q1), mine(q2)
    mix = Mix(half)
    v_p1, v_p2 = mix.view(got, core * half), mix.view(got, heads + core * half)
    v_l1, v_l2 = mix.view(first_loc, core * half), mix.view(second_loc, core * half)
    f_terms = scale(v_l1, jnp.where(upper, one, q1h)) + scale(v_p1, jnp.where(upper, e1h, one))
    g_terms = scale(v_l2, jnp.where(upper, q2h, one)) + scale(v_p2, jnp.where(upper, one, e2h))
    low_terms = scale(v_p1, up * one) + scale(v_l1, (1 - up) * one)
    high_terms = scale(v_l2, up * one) + scale(v_p2, (1 - up) * one)
    e_f, e_g = e1h * q1h, e2h * q2h
    low_fe = jnp.where(upper, q1h, e1h)
    high_ge = jnp.where(upper, e2h, q2h)
    lower = unit % 2 == 0
    msg_terms, msg_e = next_message(f_terms, g_terms, e_f, e_g, lower, levels == 1)
    logical = [(f_terms, [(0, 0)]), (g_terms, [(0, 1)]), (low_terms, [(1, 0)]), (high_terms, [(1, 1)])]
    logical += [(t, [(2, b)]) for b, t in enumerate(msg_terms)]
    state, edges, msg = mix.run(
        logical,
        [(f32, 2), (f32, 2), (LINK, len(msg_terms))],
        [(tail_slot(list(msg_e), inner, LINK), 2)],
    )
    zero_h = jnp.zeros((half,), f32)
    e_pre, e_abv = one, one
    have_acc = False
    for level in range(levels):
        size = 1 << level
        lower = (unit // size) % 2 == 0
        last = level == levels - 1
        pairs = [(i, i ^ (2 * size)) for i in range(seq_count)]
        got = lax.ppermute(msg, "seq", pairs)
        got_e = read_tail(got, 1 if last else 2, half)
        mix = Mix(half)
        v_f, v_g = mix.view(state, 0), mix.view(state, half)
        if have_acc:
            v_pre, v_abv = mix.view(acc, 0), mix.view(acc, half)
        else:
            v_pre, v_abv = [], []
        if not last:
            p_f, p_g = got_e[0], got_e[1]
            w_f, w_g = mix.view(got, 0), mix.view(got, half)
            f_terms = scale(v_f, jnp.where(lower, p_f, one)) + scale(w_f, jnp.where(lower, one, e_f))
            g_terms = scale(v_g, jnp.where(lower, one, p_g)) + scale(w_g, jnp.where(lower, e_g, one))
            abv_terms = v_abv + scale(w_g, jnp.where(lower, e_abv, zero_h))
            pre_terms = v_pre + scale(w_f, jnp.where(lower, zero_h, e_pre))
            e_abv = jnp.where(lower, e_abv * p_g, e_abv)
            e_pre = jnp.where(lower, e_pre, e_pre * p_f)
            e_f, e_g = e_f * p_f, e_g * p_g
            next_lower = (unit // (2 * size)) % 2 == 0
            msg_terms, msg_e = next_message(f_terms, g_terms, e_f, e_g, next_lower, level + 1 == levels - 1)
            logical = [(f_terms, [(0, 0)]), (g_terms, [(0, 1)])]
            logical += [(pre_terms, [(1, 0)]), (abv_terms, [(1, 1)])]
            logical += [(t, [(2, b)]) for b, t in enumerate(msg_terms)]
            state, acc, msg = mix.run(
                logical,
                [(f32, 2), (f32, 2), (LINK, len(msg_terms))],
                [(tail_slot(list(msg_e), inner, LINK), 2)],
            )
            have_acc = True
        else:
            p_w = got_e[0]
            w = mix.view(got, 0)
            v_low, v_high = mix.view(edges, 0), mix.view(edges, half)
            first_terms = v_pre + scale(w, jnp.where(lower, zero_h, e_pre))
            second_terms = (
                v_abv
                + scale(v_f, jnp.where(lower, e_abv * p_w, e_abv))
                + scale(w, jnp.where(lower, e_abv, e_abv * e_f))
            )
            own_first = scale(first_terms, jnp.where(upper, low_fe, one)) + scale(v_low, up * one)
            own_second = scale(second_terms, jnp.where(upper, one, high_ge)) + scale(v_high, (1 - up) * one)
            other_first = scale(first_terms, jnp.where(upper, one, low_fe)) + scale(v_low, (1 - up) * one)
            other_second = scale(second_terms, jnp.where(upper, high_ge, one)) + scale(v_high, up * one)
            logical = [(own_first, [(0, 0)]), (own_second, [(0, 1)])]
            logical += [(other_first, [(1, 0)]), (other_second, [(1, 1)])]
            own, other = mix.run(logical, [(f32, 2), (f32, 2)])
    swapped = lax.ppermute(other, "seq", [(i, i ^ 1) for i in range(seq_count)])

    def whole(own_half, got_half):
        return jnp.where(
            upper,
            jnp.concatenate([got_half, own_half], axis=0),
            jnp.concatenate([own_half, got_half], axis=0),
        )

    return whole(own[:half], swapped[:half]), whole(own[half:], swapped[half:])


def on_device(
    inner_rows,
    gate_rows,
    input_proj,
    step_raw,
    decay_rate,
    skip_gain,
    conv_inner,
    conv_proj,
    norm_gain,
):
    tokens = inner_rows.shape[0]
    half_rows = tokens // 2
    head_count = step_raw.shape[1]
    inner_width = inner_rows.shape[1]
    group_count = input_proj.shape[1] // (2 * STATE)
    rim_rows = KERNEL - 1
    seq_count = lax.axis_size("seq")
    seq_pos = lax.axis_index("seq")
    is_last = seq_pos == seq_count - 1
    my_group = lax.axis_index("head") * head_count // GROUP_HEADS
    joined = jnp.concatenate([inner_rows, input_proj], axis=1)
    edge_rows = jnp.concatenate(
        [joined[tokens - rim_rows :], joined[half_rows - rim_rows : half_rows]], axis=0
    )
    extended = extended_2(edge_rows, (("seq", 0),), rim_rows)
    lead_first = extended[:rim_rows]
    lead_second = jnp.where(
        is_last, joined[half_rows - rim_rows : half_rows], extended[3 * rim_rows :]
    )
    conv_taps = jnp.concatenate([conv_inner, conv_proj], axis=1)
    step_size = jax.nn.softplus(step_raw)
    causal = jnp.arange(half_rows)[:, None] >= jnp.arange(half_rows)[None, :]

    def local_block(lead_rows, rows_in, block_step):
        padded = jnp.concatenate([lead_rows, rows_in], axis=0).astype(jnp.float32)
        conv_sum = jnp.zeros((half_rows, joined.shape[1]), jnp.float32)
        for offset in range(KERNEL):
            conv_sum = conv_sum + conv_taps[offset][None, :] * padded[offset : offset + half_rows]
        conv_out = jax.nn.silu(conv_sum).astype(jnp.bfloat16)
        inner_conv = conv_out[:, :inner_width].reshape(half_rows, head_count, HEAD_SIZE)
        b_rows = lax.dynamic_slice_in_dim(conv_out, inner_width + my_group * STATE, STATE, 1)
        c_rows = lax.dynamic_slice_in_dim(
            conv_out, inner_width + (group_count + my_group) * STATE, STATE, 1
        )
        log_cum = jnp.cumsum(-block_step * decay_rate[None, :], axis=0)
        score_grid = jnp.dot(c_rows, b_rows.T, preferred_element_type=jnp.float32)
        log_gap = log_cum.T[:, :, None] - log_cum.T[:, None, :]
        decay_grid = jnp.where(causal[None], jnp.exp(jnp.where(causal[None], log_gap, 0.0)), 0.0)
        weights = (score_grid[None] * decay_grid * block_step.T[:, None, :]).astype(jnp.bfloat16)
        intra_out = jnp.einsum(
            "hts,shp->thp", weights, inner_conv, preferred_element_type=jnp.float32
        )
        tail_decay = jnp.exp(log_cum[-1][None, :] - log_cum) * block_step
        x_weighted = (inner_conv.astype(jnp.float32) * tail_decay[:, :, None]).astype(jnp.bfloat16)
        local_state = jnp.einsum(
            "shp,sn->hpn", x_weighted, b_rows, preferred_element_type=jnp.float32
        )
        partial_out = intra_out + skip_gain[None, :, None] * inner_conv.astype(jnp.float32)
        return (partial_out, log_cum, c_rows, (jnp.exp(log_cum[-1]), local_state))

    def finish_block(partial_out, log_cum, c_rows, state_in):
        inter_out = jnp.einsum(
            "tn,hpn->thp", c_rows.astype(jnp.float32), state_in, precision=lax.Precision.HIGHEST
        )
        total_out = partial_out + jnp.exp(log_cum)[:, :, None] * inter_out
        return total_out.reshape(half_rows, inner_width)

    first_out, first_cum, first_c, first_elem = local_block(
        lead_first, joined[:half_rows], step_size[:half_rows]
    )
    second_out, second_cum, second_c, second_elem = local_block(
        lead_second, joined[half_rows:], step_size[half_rows:]
    )
    first_in, second_in = kernel_states(
        first_elem[1], second_elem[1], first_cum[-1], second_cum[-1], seq_pos, seq_count
    )
    ssm_out = jnp.concatenate(
        [
            finish_block(first_out, first_cum, first_c, first_in),
            finish_block(second_out, second_cum, second_c, second_in),
        ],
        axis=0,
    )
    gated = ssm_out * jax.nn.silu(gate_rows.astype(jnp.float32))
    partial_sq = jnp.sum(gated * gated, axis=1)
    other_sq = partner(partial_sq, "head", 0)
    mean_sq = (partial_sq + other_sq) / (GROUP_HEADS * HEAD_SIZE)
    normed = gated * lax.rsqrt(mean_sq + 1e-05)[:, None] * norm_gain[None, :]
    return normed.astype(jnp.bfloat16)


def solution(mesh):
    in_specs = (
        P("seq", "head"),
        P("seq", "head"),
        P("seq", None),
        P("seq", "head"),
        P("head"),
        P("head"),
        P(None, "head"),
        P(),
        P("head"),
    )
    out_specs = P("seq", "head")
    return jax.shard_map(
        on_device, mesh=mesh, in_specs=in_specs, out_specs=out_specs, check_vma=False
    )
```

```python
import jax
import jax.numpy as jnp
from jax import lax
from jax.sharding import PartitionSpec as P

HEAD_SIZE = 64
STATE = 128
GROUP_HEADS = 32
KERNEL = 4


def extended_2(block, sides, width):
    for axis, dim in sides:
        count = lax.axis_size(axis)
        forward = [(i, i + 1) for i in range(count - 1)]
        backward = [(target, source) for source, target in forward]
        tail, head = lax.optimization_barrier(
            (
                lax.slice_in_dim(block, block.shape[dim] - width, None, axis=dim),
                lax.slice_in_dim(block, 0, width, axis=dim),
            )
        )
        low = lax.ppermute(tail, axis, forward)
        high = lax.ppermute(head, axis, backward)
        block = jnp.concatenate([low, block, high], axis=dim)
    return block


def partner(array, axis, stride):
    return lax.ppermute(array, axis, [(i, i ^ 1 << stride) for i in range(lax.axis_size(axis))])


LINK = jnp.bfloat16


def pack(maps, decays, kind):
    flat = [m.reshape(-1, m.shape[-1]) for m in maps]
    lanes = flat[0].shape[1]
    rows = jnp.stack(decays)
    high = rows.astype(kind)
    low = (rows - high.astype(jnp.float32)).astype(kind)
    tail = jnp.concatenate([high, low], axis=0)
    tail = jnp.pad(tail, ((0, 8 - tail.shape[0]), (0, lanes - tail.shape[1])))
    return jnp.concatenate([f.astype(kind) for f in flat] + [tail], axis=0)


def unpack(message, count, shape):
    rows = shape[0] * shape[1]
    maps = [
        message[i * rows : (i + 1) * rows].astype(jnp.float32).reshape(shape) for i in range(count)
    ]
    tail = message[count * rows :].astype(jnp.float32)
    decays = [tail[i, : shape[0]] + tail[count + i, : shape[0]] for i in range(count)]
    return maps, decays


def col(v):
    return v[:, None, None]


def butterfly_states(sub_f, sub_g, e_f, e_g, index, count, stride, seq_count):
    levels = count.bit_length() - 1
    assert 1 << levels == count
    shape = sub_f.shape
    if levels == 0:
        return jnp.zeros_like(sub_f), sub_f
    ones = jnp.ones((shape[0],), jnp.float32)
    zeros = jnp.zeros((shape[0],), jnp.float32)
    prefix = jnp.zeros_like(sub_f)
    above = jnp.zeros_like(sub_f)
    e_pre, e_abv = ones, ones
    for level in range(levels):
        size = 1 << level
        lower = (index // size) % 2 == 0
        pairs = [(i, i ^ (size * stride)) for i in range(seq_count)]
        if level < levels - 1:
            got = lax.ppermute(pack((sub_f, sub_g), (e_f, e_g), LINK), "seq", pairs)
            (got_f, got_g), (p_f, p_g) = unpack(got, 2, shape)
            new_f = col(jnp.where(lower, p_f, ones)) * sub_f + col(jnp.where(lower, ones, e_f)) * got_f
            new_g = col(jnp.where(lower, ones, p_g)) * sub_g + col(jnp.where(lower, e_g, ones)) * got_g
            above = above + col(jnp.where(lower, e_abv, zeros)) * got_g
            prefix = prefix + col(jnp.where(lower, zeros, e_pre)) * got_f
            e_abv = jnp.where(lower, e_abv * p_g, e_abv)
            e_pre = jnp.where(lower, e_pre, e_pre * p_f)
            sub_f, sub_g = new_f, new_g
            e_f, e_g = e_f * p_f, e_g * p_g
        else:
            sent = col(jnp.where(lower, ones, e_g)) * sub_f + col(jnp.where(lower, zeros, ones)) * sub_g
            sent_e = jnp.where(lower, e_f, e_f * e_g)
            got = lax.ppermute(pack((sent,), (sent_e,), LINK), "seq", pairs)
            (got_w,), (p_w,) = unpack(got, 1, shape)
            first_in = prefix + col(jnp.where(lower, zeros, e_pre)) * got_w
            second_in = (
                above
                + col(jnp.where(lower, e_abv * p_w, e_abv)) * sub_f
                + col(jnp.where(lower, e_abv, e_abv * e_f)) * got_w
            )
    return first_in, second_in


def block_states(first_loc, second_loc, first_log, second_log, seq_pos, seq_count):
    heads = first_loc.shape[0]
    e1, e2 = jnp.exp(first_log), jnp.exp(second_log)
    if seq_count % 2 or heads % 2:
        return butterfly_states(first_loc, second_loc, e1, e2, seq_pos, seq_count, 1, seq_count)
    half = heads // 2
    core = seq_pos % 2
    upper = core == 1
    pairs = [(i, i ^ 1) for i in range(seq_count)]

    def part(x, which):
        return lax.dynamic_slice_in_dim(x, which * half, half, 0)

    theirs = 1 - core
    sent = pack(
        (part(first_loc, theirs), part(second_loc, theirs)), (part(e1, theirs), part(e2, theirs)), jnp.float32
    )
    got = lax.ppermute(sent, "seq", pairs)
    (p1, p2), (q1, q2) = unpack(got, 2, (half, *first_loc.shape[1:]))
    l1, l2, e1h, e2h = part(first_loc, core), part(second_loc, core), part(e1, core), part(e2, core)
    ones = jnp.ones((half,), jnp.float32)
    pair_f = col(jnp.where(upper, ones, q1)) * l1 + col(jnp.where(upper, e1h, ones)) * p1
    pair_g = col(jnp.where(upper, q2, ones)) * l2 + col(jnp.where(upper, ones, e2h)) * p2
    low_f = jnp.where(upper, p1, l1)
    low_fe = jnp.where(upper, q1, e1h)
    high_g = jnp.where(upper, l2, p2)
    high_ge = jnp.where(upper, e2h, q2)

    prefix, wrapped = butterfly_states(
        pair_f, pair_g, e1h * q1, e2h * q2, seq_pos // 2, seq_count // 2, 2, seq_count
    )
    after_low = col(low_fe) * prefix + low_f
    before_high = col(high_ge) * wrapped + high_g
    own = (jnp.where(upper, after_low, prefix), jnp.where(upper, wrapped, before_high))
    other = (jnp.where(upper, prefix, after_low), jnp.where(upper, before_high, wrapped))
    got_1, got_2 = lax.ppermute(other, "seq", pairs)

    def whole(own_half, got_half):
        return jnp.where(
            upper,
            jnp.concatenate([got_half, own_half], axis=0),
            jnp.concatenate([own_half, got_half], axis=0),
        )

    return whole(own[0], got_1), whole(own[1], got_2)


def on_device(
    inner_rows,
    gate_rows,
    input_proj,
    step_raw,
    decay_rate,
    skip_gain,
    conv_inner,
    conv_proj,
    norm_gain,
):
    tokens = inner_rows.shape[0]
    half_rows = tokens // 2
    head_count = step_raw.shape[1]
    inner_width = inner_rows.shape[1]
    group_count = input_proj.shape[1] // (2 * STATE)
    rim_rows = KERNEL - 1
    seq_count = lax.axis_size("seq")
    seq_pos = lax.axis_index("seq")
    is_last = seq_pos == seq_count - 1
    my_group = lax.axis_index("head") * head_count // GROUP_HEADS
    joined = jnp.concatenate([inner_rows, input_proj], axis=1)
    edge_rows = jnp.concatenate(
        [joined[tokens - rim_rows :], joined[half_rows - rim_rows : half_rows]], axis=0
    )
    extended = extended_2(edge_rows, (("seq", 0),), rim_rows)
    lead_first = extended[:rim_rows]
    lead_second = jnp.where(
        is_last, joined[half_rows - rim_rows : half_rows], extended[3 * rim_rows :]
    )
    conv_taps = jnp.concatenate([conv_inner, conv_proj], axis=1)
    step_size = jax.nn.softplus(step_raw)
    causal = jnp.arange(half_rows)[:, None] >= jnp.arange(half_rows)[None, :]

    def local_block(lead_rows, rows_in, block_step):
        padded = jnp.concatenate([lead_rows, rows_in], axis=0).astype(jnp.float32)
        conv_sum = jnp.zeros((half_rows, joined.shape[1]), jnp.float32)
        for offset in range(KERNEL):
            conv_sum = conv_sum + conv_taps[offset][None, :] * padded[offset : offset + half_rows]
        conv_out = jax.nn.silu(conv_sum).astype(jnp.bfloat16)
        inner_conv = conv_out[:, :inner_width].reshape(half_rows, head_count, HEAD_SIZE)
        b_rows = lax.dynamic_slice_in_dim(conv_out, inner_width + my_group * STATE, STATE, 1)
        c_rows = lax.dynamic_slice_in_dim(
            conv_out, inner_width + (group_count + my_group) * STATE, STATE, 1
        )
        log_cum = jnp.cumsum(-block_step * decay_rate[None, :], axis=0)
        score_grid = jnp.dot(c_rows, b_rows.T, preferred_element_type=jnp.float32)
        log_gap = log_cum.T[:, :, None] - log_cum.T[:, None, :]
        decay_grid = jnp.where(causal[None], jnp.exp(jnp.where(causal[None], log_gap, 0.0)), 0.0)
        weights = (score_grid[None] * decay_grid * block_step.T[:, None, :]).astype(jnp.bfloat16)
        intra_out = jnp.einsum(
            "hts,shp->thp", weights, inner_conv, preferred_element_type=jnp.float32
        )
        tail_decay = jnp.exp(log_cum[-1][None, :] - log_cum) * block_step
        x_weighted = (inner_conv.astype(jnp.float32) * tail_decay[:, :, None]).astype(jnp.bfloat16)
        local_state = jnp.einsum(
            "shp,sn->hpn", x_weighted, b_rows, preferred_element_type=jnp.float32
        )
        partial_out = intra_out + skip_gain[None, :, None] * inner_conv.astype(jnp.float32)
        return (partial_out, log_cum, c_rows, (jnp.exp(log_cum[-1]), local_state))

    def finish_block(partial_out, log_cum, c_rows, state_in):
        inter_out = jnp.einsum(
            "tn,hpn->thp", c_rows.astype(jnp.float32), state_in, precision=lax.Precision.HIGHEST
        )
        total_out = partial_out + jnp.exp(log_cum)[:, :, None] * inter_out
        return total_out.reshape(half_rows, inner_width)

    first_out, first_cum, first_c, first_elem = local_block(
        lead_first, joined[:half_rows], step_size[:half_rows]
    )
    second_out, second_cum, second_c, second_elem = local_block(
        lead_second, joined[half_rows:], step_size[half_rows:]
    )
    first_in, second_in = block_states(
        first_elem[1], second_elem[1], first_cum[-1], second_cum[-1], seq_pos, seq_count
    )
    ssm_out = jnp.concatenate(
        [
            finish_block(first_out, first_cum, first_c, first_in),
            finish_block(second_out, second_cum, second_c, second_in),
        ],
        axis=0,
    )
    gated = ssm_out * jax.nn.silu(gate_rows.astype(jnp.float32))
    partial_sq = jnp.sum(gated * gated, axis=1)
    other_sq = partner(partial_sq, "head", 0)
    mean_sq = (partial_sq + other_sq) / (GROUP_HEADS * HEAD_SIZE)
    normed = gated * lax.rsqrt(mean_sq + 1e-05)[:, None] * norm_gain[None, :]
    return normed.astype(jnp.bfloat16)


def solution(mesh):
    in_specs = (
        P("seq", "head"),
        P("seq", "head"),
        P("seq", None),
        P("seq", "head"),
        P("head"),
        P("head"),
        P(None, "head"),
        P(),
        P("head"),
    )
    out_specs = P("seq", "head")
    return jax.shard_map(
        on_device, mesh=mesh, in_specs=in_specs, out_specs=out_specs, check_vma=False
    )
```

```python
import jax
import jax.numpy as jnp
from jax import lax
from jax.sharding import PartitionSpec as P

HEAD_SIZE = 64
STATE = 128
GROUP_HEADS = 32
KERNEL = 4


def extended_2(block, sides, width):
    for axis, dim in sides:
        count = lax.axis_size(axis)
        forward = [(i, i + 1) for i in range(count - 1)]
        backward = [(target, source) for source, target in forward]
        tail, head = lax.optimization_barrier(
            (
                lax.slice_in_dim(block, block.shape[dim] - width, None, axis=dim),
                lax.slice_in_dim(block, 0, width, axis=dim),
            )
        )
        low = lax.ppermute(tail, axis, forward)
        high = lax.ppermute(head, axis, backward)
        block = jnp.concatenate([low, block, high], axis=dim)
    return block


def partner(array, axis, stride):
    return lax.ppermute(array, axis, [(i, i ^ 1 << stride) for i in range(lax.axis_size(axis))])


LINK = jnp.bfloat16


def pack(maps, decays, kind):
    flat = [m.reshape(-1, m.shape[-1]) for m in maps]
    lanes = flat[0].shape[1]
    rows = jnp.stack(decays)
    high = rows.astype(kind)
    low = (rows - high.astype(jnp.float32)).astype(kind)
    tail = jnp.concatenate([high, low], axis=0)
    tail = jnp.pad(tail, ((0, 8 - tail.shape[0]), (0, lanes - tail.shape[1])))
    return jnp.concatenate([f.astype(kind) for f in flat] + [tail], axis=0)


def unpack(message, count, shape):
    rows = shape[0] * shape[1]
    maps = [
        message[i * rows : (i + 1) * rows].astype(jnp.float32).reshape(shape) for i in range(count)
    ]
    tail = message[count * rows :].astype(jnp.float32)
    decays = [tail[i, : shape[0]] + tail[count + i, : shape[0]] for i in range(count)]
    return maps, decays


def col(v):
    return v[:, None, None]


def butterfly_states(sub_f, sub_g, e_f, e_g, index, count, stride, seq_count):
    levels = count.bit_length() - 1
    assert 1 << levels == count
    shape = sub_f.shape
    if levels == 0:
        return jnp.zeros_like(sub_f), sub_f
    ones = jnp.ones((shape[0],), jnp.float32)
    zeros = jnp.zeros((shape[0],), jnp.float32)
    prefix = jnp.zeros_like(sub_f)
    above = jnp.zeros_like(sub_f)
    e_pre, e_abv = ones, ones
    for level in range(levels):
        size = 1 << level
        lower = (index // size) % 2 == 0
        pairs = [(i, i ^ (size * stride)) for i in range(seq_count)]
        if level < levels - 1:
            got = lax.ppermute(pack((sub_f, sub_g), (e_f, e_g), LINK), "seq", pairs)
            (got_f, got_g), (p_f, p_g) = unpack(got, 2, shape)
            new_f = col(jnp.where(lower, p_f, ones)) * sub_f + col(jnp.where(lower, ones, e_f)) * got_f
            new_g = col(jnp.where(lower, ones, p_g)) * sub_g + col(jnp.where(lower, e_g, ones)) * got_g
            above = above + col(jnp.where(lower, e_abv, zeros)) * got_g
            prefix = prefix + col(jnp.where(lower, zeros, e_pre)) * got_f
            e_abv = jnp.where(lower, e_abv * p_g, e_abv)
            e_pre = jnp.where(lower, e_pre, e_pre * p_f)
            sub_f, sub_g = new_f, new_g
            e_f, e_g = e_f * p_f, e_g * p_g
        else:
            sent = col(jnp.where(lower, ones, e_g)) * sub_f + col(jnp.where(lower, zeros, ones)) * sub_g
            sent_e = jnp.where(lower, e_f, e_f * e_g)
            got = lax.ppermute(pack((sent,), (sent_e,), LINK), "seq", pairs)
            (got_w,), (p_w,) = unpack(got, 1, shape)
            first_in = prefix + col(jnp.where(lower, zeros, e_pre)) * got_w
            second_in = (
                above
                + col(jnp.where(lower, e_abv * p_w, e_abv)) * sub_f
                + col(jnp.where(lower, e_abv, e_abv * e_f)) * got_w
            )
    return first_in, second_in


def block_states(first_loc, second_loc, first_log, second_log, seq_pos, seq_count):
    heads = first_loc.shape[0]
    e1, e2 = jnp.exp(first_log), jnp.exp(second_log)
    if seq_count % 2 or heads % 2:
        return butterfly_states(first_loc, second_loc, e1, e2, seq_pos, seq_count, 1, seq_count)
    half = heads // 2
    core = seq_pos % 2
    upper = core == 1
    pairs = [(i, i ^ 1) for i in range(seq_count)]

    def part(x, which):
        return lax.dynamic_slice_in_dim(x, which * half, half, 0)

    theirs = 1 - core
    sent = pack(
        (part(first_loc, theirs), part(second_loc, theirs)), (part(e1, theirs), part(e2, theirs)), jnp.float32
    )
    got = lax.ppermute(sent, "seq", pairs)
    (p1, p2), (q1, q2) = unpack(got, 2, (half, *first_loc.shape[1:]))
    l1, l2, e1h, e2h = part(first_loc, core), part(second_loc, core), part(e1, core), part(e2, core)
    ones = jnp.ones((half,), jnp.float32)
    pair_f = col(jnp.where(upper, ones, q1)) * l1 + col(jnp.where(upper, e1h, ones)) * p1
    pair_g = col(jnp.where(upper, q2, ones)) * l2 + col(jnp.where(upper, ones, e2h)) * p2
    low_f = jnp.where(upper, p1, l1)
    low_fe = jnp.where(upper, q1, e1h)
    high_g = jnp.where(upper, l2, p2)
    high_ge = jnp.where(upper, e2h, q2)

    prefix, wrapped = butterfly_states(
        pair_f, pair_g, e1h * q1, e2h * q2, seq_pos // 2, seq_count // 2, 2, seq_count
    )
    after_low = col(low_fe) * prefix + low_f
    before_high = col(high_ge) * wrapped + high_g
    own = (jnp.where(upper, after_low, prefix), jnp.where(upper, wrapped, before_high))
    other = (jnp.where(upper, prefix, after_low), jnp.where(upper, before_high, wrapped))
    got_1, got_2 = lax.ppermute(other, "seq", pairs)

    def whole(own_half, got_half):
        return jnp.where(
            upper,
            jnp.concatenate([got_half, own_half], axis=0),
            jnp.concatenate([own_half, got_half], axis=0),
        )

    return whole(own[0], got_1), whole(own[1], got_2)


def on_device(
    inner_rows,
    gate_rows,
    input_proj,
    step_raw,
    decay_rate,
    skip_gain,
    conv_inner,
    conv_proj,
    norm_gain,
):
    tokens = inner_rows.shape[0]
    half_rows = tokens // 2
    head_count = step_raw.shape[1]
    inner_width = inner_rows.shape[1]
    group_count = input_proj.shape[1] // (2 * STATE)
    rim_rows = KERNEL - 1
    seq_count = lax.axis_size("seq")
    seq_pos = lax.axis_index("seq")
    is_last = seq_pos == seq_count - 1
    my_group = lax.axis_index("head") * head_count // GROUP_HEADS

    def edges(rows):
        return jnp.concatenate(
            [rows[tokens - rim_rows :], rows[half_rows - rim_rows : half_rows]], axis=0
        )

    edge_rows = jnp.concatenate([edges(inner_rows), edges(input_proj)], axis=1)
    extended = extended_2(edge_rows, (("seq", 0),), rim_rows)
    lead_first = extended[:rim_rows]
    lead_second = jnp.where(
        is_last, edge_rows[rim_rows:], extended[3 * rim_rows :]
    )
    step_size = jax.nn.softplus(step_raw)
    causal = jnp.arange(half_rows)[:, None] >= jnp.arange(half_rows)[None, :]

    def conv(lead_rows, rows_in, taps):
        padded = jnp.concatenate([lead_rows, rows_in], axis=0).astype(jnp.float32)
        conv_sum = jnp.zeros((half_rows, rows_in.shape[1]), jnp.float32)
        for offset in range(KERNEL):
            conv_sum = conv_sum + taps[offset][None, :] * padded[offset : offset + half_rows]
        return jax.nn.silu(conv_sum).astype(jnp.bfloat16)

    def local_block(lead_rows, inner_in, proj_in, block_step):
        inner_out = conv(lead_rows[:, :inner_width], inner_in, conv_inner)
        proj_out = conv(lead_rows[:, inner_width:], proj_in, conv_proj)
        inner_conv = inner_out.reshape(half_rows, head_count, HEAD_SIZE)
        b_rows = lax.dynamic_slice_in_dim(proj_out, my_group * STATE, STATE, 1)
        c_rows = lax.dynamic_slice_in_dim(proj_out, (group_count + my_group) * STATE, STATE, 1)
        log_cum = jnp.cumsum(-block_step * decay_rate[None, :], axis=0)
        score_grid = jnp.dot(c_rows, b_rows.T, preferred_element_type=jnp.float32)
        log_gap = log_cum.T[:, :, None] - log_cum.T[:, None, :]
        decay_grid = jnp.where(causal[None], jnp.exp(jnp.where(causal[None], log_gap, 0.0)), 0.0)
        weights = (score_grid[None] * decay_grid * block_step.T[:, None, :]).astype(jnp.bfloat16)
        intra_out = jnp.einsum(
            "hts,shp->thp", weights, inner_conv, preferred_element_type=jnp.float32
        )
        tail_decay = jnp.exp(log_cum[-1][None, :] - log_cum) * block_step
        x_weighted = (inner_conv.astype(jnp.float32) * tail_decay[:, :, None]).astype(jnp.bfloat16)
        local_state = jnp.einsum(
            "shp,sn->hpn", x_weighted, b_rows, preferred_element_type=jnp.float32
        )
        partial_out = intra_out + skip_gain[None, :, None] * inner_conv.astype(jnp.float32)
        return (partial_out, log_cum, c_rows, (jnp.exp(log_cum[-1]), local_state))

    def finish_block(partial_out, log_cum, c_rows, state_in):
        inter_out = jnp.einsum(
            "tn,hpn->thp", c_rows.astype(jnp.float32), state_in, precision=lax.Precision.HIGHEST
        )
        total_out = partial_out + jnp.exp(log_cum)[:, :, None] * inter_out
        return total_out.reshape(half_rows, inner_width)

    first_out, first_cum, first_c, first_elem = local_block(
        lead_first, inner_rows[:half_rows], input_proj[:half_rows], step_size[:half_rows]
    )
    second_out, second_cum, second_c, second_elem = local_block(
        lead_second, inner_rows[half_rows:], input_proj[half_rows:], step_size[half_rows:]
    )
    first_in, second_in = block_states(
        first_elem[1], second_elem[1], first_cum[-1], second_cum[-1], seq_pos, seq_count
    )
    ssm_out = jnp.concatenate(
        [
            finish_block(first_out, first_cum, first_c, first_in),
            finish_block(second_out, second_cum, second_c, second_in),
        ],
        axis=0,
    )
    gated = ssm_out * jax.nn.silu(gate_rows.astype(jnp.float32))
    partial_sq = jnp.sum(gated * gated, axis=1)
    other_sq = partner(partial_sq, "head", 0)
    mean_sq = (partial_sq + other_sq) / (GROUP_HEADS * HEAD_SIZE)
    normed = gated * lax.rsqrt(mean_sq + 1e-05)[:, None] * norm_gain[None, :]
    return normed.astype(jnp.bfloat16)


def solution(mesh):
    in_specs = (
        P("seq", "head"),
        P("seq", "head"),
        P("seq", None),
        P("seq", "head"),
        P("head"),
        P("head"),
        P(None, "head"),
        P(),
        P("head"),
    )
    out_specs = P("seq", "head")
    return jax.shard_map(
        on_device, mesh=mesh, in_specs=in_specs, out_specs=out_specs, check_vma=False
    )
```

```python
import jax
import jax.numpy as jnp
from jax import lax
from jax.sharding import PartitionSpec as P

HEAD_SIZE = 64
STATE = 128
GROUP_HEADS = 32
KERNEL = 4


def extended_2(block, sides, width):
    for axis, dim in sides:
        count = lax.axis_size(axis)
        forward = [(i, i + 1) for i in range(count - 1)]
        backward = [(target, source) for source, target in forward]
        tail, head = lax.optimization_barrier(
            (
                lax.slice_in_dim(block, block.shape[dim] - width, None, axis=dim),
                lax.slice_in_dim(block, 0, width, axis=dim),
            )
        )
        low = lax.ppermute(tail, axis, forward)
        high = lax.ppermute(head, axis, backward)
        block = jnp.concatenate([low, block, high], axis=dim)
    return block


def partner(array, axis, stride):
    return lax.ppermute(array, axis, [(i, i ^ 1 << stride) for i in range(lax.axis_size(axis))])


LINK = jnp.bfloat16


def pack(maps, decays, kind):
    flat = [m.reshape(-1, m.shape[-1]) for m in maps]
    lanes = flat[0].shape[1]
    rows = jnp.stack(decays)
    high = rows.astype(kind)
    low = (rows - high.astype(jnp.float32)).astype(kind)
    tail = jnp.concatenate([high, low], axis=0)
    tail = jnp.pad(tail, ((0, 8 - tail.shape[0]), (0, lanes - tail.shape[1])))
    return jnp.concatenate([f.astype(kind) for f in flat] + [tail], axis=0)


def unpack(message, count, shape):
    rows = shape[0] * shape[1]
    maps = [
        message[i * rows : (i + 1) * rows].astype(jnp.float32).reshape(shape) for i in range(count)
    ]
    tail = message[count * rows :].astype(jnp.float32)
    decays = [tail[i, : shape[0]] + tail[count + i, : shape[0]] for i in range(count)]
    return maps, decays


def col(v):
    return v[:, None, None]


def to_link(x, rows):
    high = x.astype(LINK)
    low = (x - high.astype(jnp.float32)).astype(LINK)
    row = lax.broadcasted_iota(jnp.int32, x.shape, x.ndim - 2)
    return jnp.where(row == rows + 1, low, high)


def from_link(m, rows):
    x = m.astype(jnp.float32)
    return x, x[..., rows : rows + 1, :] + x[..., rows + 1 : rows + 2, :]


def butterfly_states(sub_f, sub_g, e_f, e_g, index, count, stride, seq_count):
    levels = count.bit_length() - 1
    assert 1 << levels == count
    heads, rows, lanes = sub_f.shape
    if levels == 0:
        return jnp.zeros_like(sub_f), sub_f
    shape = (heads, rows + 8, lanes)

    def with_decay(x, e):
        return jnp.concatenate([x, jnp.broadcast_to(e[:, None, None], (heads, 8, lanes))], axis=1)

    is_map = lax.broadcasted_iota(jnp.int32, shape, 1) < rows

    def decay(x):
        return x[:, rows : rows + 1, :]

    ones = jnp.ones((heads,), jnp.float32)
    zeros = jnp.zeros((heads,), jnp.float32)
    big_f, big_g = with_decay(sub_f, e_f), with_decay(sub_g, e_g)
    prefix = with_decay(jnp.zeros_like(sub_f), ones)
    above = with_decay(jnp.zeros_like(sub_f), ones)

    def last_message(f, g, lower):
        ef, eg = decay(f), decay(g)
        body = jnp.where(lower, f, eg * f + g)
        return jnp.where(is_map, body, jnp.where(lower, ef, ef * eg))

    first_lower = index % 2 == 0
    if levels == 1:
        msg = to_link(last_message(big_f, big_g, first_lower)[None], rows)
    else:
        msg = to_link(jnp.stack([big_f, big_g]), rows)
    for level in range(levels):
        size = 1 << level
        lower = (index // size) % 2 == 0
        pairs = [(i, i ^ (size * stride)) for i in range(seq_count)]
        got, got_e = from_link(lax.ppermute(msg, "seq", pairs), rows)
        e_f, e_g, e_pre, e_abv = decay(big_f), decay(big_g), decay(prefix), decay(above)
        if level < levels - 1:
            got_f, got_g = got[0], got[1]
            p_f, p_g = got_e[0], got_e[1]
            new_f = jnp.where(
                is_map,
                jnp.where(lower, p_f * big_f + got_f, big_f + e_f * got_f),
                e_f * p_f,
            )
            new_g = jnp.where(
                is_map,
                jnp.where(lower, big_g + e_g * got_g, p_g * big_g + got_g),
                e_g * p_g,
            )
            above = jnp.where(
                is_map,
                jnp.where(lower, above + e_abv * got_g, above),
                jnp.where(lower, e_abv * p_g, e_abv),
            )
            prefix = jnp.where(
                is_map,
                jnp.where(lower, prefix, prefix + e_pre * got_f),
                jnp.where(lower, e_pre, e_pre * p_f),
            )
            big_f, big_g = new_f, new_g
            next_lower = (index // (2 * size)) % 2 == 0
            if level + 1 == levels - 1:
                msg = to_link(last_message(big_f, big_g, next_lower)[None], rows)
            else:
                msg = to_link(jnp.stack([big_f, big_g]), rows)
        else:
            got_w, p_w = got[0], got_e[0]
            first_in = jnp.where(lower, prefix, prefix + e_pre * got_w)
            second_in = jnp.where(
                lower,
                above + e_abv * p_w * big_f + e_abv * got_w,
                above + e_abv * big_f + e_abv * e_f * got_w,
            )
    return first_in[:, :rows], second_in[:, :rows]


def block_states(first_loc, second_loc, first_log, second_log, seq_pos, seq_count):
    heads = first_loc.shape[0]
    e1, e2 = jnp.exp(first_log), jnp.exp(second_log)
    if seq_count % 2 or heads % 2:
        return butterfly_states(first_loc, second_loc, e1, e2, seq_pos, seq_count, 1, seq_count)
    half = heads // 2
    core = seq_pos % 2
    upper = core == 1
    pairs = [(i, i ^ 1) for i in range(seq_count)]

    def part(x, which):
        return lax.dynamic_slice_in_dim(x, which * half, half, 0)

    theirs = 1 - core
    sent = pack(
        (part(first_loc, theirs), part(second_loc, theirs)), (part(e1, theirs), part(e2, theirs)), jnp.float32
    )
    got = lax.ppermute(sent, "seq", pairs)
    (p1, p2), (q1, q2) = unpack(got, 2, (half, *first_loc.shape[1:]))
    l1, l2, e1h, e2h = part(first_loc, core), part(second_loc, core), part(e1, core), part(e2, core)
    ones = jnp.ones((half,), jnp.float32)
    pair_f = col(jnp.where(upper, ones, q1)) * l1 + col(jnp.where(upper, e1h, ones)) * p1
    pair_g = col(jnp.where(upper, q2, ones)) * l2 + col(jnp.where(upper, ones, e2h)) * p2
    low_f = jnp.where(upper, p1, l1)
    low_fe = jnp.where(upper, q1, e1h)
    high_g = jnp.where(upper, l2, p2)
    high_ge = jnp.where(upper, e2h, q2)

    prefix, wrapped = butterfly_states(
        pair_f, pair_g, e1h * q1, e2h * q2, seq_pos // 2, seq_count // 2, 2, seq_count
    )
    after_low = col(low_fe) * prefix + low_f
    before_high = col(high_ge) * wrapped + high_g
    own = (jnp.where(upper, after_low, prefix), jnp.where(upper, wrapped, before_high))
    other = (jnp.where(upper, prefix, after_low), jnp.where(upper, before_high, wrapped))
    got_1, got_2 = lax.ppermute(other, "seq", pairs)

    def whole(own_half, got_half):
        return jnp.where(
            upper,
            jnp.concatenate([got_half, own_half], axis=0),
            jnp.concatenate([own_half, got_half], axis=0),
        )

    return whole(own[0], got_1), whole(own[1], got_2)


def on_device(
    inner_rows,
    gate_rows,
    input_proj,
    step_raw,
    decay_rate,
    skip_gain,
    conv_inner,
    conv_proj,
    norm_gain,
):
    tokens = inner_rows.shape[0]
    half_rows = tokens // 2
    head_count = step_raw.shape[1]
    inner_width = inner_rows.shape[1]
    group_count = input_proj.shape[1] // (2 * STATE)
    rim_rows = KERNEL - 1
    seq_count = lax.axis_size("seq")
    seq_pos = lax.axis_index("seq")
    is_last = seq_pos == seq_count - 1
    my_group = lax.axis_index("head") * head_count // GROUP_HEADS

    def edges(rows):
        return jnp.concatenate(
            [rows[tokens - rim_rows :], rows[half_rows - rim_rows : half_rows]], axis=0
        )

    edge_rows = jnp.concatenate([edges(inner_rows), edges(input_proj)], axis=1)
    extended = extended_2(edge_rows, (("seq", 0),), rim_rows)
    lead_first = extended[:rim_rows]
    lead_second = jnp.where(
        is_last, edge_rows[rim_rows:], extended[3 * rim_rows :]
    )
    step_size = jax.nn.softplus(step_raw)
    causal = jnp.arange(half_rows)[:, None] >= jnp.arange(half_rows)[None, :]

    def conv(lead_rows, rows_in, taps):
        padded = jnp.concatenate([lead_rows, rows_in], axis=0).astype(jnp.float32)
        conv_sum = jnp.zeros((half_rows, rows_in.shape[1]), jnp.float32)
        for offset in range(KERNEL):
            conv_sum = conv_sum + taps[offset][None, :] * padded[offset : offset + half_rows]
        return jax.nn.silu(conv_sum).astype(jnp.bfloat16)

    def local_block(lead_rows, inner_in, proj_in, block_step):
        inner_out = conv(lead_rows[:, :inner_width], inner_in, conv_inner)
        proj_out = conv(lead_rows[:, inner_width:], proj_in, conv_proj)
        inner_conv = inner_out.reshape(half_rows, head_count, HEAD_SIZE)
        b_rows = lax.dynamic_slice_in_dim(proj_out, my_group * STATE, STATE, 1)
        c_rows = lax.dynamic_slice_in_dim(proj_out, (group_count + my_group) * STATE, STATE, 1)
        log_cum = jnp.cumsum(-block_step * decay_rate[None, :], axis=0)
        score_grid = jnp.dot(c_rows, b_rows.T, preferred_element_type=jnp.float32)
        log_gap = log_cum.T[:, :, None] - log_cum.T[:, None, :]
        decay_grid = jnp.where(causal[None], jnp.exp(jnp.where(causal[None], log_gap, 0.0)), 0.0)
        weights = (score_grid[None] * decay_grid * block_step.T[:, None, :]).astype(jnp.bfloat16)
        intra_out = jnp.einsum(
            "hts,shp->thp", weights, inner_conv, preferred_element_type=jnp.float32
        )
        tail_decay = jnp.exp(log_cum[-1][None, :] - log_cum) * block_step
        x_weighted = (inner_conv.astype(jnp.float32) * tail_decay[:, :, None]).astype(jnp.bfloat16)
        local_state = jnp.einsum(
            "shp,sn->hpn", x_weighted, b_rows, preferred_element_type=jnp.float32
        )
        partial_out = intra_out + skip_gain[None, :, None] * inner_conv.astype(jnp.float32)
        return (partial_out, log_cum, c_rows, (jnp.exp(log_cum[-1]), local_state))

    def finish_block(partial_out, log_cum, c_rows, state_in):
        inter_out = jnp.einsum(
            "tn,hpn->thp", c_rows.astype(jnp.float32), state_in, precision=lax.Precision.HIGHEST
        )
        total_out = partial_out + jnp.exp(log_cum)[:, :, None] * inter_out
        return total_out.reshape(half_rows, inner_width)

    first_out, first_cum, first_c, first_elem = local_block(
        lead_first, inner_rows[:half_rows], input_proj[:half_rows], step_size[:half_rows]
    )
    second_out, second_cum, second_c, second_elem = local_block(
        lead_second, inner_rows[half_rows:], input_proj[half_rows:], step_size[half_rows:]
    )
    first_in, second_in = block_states(
        first_elem[1], second_elem[1], first_cum[-1], second_cum[-1], seq_pos, seq_count
    )
    ssm_out = jnp.concatenate(
        [
            finish_block(first_out, first_cum, first_c, first_in),
            finish_block(second_out, second_cum, second_c, second_in),
        ],
        axis=0,
    )
    gated = ssm_out * jax.nn.silu(gate_rows.astype(jnp.float32))
    partial_sq = jnp.sum(gated * gated, axis=1)
    other_sq = partner(partial_sq, "head", 0)
    mean_sq = (partial_sq + other_sq) / (GROUP_HEADS * HEAD_SIZE)
    normed = gated * lax.rsqrt(mean_sq + 1e-05)[:, None] * norm_gain[None, :]
    return normed.astype(jnp.bfloat16)


def solution(mesh):
    in_specs = (
        P("seq", "head"),
        P("seq", "head"),
        P("seq", None),
        P("seq", "head"),
        P("head"),
        P("head"),
        P(None, "head"),
        P(),
        P("head"),
    )
    out_specs = P("seq", "head")
    return jax.shard_map(
        on_device, mesh=mesh, in_specs=in_specs, out_specs=out_specs, check_vma=False
    )
```

```python
import jax
import jax.numpy as jnp
from jax import lax
from jax.sharding import PartitionSpec as P

HEAD_SIZE = 64
STATE = 128
GROUP_HEADS = 32
KERNEL = 4


def extended_2(block, sides, width):
    for axis, dim in sides:
        count = lax.axis_size(axis)
        forward = [(i, i + 1) for i in range(count - 1)]
        backward = [(target, source) for source, target in forward]
        tail, head = lax.optimization_barrier(
            (
                lax.slice_in_dim(block, block.shape[dim] - width, None, axis=dim),
                lax.slice_in_dim(block, 0, width, axis=dim),
            )
        )
        low = lax.ppermute(tail, axis, forward)
        high = lax.ppermute(head, axis, backward)
        block = jnp.concatenate([low, block, high], axis=dim)
    return block


def partner(array, axis, stride):
    return lax.ppermute(array, axis, [(i, i ^ 1 << stride) for i in range(lax.axis_size(axis))])


LINK = jnp.bfloat16


def pack(maps, decays, kind):
    flat = [m.reshape(-1, m.shape[-1]) for m in maps]
    lanes = flat[0].shape[1]
    rows = jnp.stack(decays)
    high = rows.astype(kind)
    low = (rows - high.astype(jnp.float32)).astype(kind)
    tail = jnp.concatenate([high, low], axis=0)
    tail = jnp.pad(tail, ((0, 8 - tail.shape[0]), (0, lanes - tail.shape[1])))
    return jnp.concatenate([f.astype(kind) for f in flat] + [tail], axis=0)


def unpack(message, count, shape):
    rows = shape[0] * shape[1]
    maps = [
        message[i * rows : (i + 1) * rows].astype(jnp.float32).reshape(shape) for i in range(count)
    ]
    tail = message[count * rows :].astype(jnp.float32)
    decays = [tail[i, : shape[0]] + tail[count + i, : shape[0]] for i in range(count)]
    return maps, decays


def col(v):
    return v[:, None, None]


def to_link(x, rows):
    high = x.astype(LINK)
    low = (x - high.astype(jnp.float32)).astype(LINK)
    row = lax.broadcasted_iota(jnp.int32, x.shape, x.ndim - 2)
    return jnp.where(row == rows + 1, low, high)


def from_link(m, rows):
    x = m.astype(jnp.float32)
    return x, x[..., rows : rows + 1, :] + x[..., rows + 1 : rows + 2, :]


def butterfly_states(sub_f, sub_g, e_f, e_g, index, count, stride, seq_count):
    levels = count.bit_length() - 1
    assert 1 << levels == count
    heads, rows, lanes = sub_f.shape
    if levels == 0:
        return jnp.zeros_like(sub_f), sub_f
    shape = (heads, rows + 8, lanes)

    def with_decay(x, e):
        return jnp.concatenate([x, jnp.broadcast_to(e[:, None, None], (heads, 8, lanes))], axis=1)

    is_map = lax.broadcasted_iota(jnp.int32, shape, 1) < rows

    def decay(x):
        return x[:, rows : rows + 1, :]

    ones = jnp.ones((heads,), jnp.float32)
    zeros = jnp.zeros((heads,), jnp.float32)
    big_f, big_g = with_decay(sub_f, e_f), with_decay(sub_g, e_g)
    prefix = with_decay(jnp.zeros_like(sub_f), ones)
    above = with_decay(jnp.zeros_like(sub_f), ones)

    def last_message(f, g, lower):
        ef, eg = decay(f), decay(g)
        body = jnp.where(lower, f, eg * f + g)
        return jnp.where(is_map, body, jnp.where(lower, ef, ef * eg))

    first_lower = index % 2 == 0
    if levels == 1:
        msg = to_link(last_message(big_f, big_g, first_lower)[None], rows)
    else:
        msg = to_link(jnp.stack([big_f, big_g]), rows)
    for level in range(levels):
        size = 1 << level
        lower = (index // size) % 2 == 0
        pairs = [(i, i ^ (size * stride)) for i in range(seq_count)]
        got, got_e = from_link(lax.ppermute(msg, "seq", pairs), rows)
        e_f, e_g, e_pre, e_abv = decay(big_f), decay(big_g), decay(prefix), decay(above)
        if level < levels - 1:
            got_f, got_g = got[0], got[1]
            p_f, p_g = got_e[0], got_e[1]
            new_f = jnp.where(
                is_map,
                jnp.where(lower, p_f * big_f + got_f, big_f + e_f * got_f),
                e_f * p_f,
            )
            new_g = jnp.where(
                is_map,
                jnp.where(lower, big_g + e_g * got_g, p_g * big_g + got_g),
                e_g * p_g,
            )
            above = jnp.where(
                is_map,
                jnp.where(lower, above + e_abv * got_g, above),
                jnp.where(lower, e_abv * p_g, e_abv),
            )
            prefix = jnp.where(
                is_map,
                jnp.where(lower, prefix, prefix + e_pre * got_f),
                jnp.where(lower, e_pre, e_pre * p_f),
            )
            big_f, big_g = new_f, new_g
            next_lower = (index // (2 * size)) % 2 == 0
            if level + 1 == levels - 1:
                msg = to_link(last_message(big_f, big_g, next_lower)[None], rows)
            else:
                msg = to_link(jnp.stack([big_f, big_g]), rows)
        else:
            got_w, p_w = got[0], got_e[0]
            first_in = jnp.where(lower, prefix, prefix + e_pre * got_w)
            second_in = jnp.where(
                lower,
                above + e_abv * p_w * big_f + e_abv * got_w,
                above + e_abv * big_f + e_abv * e_f * got_w,
            )
    return first_in[:, :rows], second_in[:, :rows]


def block_states(first_loc, second_loc, first_log, second_log, seq_pos, seq_count):
    heads = first_loc.shape[0]
    e1, e2 = jnp.exp(first_log), jnp.exp(second_log)
    if seq_count % 2 or heads % 2:
        return butterfly_states(first_loc, second_loc, e1, e2, seq_pos, seq_count, 1, seq_count)
    half = heads // 2
    core = seq_pos % 2
    upper = core == 1
    pairs = [(i, i ^ 1) for i in range(seq_count)]

    def part(x, which):
        return lax.dynamic_slice_in_dim(x, which * half, half, 0)

    theirs = 1 - core
    sent = pack(
        (part(first_loc, theirs), part(second_loc, theirs)), (part(e1, theirs), part(e2, theirs)), jnp.float32
    )
    got = lax.ppermute(sent, "seq", pairs)
    (p1, p2), (q1, q2) = unpack(got, 2, (half, *first_loc.shape[1:]))
    l1, l2, e1h, e2h = part(first_loc, core), part(second_loc, core), part(e1, core), part(e2, core)
    ones = jnp.ones((half,), jnp.float32)
    pair_f = col(jnp.where(upper, ones, q1)) * l1 + col(jnp.where(upper, e1h, ones)) * p1
    pair_g = col(jnp.where(upper, q2, ones)) * l2 + col(jnp.where(upper, ones, e2h)) * p2
    low_f = jnp.where(upper, p1, l1)
    low_fe = jnp.where(upper, q1, e1h)
    high_g = jnp.where(upper, l2, p2)
    high_ge = jnp.where(upper, e2h, q2)

    prefix, wrapped = butterfly_states(
        pair_f, pair_g, e1h * q1, e2h * q2, seq_pos // 2, seq_count // 2, 2, seq_count
    )
    after_low = col(low_fe) * prefix + low_f
    before_high = col(high_ge) * wrapped + high_g
    own = (jnp.where(upper, after_low, prefix), jnp.where(upper, wrapped, before_high))
    other = (jnp.where(upper, prefix, after_low), jnp.where(upper, before_high, wrapped))
    got_1, got_2 = lax.ppermute(other, "seq", pairs)

    def whole(own_half, got_half):
        return jnp.where(
            upper,
            jnp.concatenate([got_half, own_half], axis=0),
            jnp.concatenate([own_half, got_half], axis=0),
        )

    return whole(own[0], got_1), whole(own[1], got_2)


def on_device(
    inner_rows,
    gate_rows,
    input_proj,
    step_raw,
    decay_rate,
    skip_gain,
    conv_inner,
    conv_proj,
    norm_gain,
):
    tokens = inner_rows.shape[0]
    half_rows = tokens // 2
    head_count = step_raw.shape[1]
    inner_width = inner_rows.shape[1]
    group_count = input_proj.shape[1] // (2 * STATE)
    rim_rows = KERNEL - 1
    seq_count = lax.axis_size("seq")
    seq_pos = lax.axis_index("seq")
    is_last = seq_pos == seq_count - 1
    my_group = lax.axis_index("head") * head_count // GROUP_HEADS

    def edges(rows):
        return jnp.concatenate(
            [rows[tokens - rim_rows :], rows[half_rows - rim_rows : half_rows]], axis=0
        )

    edge_rows = jnp.concatenate([edges(inner_rows), edges(input_proj)], axis=1)
    extended = extended_2(edge_rows, (("seq", 0),), rim_rows)
    lead_first = extended[:rim_rows]
    lead_second = jnp.where(
        is_last, edge_rows[rim_rows:], extended[3 * rim_rows :]
    )
    step_size = jax.nn.softplus(step_raw)
    causal = jnp.arange(half_rows)[:, None] >= jnp.arange(half_rows)[None, :]

    def conv(lead_rows, rows_in, taps):
        padded = jnp.concatenate([lead_rows, rows_in], axis=0).astype(jnp.float32)
        conv_sum = jnp.zeros((half_rows, rows_in.shape[1]), jnp.float32)
        for offset in range(KERNEL):
            conv_sum = conv_sum + taps[offset][None, :] * padded[offset : offset + half_rows]
        return jax.nn.silu(conv_sum).astype(jnp.bfloat16)

    def local_block(lead_rows, inner_in, proj_in, block_step):
        inner_out = conv(lead_rows[:, :inner_width], inner_in, conv_inner)
        proj_out = conv(lead_rows[:, inner_width:], proj_in, conv_proj)
        inner_conv = inner_out.reshape(half_rows, head_count, HEAD_SIZE)
        b_rows = lax.dynamic_slice_in_dim(proj_out, my_group * STATE, STATE, 1)
        c_rows = lax.dynamic_slice_in_dim(proj_out, (group_count + my_group) * STATE, STATE, 1)
        log_cum = jnp.cumsum(-block_step * decay_rate[None, :], axis=0)
        score_grid = jnp.dot(c_rows, b_rows.T, preferred_element_type=jnp.float32)
        log_gap = log_cum.T[:, :, None] - log_cum.T[:, None, :]
        decay_grid = jnp.where(causal[None], jnp.exp(jnp.where(causal[None], log_gap, 0.0)), 0.0)
        weights = (score_grid[None] * decay_grid * block_step.T[:, None, :]).astype(jnp.bfloat16)
        intra_out = jnp.einsum(
            "hts,shp->thp", weights, inner_conv, preferred_element_type=jnp.float32
        )
        tail_decay = jnp.exp(log_cum[-1][None, :] - log_cum) * block_step
        x_weighted = (inner_conv.astype(jnp.float32) * tail_decay[:, :, None]).astype(jnp.bfloat16)
        local_state = jnp.einsum(
            "shp,sn->hpn", x_weighted, b_rows, preferred_element_type=jnp.float32
        )
        partial_out = intra_out + skip_gain[None, :, None] * inner_conv.astype(jnp.float32)
        return (partial_out, log_cum, c_rows, (jnp.exp(log_cum[-1]), local_state))

    def finish_block(partial_out, log_cum, c_rows, state_in):
        inter_out = jnp.einsum(
            "tn,hpn->thp", c_rows.astype(jnp.float32), state_in, precision=lax.Precision.HIGHEST
        )
        total_out = partial_out + jnp.exp(log_cum)[:, :, None] * inter_out
        return total_out.reshape(half_rows, inner_width)

    first_out, first_cum, first_c, first_elem = local_block(
        lead_first, inner_rows[:half_rows], input_proj[:half_rows], step_size[:half_rows]
    )
    second_out, second_cum, second_c, second_elem = local_block(
        lead_second, inner_rows[half_rows:], input_proj[half_rows:], step_size[half_rows:]
    )
    gate_act, first_out, second_out = lax.optimization_barrier(
        (jax.nn.silu(gate_rows.astype(jnp.float32)), first_out, second_out)
    )
    first_in, second_in = block_states(
        first_elem[1], second_elem[1], first_cum[-1], second_cum[-1], seq_pos, seq_count
    )
    ssm_out = jnp.concatenate(
        [
            finish_block(first_out, first_cum, first_c, first_in),
            finish_block(second_out, second_cum, second_c, second_in),
        ],
        axis=0,
    )
    gated = ssm_out * gate_act
    partial_sq = jnp.sum(gated * gated, axis=1)
    other_sq = partner(partial_sq, "head", 0)
    mean_sq = (partial_sq + other_sq) / (GROUP_HEADS * HEAD_SIZE)
    normed = gated * lax.rsqrt(mean_sq + 1e-05)[:, None] * norm_gain[None, :]
    return normed.astype(jnp.bfloat16)


def solution(mesh):
    in_specs = (
        P("seq", "head"),
        P("seq", "head"),
        P("seq", None),
        P("seq", "head"),
        P("head"),
        P("head"),
        P(None, "head"),
        P(),
        P("head"),
    )
    out_specs = P("seq", "head")
    return jax.shard_map(
        on_device, mesh=mesh, in_specs=in_specs, out_specs=out_specs, check_vma=False
    )
```

```python
import jax
import jax.numpy as jnp
from jax import lax
from jax.sharding import PartitionSpec as P

HEAD_SIZE = 64
STATE = 128
GROUP_HEADS = 32
KERNEL = 4


def extended_2(block, sides, width):
    for axis, dim in sides:
        count = lax.axis_size(axis)
        forward = [(i, i + 1) for i in range(count - 1)]
        backward = [(target, source) for source, target in forward]
        tail, head = lax.optimization_barrier(
            (
                lax.slice_in_dim(block, block.shape[dim] - width, None, axis=dim),
                lax.slice_in_dim(block, 0, width, axis=dim),
            )
        )
        low = lax.ppermute(tail, axis, forward)
        high = lax.ppermute(head, axis, backward)
        block = jnp.concatenate([low, block, high], axis=dim)
    return block


def partner(array, axis, stride):
    return lax.ppermute(array, axis, [(i, i ^ 1 << stride) for i in range(lax.axis_size(axis))])


LINK = jnp.bfloat16


def pack(maps, decays, kind):
    flat = [m.reshape(-1, m.shape[-1]) for m in maps]
    lanes = flat[0].shape[1]
    rows = jnp.stack(decays)
    high = rows.astype(kind)
    low = (rows - high.astype(jnp.float32)).astype(kind)
    tail = jnp.concatenate([high, low], axis=0)
    tail = jnp.pad(tail, ((0, 8 - tail.shape[0]), (0, lanes - tail.shape[1])))
    return jnp.concatenate([f.astype(kind) for f in flat] + [tail], axis=0)


def unpack(message, count, shape):
    rows = shape[0] * shape[1]
    maps = [
        message[i * rows : (i + 1) * rows].astype(jnp.float32).reshape(shape) for i in range(count)
    ]
    tail = message[count * rows :].astype(jnp.float32)
    decays = [tail[i, : shape[0]] + tail[count + i, : shape[0]] for i in range(count)]
    return maps, decays


def col(v):
    return v[:, None, None]


def to_link(x, rows):
    high = x.astype(LINK)
    low = (x - high.astype(jnp.float32)).astype(LINK)
    row = lax.broadcasted_iota(jnp.int32, x.shape, x.ndim - 2)
    return jnp.where(row == rows + 1, low, high)


def from_link(m, rows):
    x = m.astype(jnp.float32)
    return x, x[..., rows : rows + 1, :] + x[..., rows + 1 : rows + 2, :]


def butterfly_states(sub_f, sub_g, e_f, e_g, index, count, stride, seq_count):
    levels = count.bit_length() - 1
    assert 1 << levels == count
    heads, rows, lanes = sub_f.shape
    if levels == 0:
        return jnp.zeros_like(sub_f), sub_f
    shape = (heads, rows + 8, lanes)

    def with_decay(x, e):
        return jnp.concatenate([x, jnp.broadcast_to(e[:, None, None], (heads, 8, lanes))], axis=1)

    is_map = lax.broadcasted_iota(jnp.int32, shape, 1) < rows

    def decay(x):
        return x[:, rows : rows + 1, :]

    ones = jnp.ones((heads,), jnp.float32)
    zeros = jnp.zeros((heads,), jnp.float32)
    big_f, big_g = with_decay(sub_f, e_f), with_decay(sub_g, e_g)
    prefix = with_decay(jnp.zeros_like(sub_f), ones)
    above = with_decay(jnp.zeros_like(sub_f), ones)

    def last_message(f, g, lower):
        ef, eg = decay(f), decay(g)
        body = jnp.where(lower, f, eg * f + g)
        return jnp.where(is_map, body, jnp.where(lower, ef, ef * eg))

    first_lower = index % 2 == 0
    if levels == 1:
        msg = to_link(last_message(big_f, big_g, first_lower)[None], rows)
    else:
        msg = to_link(jnp.stack([big_f, big_g]), rows)
    for level in range(levels):
        size = 1 << level
        lower = (index // size) % 2 == 0
        pairs = [(i, i ^ (size * stride)) for i in range(seq_count)]
        got, got_e = from_link(lax.ppermute(msg, "seq", pairs), rows)
        e_f, e_g, e_pre, e_abv = decay(big_f), decay(big_g), decay(prefix), decay(above)
        if level < levels - 1:
            got_f, got_g = got[0], got[1]
            p_f, p_g = got_e[0], got_e[1]
            new_f = jnp.where(
                is_map,
                jnp.where(lower, p_f * big_f + got_f, big_f + e_f * got_f),
                e_f * p_f,
            )
            new_g = jnp.where(
                is_map,
                jnp.where(lower, big_g + e_g * got_g, p_g * big_g + got_g),
                e_g * p_g,
            )
            above = jnp.where(
                is_map,
                jnp.where(lower, above + e_abv * got_g, above),
                jnp.where(lower, e_abv * p_g, e_abv),
            )
            prefix = jnp.where(
                is_map,
                jnp.where(lower, prefix, prefix + e_pre * got_f),
                jnp.where(lower, e_pre, e_pre * p_f),
            )
            big_f, big_g = new_f, new_g
            next_lower = (index // (2 * size)) % 2 == 0
            if level + 1 == levels - 1:
                msg = to_link(last_message(big_f, big_g, next_lower)[None], rows)
            else:
                msg = to_link(jnp.stack([big_f, big_g]), rows)
        else:
            got_w, p_w = got[0], got_e[0]
            first_in = jnp.where(lower, prefix, prefix + e_pre * got_w)
            second_in = jnp.where(
                lower,
                above + e_abv * p_w * big_f + e_abv * got_w,
                above + e_abv * big_f + e_abv * e_f * got_w,
            )
    return first_in[:, :rows], second_in[:, :rows]


def block_states(first_loc, second_loc, first_log, second_log, seq_pos, seq_count):
    heads = first_loc.shape[0]
    e1, e2 = jnp.exp(first_log), jnp.exp(second_log)
    if seq_count % 2 or heads % 2:
        return butterfly_states(first_loc, second_loc, e1, e2, seq_pos, seq_count, 1, seq_count)
    half = heads // 2
    core = seq_pos % 2
    upper = core == 1
    pairs = [(i, i ^ 1) for i in range(seq_count)]

    def part(x, which):
        return lax.dynamic_slice_in_dim(x, which * half, half, 0)

    theirs = 1 - core
    sent = pack(
        (part(first_loc, theirs), part(second_loc, theirs)), (part(e1, theirs), part(e2, theirs)), jnp.float32
    )
    got = lax.ppermute(sent, "seq", pairs)
    (p1, p2), (q1, q2) = unpack(got, 2, (half, *first_loc.shape[1:]))
    l1, l2, e1h, e2h = part(first_loc, core), part(second_loc, core), part(e1, core), part(e2, core)
    ones = jnp.ones((half,), jnp.float32)
    pair_f = col(jnp.where(upper, ones, q1)) * l1 + col(jnp.where(upper, e1h, ones)) * p1
    pair_g = col(jnp.where(upper, q2, ones)) * l2 + col(jnp.where(upper, ones, e2h)) * p2
    low_f = jnp.where(upper, p1, l1)
    low_fe = jnp.where(upper, q1, e1h)
    high_g = jnp.where(upper, l2, p2)
    high_ge = jnp.where(upper, e2h, q2)

    prefix, wrapped = butterfly_states(
        pair_f, pair_g, e1h * q1, e2h * q2, seq_pos // 2, seq_count // 2, 2, seq_count
    )
    after_low = col(low_fe) * prefix + low_f
    before_high = col(high_ge) * wrapped + high_g
    own = (jnp.where(upper, after_low, prefix), jnp.where(upper, wrapped, before_high))
    other = jnp.stack([jnp.where(upper, prefix, after_low), jnp.where(upper, before_high, wrapped)])
    got_1, got_2 = lax.ppermute(other, "seq", pairs)

    def whole(own_half, got_half):
        return jnp.where(
            upper,
            jnp.concatenate([got_half, own_half], axis=0),
            jnp.concatenate([own_half, got_half], axis=0),
        )

    return whole(own[0], got_1), whole(own[1], got_2)


def on_device(
    inner_rows,
    gate_rows,
    input_proj,
    step_raw,
    decay_rate,
    skip_gain,
    conv_inner,
    conv_proj,
    norm_gain,
):
    tokens = inner_rows.shape[0]
    half_rows = tokens // 2
    head_count = step_raw.shape[1]
    inner_width = inner_rows.shape[1]
    group_count = input_proj.shape[1] // (2 * STATE)
    rim_rows = KERNEL - 1
    seq_count = lax.axis_size("seq")
    seq_pos = lax.axis_index("seq")
    is_last = seq_pos == seq_count - 1
    my_group = lax.axis_index("head") * head_count // GROUP_HEADS

    def edges(rows):
        return jnp.concatenate(
            [rows[tokens - rim_rows :], rows[half_rows - rim_rows : half_rows]], axis=0
        )

    edge_rows = jnp.concatenate([edges(inner_rows), edges(input_proj)], axis=1)
    extended = extended_2(edge_rows, (("seq", 0),), rim_rows)
    lead_first = extended[:rim_rows]
    lead_second = jnp.where(
        is_last, edge_rows[rim_rows:], extended[3 * rim_rows :]
    )
    step_size = jax.nn.softplus(step_raw)
    causal = jnp.arange(half_rows)[:, None] >= jnp.arange(half_rows)[None, :]

    def conv(lead_rows, rows_in, taps):
        padded = jnp.concatenate([lead_rows, rows_in], axis=0).astype(jnp.float32)
        conv_sum = jnp.zeros((half_rows, rows_in.shape[1]), jnp.float32)
        for offset in range(KERNEL):
            conv_sum = conv_sum + taps[offset][None, :] * padded[offset : offset + half_rows]
        return jax.nn.silu(conv_sum).astype(jnp.bfloat16)

    def local_block(lead_rows, inner_in, proj_in, block_step):
        inner_out = conv(lead_rows[:, :inner_width], inner_in, conv_inner)
        proj_out = conv(lead_rows[:, inner_width:], proj_in, conv_proj)
        inner_conv = inner_out.reshape(half_rows, head_count, HEAD_SIZE)
        b_rows = lax.dynamic_slice_in_dim(proj_out, my_group * STATE, STATE, 1)
        c_rows = lax.dynamic_slice_in_dim(proj_out, (group_count + my_group) * STATE, STATE, 1)
        log_cum = jnp.cumsum(-block_step * decay_rate[None, :], axis=0)
        score_grid = jnp.dot(c_rows, b_rows.T, preferred_element_type=jnp.float32)
        log_gap = log_cum.T[:, :, None] - log_cum.T[:, None, :]
        decay_grid = jnp.where(causal[None], jnp.exp(jnp.where(causal[None], log_gap, 0.0)), 0.0)
        weights = (score_grid[None] * decay_grid * block_step.T[:, None, :]).astype(jnp.bfloat16)
        intra_out = jnp.einsum(
            "hts,shp->thp", weights, inner_conv, preferred_element_type=jnp.float32
        )
        tail_decay = jnp.exp(log_cum[-1][None, :] - log_cum) * block_step
        x_weighted = (inner_conv.astype(jnp.float32) * tail_decay[:, :, None]).astype(jnp.bfloat16)
        local_state = jnp.einsum(
            "shp,sn->hpn", x_weighted, b_rows, preferred_element_type=jnp.float32
        )
        partial_out = intra_out + skip_gain[None, :, None] * inner_conv.astype(jnp.float32)
        return (partial_out, log_cum, c_rows, (jnp.exp(log_cum[-1]), local_state))

    def finish_block(partial_out, log_cum, c_rows, state_in):
        inter_out = jnp.einsum(
            "tn,hpn->thp", c_rows.astype(jnp.float32), state_in, precision=lax.Precision.HIGHEST
        )
        total_out = partial_out + jnp.exp(log_cum)[:, :, None] * inter_out
        return total_out.reshape(half_rows, inner_width)

    first_out, first_cum, first_c, first_elem = local_block(
        lead_first, inner_rows[:half_rows], input_proj[:half_rows], step_size[:half_rows]
    )
    second_out, second_cum, second_c, second_elem = local_block(
        lead_second, inner_rows[half_rows:], input_proj[half_rows:], step_size[half_rows:]
    )
    first_in, second_in = block_states(
        first_elem[1], second_elem[1], first_cum[-1], second_cum[-1], seq_pos, seq_count
    )
    ssm_out = jnp.concatenate(
        [
            finish_block(first_out, first_cum, first_c, first_in),
            finish_block(second_out, second_cum, second_c, second_in),
        ],
        axis=0,
    )
    gated = ssm_out * jax.nn.silu(gate_rows.astype(jnp.float32))
    partial_sq = jnp.sum(gated * gated, axis=1)
    other_sq = partner(partial_sq, "head", 0)
    mean_sq = (partial_sq + other_sq) / (GROUP_HEADS * HEAD_SIZE)
    normed = gated * lax.rsqrt(mean_sq + 1e-05)[:, None] * norm_gain[None, :]
    return normed.astype(jnp.bfloat16)


def solution(mesh):
    in_specs = (
        P("seq", "head"),
        P("seq", "head"),
        P("seq", None),
        P("seq", "head"),
        P("head"),
        P("head"),
        P(None, "head"),
        P(),
        P("head"),
    )
    out_specs = P("seq", "head")
    return jax.shard_map(
        on_device, mesh=mesh, in_specs=in_specs, out_specs=out_specs, check_vma=False
    )
```

```python
import jax
import jax.numpy as jnp
from jax import lax
from jax.sharding import PartitionSpec as P

HEAD_SIZE = 64
STATE = 128
GROUP_HEADS = 32
KERNEL = 4


def extended_2(block, sides, width):
    for axis, dim in sides:
        count = lax.axis_size(axis)
        forward = [(i, (i + 1) % count) for i in range(count)]
        backward = [(target, source) for source, target in forward]
        tail, head = lax.optimization_barrier(
            (
                lax.slice_in_dim(block, block.shape[dim] - width, None, axis=dim),
                lax.slice_in_dim(block, 0, width, axis=dim),
            )
        )
        low = lax.ppermute(tail, axis, forward)
        high = lax.ppermute(head, axis, backward)
        low = jnp.where(lax.axis_index(axis) == 0, jnp.zeros_like(low), low)
        high = jnp.where(lax.axis_index(axis) == count - 1, jnp.zeros_like(high), high)
        block = jnp.concatenate([low, block, high], axis=dim)
    return block


def partner(array, axis, stride):
    return lax.ppermute(array, axis, [(i, i ^ 1 << stride) for i in range(lax.axis_size(axis))])


LINK = jnp.bfloat16


def pack(maps, decays, kind):
    flat = [m.reshape(-1, m.shape[-1]) for m in maps]
    lanes = flat[0].shape[1]
    rows = jnp.stack(decays)
    high = rows.astype(kind)
    low = (rows - high.astype(jnp.float32)).astype(kind)
    tail = jnp.concatenate([high, low], axis=0)
    tail = jnp.pad(tail, ((0, 8 - tail.shape[0]), (0, lanes - tail.shape[1])))
    return jnp.concatenate([f.astype(kind) for f in flat] + [tail], axis=0)


def unpack(message, count, shape):
    rows = shape[0] * shape[1]
    maps = [
        message[i * rows : (i + 1) * rows].astype(jnp.float32).reshape(shape) for i in range(count)
    ]
    tail = message[count * rows :].astype(jnp.float32)
    decays = [tail[i, : shape[0]] + tail[count + i, : shape[0]] for i in range(count)]
    return maps, decays


def col(v):
    return v[:, None, None]


def to_link(x, rows):
    high = x.astype(LINK)
    low = (x - high.astype(jnp.float32)).astype(LINK)
    row = lax.broadcasted_iota(jnp.int32, x.shape, x.ndim - 2)
    return jnp.where(row == rows + 1, low, high)


def from_link(m, rows):
    x = m.astype(jnp.float32)
    return x, x[..., rows : rows + 1, :] + x[..., rows + 1 : rows + 2, :]


def butterfly_states(sub_f, sub_g, e_f, e_g, index, count, stride, seq_count):
    levels = count.bit_length() - 1
    assert 1 << levels == count
    heads, rows, lanes = sub_f.shape
    if levels == 0:
        return jnp.zeros_like(sub_f), sub_f
    shape = (heads, rows + 8, lanes)

    def with_decay(x, e):
        return jnp.concatenate([x, jnp.broadcast_to(e[:, None, None], (heads, 8, lanes))], axis=1)

    is_map = lax.broadcasted_iota(jnp.int32, shape, 1) < rows

    def decay(x):
        return x[:, rows : rows + 1, :]

    ones = jnp.ones((heads,), jnp.float32)
    zeros = jnp.zeros((heads,), jnp.float32)
    big_f, big_g = with_decay(sub_f, e_f), with_decay(sub_g, e_g)
    prefix = with_decay(jnp.zeros_like(sub_f), ones)
    above = with_decay(jnp.zeros_like(sub_f), ones)

    def last_message(f, g, lower):
        ef, eg = decay(f), decay(g)
        body = jnp.where(lower, f, eg * f + g)
        return jnp.where(is_map, body, jnp.where(lower, ef, ef * eg))

    first_lower = index % 2 == 0
    if levels == 1:
        msg = to_link(last_message(big_f, big_g, first_lower)[None], rows)
    else:
        msg = to_link(jnp.stack([big_f, big_g]), rows)
    for level in range(levels):
        size = 1 << level
        lower = (index // size) % 2 == 0
        pairs = [(i, i ^ (size * stride)) for i in range(seq_count)]
        got, got_e = from_link(lax.ppermute(msg, "seq", pairs), rows)
        e_f, e_g, e_pre, e_abv = decay(big_f), decay(big_g), decay(prefix), decay(above)
        if level < levels - 1:
            got_f, got_g = got[0], got[1]
            p_f, p_g = got_e[0], got_e[1]
            new_f = jnp.where(
                is_map,
                jnp.where(lower, p_f * big_f + got_f, big_f + e_f * got_f),
                e_f * p_f,
            )
            new_g = jnp.where(
                is_map,
                jnp.where(lower, big_g + e_g * got_g, p_g * big_g + got_g),
                e_g * p_g,
            )
            above = jnp.where(
                is_map,
                jnp.where(lower, above + e_abv * got_g, above),
                jnp.where(lower, e_abv * p_g, e_abv),
            )
            prefix = jnp.where(
                is_map,
                jnp.where(lower, prefix, prefix + e_pre * got_f),
                jnp.where(lower, e_pre, e_pre * p_f),
            )
            big_f, big_g = new_f, new_g
            next_lower = (index // (2 * size)) % 2 == 0
            if level + 1 == levels - 1:
                msg = to_link(last_message(big_f, big_g, next_lower)[None], rows)
            else:
                msg = to_link(jnp.stack([big_f, big_g]), rows)
        else:
            got_w, p_w = got[0], got_e[0]
            first_in = jnp.where(lower, prefix, prefix + e_pre * got_w)
            second_in = jnp.where(
                lower,
                above + e_abv * p_w * big_f + e_abv * got_w,
                above + e_abv * big_f + e_abv * e_f * got_w,
            )
    return first_in[:, :rows], second_in[:, :rows]


def block_states(first_loc, second_loc, first_log, second_log, seq_pos, seq_count):
    heads = first_loc.shape[0]
    e1, e2 = jnp.exp(first_log), jnp.exp(second_log)
    if seq_count % 2 or heads % 2:
        return butterfly_states(first_loc, second_loc, e1, e2, seq_pos, seq_count, 1, seq_count)
    half = heads // 2
    core = seq_pos % 2
    upper = core == 1
    pairs = [(i, i ^ 1) for i in range(seq_count)]

    def part(x, which):
        return lax.dynamic_slice_in_dim(x, which * half, half, 0)

    theirs = 1 - core
    sent = pack(
        (part(first_loc, theirs), part(second_loc, theirs)), (part(e1, theirs), part(e2, theirs)), jnp.float32
    )
    got = lax.ppermute(sent, "seq", pairs)
    (p1, p2), (q1, q2) = unpack(got, 2, (half, *first_loc.shape[1:]))
    l1, l2, e1h, e2h = part(first_loc, core), part(second_loc, core), part(e1, core), part(e2, core)
    ones = jnp.ones((half,), jnp.float32)
    pair_f = col(jnp.where(upper, ones, q1)) * l1 + col(jnp.where(upper, e1h, ones)) * p1
    pair_g = col(jnp.where(upper, q2, ones)) * l2 + col(jnp.where(upper, ones, e2h)) * p2
    low_f = jnp.where(upper, p1, l1)
    low_fe = jnp.where(upper, q1, e1h)
    high_g = jnp.where(upper, l2, p2)
    high_ge = jnp.where(upper, e2h, q2)

    prefix, wrapped = butterfly_states(
        pair_f, pair_g, e1h * q1, e2h * q2, seq_pos // 2, seq_count // 2, 2, seq_count
    )
    after_low = col(low_fe) * prefix + low_f
    before_high = col(high_ge) * wrapped + high_g
    own = (jnp.where(upper, after_low, prefix), jnp.where(upper, wrapped, before_high))
    other = jnp.stack([jnp.where(upper, prefix, after_low), jnp.where(upper, before_high, wrapped)])
    got_1, got_2 = lax.ppermute(other, "seq", pairs)

    def whole(own_half, got_half):
        return jnp.where(
            upper,
            jnp.concatenate([got_half, own_half], axis=0),
            jnp.concatenate([own_half, got_half], axis=0),
        )

    return whole(own[0], got_1), whole(own[1], got_2)


def on_device(
    inner_rows,
    gate_rows,
    input_proj,
    step_raw,
    decay_rate,
    skip_gain,
    conv_inner,
    conv_proj,
    norm_gain,
):
    tokens = inner_rows.shape[0]
    half_rows = tokens // 2
    head_count = step_raw.shape[1]
    inner_width = inner_rows.shape[1]
    group_count = input_proj.shape[1] // (2 * STATE)
    rim_rows = KERNEL - 1
    seq_count = lax.axis_size("seq")
    seq_pos = lax.axis_index("seq")
    is_last = seq_pos == seq_count - 1
    my_group = lax.axis_index("head") * head_count // GROUP_HEADS

    def edges(rows):
        return jnp.concatenate(
            [rows[tokens - rim_rows :], rows[half_rows - rim_rows : half_rows]], axis=0
        )

    edge_rows = jnp.concatenate([edges(inner_rows), edges(input_proj)], axis=1)
    extended = extended_2(edge_rows, (("seq", 0),), rim_rows)
    lead_first = extended[:rim_rows]
    lead_second = jnp.where(
        is_last, edge_rows[rim_rows:], extended[3 * rim_rows :]
    )
    step_size = jax.nn.softplus(step_raw)
    causal = jnp.arange(half_rows)[:, None] >= jnp.arange(half_rows)[None, :]

    def conv(lead_rows, rows_in, taps):
        padded = jnp.concatenate([lead_rows, rows_in], axis=0).astype(jnp.float32)
        conv_sum = jnp.zeros((half_rows, rows_in.shape[1]), jnp.float32)
        for offset in range(KERNEL):
            conv_sum = conv_sum + taps[offset][None, :] * padded[offset : offset + half_rows]
        return jax.nn.silu(conv_sum).astype(jnp.bfloat16)

    def local_block(lead_rows, inner_in, proj_in, block_step):
        inner_out = conv(lead_rows[:, :inner_width], inner_in, conv_inner)
        proj_out = conv(lead_rows[:, inner_width:], proj_in, conv_proj)
        inner_conv = inner_out.reshape(half_rows, head_count, HEAD_SIZE)
        b_rows = lax.dynamic_slice_in_dim(proj_out, my_group * STATE, STATE, 1)
        c_rows = lax.dynamic_slice_in_dim(proj_out, (group_count + my_group) * STATE, STATE, 1)
        log_cum = jnp.cumsum(-block_step * decay_rate[None, :], axis=0)
        score_grid = jnp.dot(c_rows, b_rows.T, preferred_element_type=jnp.float32)
        log_gap = log_cum.T[:, :, None] - log_cum.T[:, None, :]
        decay_grid = jnp.where(causal[None], jnp.exp(jnp.where(causal[None], log_gap, 0.0)), 0.0)
        weights = (score_grid[None] * decay_grid * block_step.T[:, None, :]).astype(jnp.bfloat16)
        intra_out = jnp.einsum(
            "hts,shp->thp", weights, inner_conv, preferred_element_type=jnp.float32
        )
        tail_decay = jnp.exp(log_cum[-1][None, :] - log_cum) * block_step
        x_weighted = (inner_conv.astype(jnp.float32) * tail_decay[:, :, None]).astype(jnp.bfloat16)
        local_state = jnp.einsum(
            "shp,sn->hpn", x_weighted, b_rows, preferred_element_type=jnp.float32
        )
        partial_out = intra_out + skip_gain[None, :, None] * inner_conv.astype(jnp.float32)
        return (partial_out, log_cum, c_rows, (jnp.exp(log_cum[-1]), local_state))

    def finish_block(partial_out, log_cum, c_rows, state_in):
        inter_out = jnp.einsum(
            "tn,hpn->thp", c_rows.astype(jnp.float32), state_in, precision=lax.Precision.HIGHEST
        )
        total_out = partial_out + jnp.exp(log_cum)[:, :, None] * inter_out
        return total_out.reshape(half_rows, inner_width)

    first_out, first_cum, first_c, first_elem = local_block(
        lead_first, inner_rows[:half_rows], input_proj[:half_rows], step_size[:half_rows]
    )
    second_out, second_cum, second_c, second_elem = local_block(
        lead_second, inner_rows[half_rows:], input_proj[half_rows:], step_size[half_rows:]
    )
    first_in, second_in = block_states(
        first_elem[1], second_elem[1], first_cum[-1], second_cum[-1], seq_pos, seq_count
    )
    ssm_out = jnp.concatenate(
        [
            finish_block(first_out, first_cum, first_c, first_in),
            finish_block(second_out, second_cum, second_c, second_in),
        ],
        axis=0,
    )
    gated = ssm_out * jax.nn.silu(gate_rows.astype(jnp.float32))
    partial_sq = jnp.sum(gated * gated, axis=1)
    other_sq = partner(partial_sq, "head", 0)
    mean_sq = (partial_sq + other_sq) / (GROUP_HEADS * HEAD_SIZE)
    normed = gated * lax.rsqrt(mean_sq + 1e-05)[:, None] * norm_gain[None, :]
    return normed.astype(jnp.bfloat16)


def solution(mesh):
    in_specs = (
        P("seq", "head"),
        P("seq", "head"),
        P("seq", None),
        P("seq", "head"),
        P("head"),
        P("head"),
        P(None, "head"),
        P(),
        P("head"),
    )
    out_specs = P("seq", "head")
    return jax.shard_map(
        on_device, mesh=mesh, in_specs=in_specs, out_specs=out_specs, check_vma=False
    )
```

```python
import jax
import jax.numpy as jnp
from jax import lax
from jax.sharding import PartitionSpec as P

HEAD_SIZE = 64
STATE = 128
GROUP_HEADS = 32
KERNEL = 4


def exchange_rims(tails, heads, axis):
    count = lax.axis_size(axis)
    pos = lax.axis_index(axis)
    forward = [(i, (i + 1) % count) for i in range(count)]
    backward = [(target, source) for source, target in forward]
    tails, heads = lax.optimization_barrier((tails, heads))
    low = lax.ppermute(tails, axis, forward)
    high = lax.ppermute(heads, axis, backward)
    low = tuple(jnp.where(pos == 0, jnp.zeros_like(x), x) for x in low)
    return low, high


def partner(array, axis, stride):
    return lax.ppermute(array, axis, [(i, i ^ 1 << stride) for i in range(lax.axis_size(axis))])


LINK = jnp.bfloat16


def pack(maps, decays, kind):
    flat = [m.reshape(-1, m.shape[-1]) for m in maps]
    lanes = flat[0].shape[1]
    rows = jnp.stack(decays)
    high = rows.astype(kind)
    low = (rows - high.astype(jnp.float32)).astype(kind)
    tail = jnp.concatenate([high, low], axis=0)
    tail = jnp.pad(tail, ((0, 8 - tail.shape[0]), (0, lanes - tail.shape[1])))
    return jnp.concatenate([f.astype(kind) for f in flat] + [tail], axis=0)


def unpack(message, count, shape):
    rows = shape[0] * shape[1]
    maps = [
        message[i * rows : (i + 1) * rows].astype(jnp.float32).reshape(shape) for i in range(count)
    ]
    tail = message[count * rows :].astype(jnp.float32)
    decays = [tail[i, : shape[0]] + tail[count + i, : shape[0]] for i in range(count)]
    return maps, decays


def col(v):
    return v[:, None, None]


def to_link(x, rows):
    high = x.astype(LINK)
    low = (x - high.astype(jnp.float32)).astype(LINK)
    row = lax.broadcasted_iota(jnp.int32, x.shape, x.ndim - 2)
    return jnp.where(row == rows + 1, low, high)


def from_link(m, rows):
    x = m.astype(jnp.float32)
    return x, x[..., rows : rows + 1, :] + x[..., rows + 1 : rows + 2, :]


def butterfly_states(sub_f, sub_g, e_f, e_g, index, count, stride, seq_count):
    levels = count.bit_length() - 1
    assert 1 << levels == count
    heads, rows, lanes = sub_f.shape
    if levels == 0:
        return jnp.zeros_like(sub_f), sub_f
    shape = (heads, rows + 8, lanes)

    def with_decay(x, e):
        return jnp.concatenate([x, jnp.broadcast_to(e[:, None, None], (heads, 8, lanes))], axis=1)

    is_map = lax.broadcasted_iota(jnp.int32, shape, 1) < rows

    def decay(x):
        return x[:, rows : rows + 1, :]

    ones = jnp.ones((heads,), jnp.float32)
    zeros = jnp.zeros((heads,), jnp.float32)
    big_f, big_g = with_decay(sub_f, e_f), with_decay(sub_g, e_g)
    prefix = with_decay(jnp.zeros_like(sub_f), ones)
    above = with_decay(jnp.zeros_like(sub_f), ones)

    def last_message(f, g, lower):
        ef, eg = decay(f), decay(g)
        body = jnp.where(lower, f, eg * f + g)
        return jnp.where(is_map, body, jnp.where(lower, ef, ef * eg))

    first_lower = index % 2 == 0
    if levels == 1:
        msg = to_link(last_message(big_f, big_g, first_lower)[None], rows)
    else:
        msg = to_link(jnp.stack([big_f, big_g]), rows)
    for level in range(levels):
        size = 1 << level
        lower = (index // size) % 2 == 0
        pairs = [(i, i ^ (size * stride)) for i in range(seq_count)]
        got, got_e = from_link(lax.ppermute(msg, "seq", pairs), rows)
        e_f, e_g, e_pre, e_abv = decay(big_f), decay(big_g), decay(prefix), decay(above)
        if level < levels - 1:
            got_f, got_g = got[0], got[1]
            p_f, p_g = got_e[0], got_e[1]
            new_f = jnp.where(
                is_map,
                jnp.where(lower, p_f * big_f + got_f, big_f + e_f * got_f),
                e_f * p_f,
            )
            new_g = jnp.where(
                is_map,
                jnp.where(lower, big_g + e_g * got_g, p_g * big_g + got_g),
                e_g * p_g,
            )
            above = jnp.where(
                is_map,
                jnp.where(lower, above + e_abv * got_g, above),
                jnp.where(lower, e_abv * p_g, e_abv),
            )
            prefix = jnp.where(
                is_map,
                jnp.where(lower, prefix, prefix + e_pre * got_f),
                jnp.where(lower, e_pre, e_pre * p_f),
            )
            big_f, big_g = new_f, new_g
            next_lower = (index // (2 * size)) % 2 == 0
            if level + 1 == levels - 1:
                msg = to_link(last_message(big_f, big_g, next_lower)[None], rows)
            else:
                msg = to_link(jnp.stack([big_f, big_g]), rows)
        else:
            got_w, p_w = got[0], got_e[0]
            first_in = jnp.where(lower, prefix, prefix + e_pre * got_w)
            second_in = jnp.where(
                lower,
                above + e_abv * p_w * big_f + e_abv * got_w,
                above + e_abv * big_f + e_abv * e_f * got_w,
            )
    return first_in[:, :rows], second_in[:, :rows]


def block_states(first_loc, second_loc, first_log, second_log, seq_pos, seq_count):
    heads = first_loc.shape[0]
    e1, e2 = jnp.exp(first_log), jnp.exp(second_log)
    if seq_count % 2 or heads % 2:
        return butterfly_states(first_loc, second_loc, e1, e2, seq_pos, seq_count, 1, seq_count)
    half = heads // 2
    core = seq_pos % 2
    upper = core == 1
    pairs = [(i, i ^ 1) for i in range(seq_count)]

    def part(x, which):
        return lax.dynamic_slice_in_dim(x, which * half, half, 0)

    theirs = 1 - core
    sent = pack(
        (part(first_loc, theirs), part(second_loc, theirs)), (part(e1, theirs), part(e2, theirs)), jnp.float32
    )
    got = lax.ppermute(sent, "seq", pairs)
    (p1, p2), (q1, q2) = unpack(got, 2, (half, *first_loc.shape[1:]))
    l1, l2, e1h, e2h = part(first_loc, core), part(second_loc, core), part(e1, core), part(e2, core)
    ones = jnp.ones((half,), jnp.float32)
    pair_f = col(jnp.where(upper, ones, q1)) * l1 + col(jnp.where(upper, e1h, ones)) * p1
    pair_g = col(jnp.where(upper, q2, ones)) * l2 + col(jnp.where(upper, ones, e2h)) * p2
    low_f = jnp.where(upper, p1, l1)
    low_fe = jnp.where(upper, q1, e1h)
    high_g = jnp.where(upper, l2, p2)
    high_ge = jnp.where(upper, e2h, q2)

    prefix, wrapped = butterfly_states(
        pair_f, pair_g, e1h * q1, e2h * q2, seq_pos // 2, seq_count // 2, 2, seq_count
    )
    after_low = col(low_fe) * prefix + low_f
    before_high = col(high_ge) * wrapped + high_g
    own = (jnp.where(upper, after_low, prefix), jnp.where(upper, wrapped, before_high))
    other = jnp.stack([jnp.where(upper, prefix, after_low), jnp.where(upper, before_high, wrapped)])
    got_1, got_2 = lax.ppermute(other, "seq", pairs)

    def whole(own_half, got_half):
        return jnp.where(
            upper,
            jnp.concatenate([got_half, own_half], axis=0),
            jnp.concatenate([own_half, got_half], axis=0),
        )

    return whole(own[0], got_1), whole(own[1], got_2)


def on_device(
    inner_rows,
    gate_rows,
    input_proj,
    step_raw,
    decay_rate,
    skip_gain,
    conv_inner,
    conv_proj,
    norm_gain,
):
    tokens = inner_rows.shape[0]
    half_rows = tokens // 2
    head_count = step_raw.shape[1]
    inner_width = inner_rows.shape[1]
    group_count = input_proj.shape[1] // (2 * STATE)
    rim_rows = KERNEL - 1
    seq_count = lax.axis_size("seq")
    seq_pos = lax.axis_index("seq")
    is_last = seq_pos == seq_count - 1
    my_group = lax.axis_index("head") * head_count // GROUP_HEADS

    tails = (inner_rows[half_rows - rim_rows : half_rows], input_proj[half_rows - rim_rows : half_rows])
    heads = (inner_rows[tokens - rim_rows :], input_proj[tokens - rim_rows :])
    lead_first, high = exchange_rims(tails, heads, "seq")
    lead_second = tuple(jnp.where(is_last, t, h) for t, h in zip(tails, high))
    step_size = jax.nn.softplus(step_raw)
    causal = jnp.arange(half_rows)[:, None] >= jnp.arange(half_rows)[None, :]

    def conv(lead_rows, rows_in, taps):
        padded = jnp.concatenate([lead_rows, rows_in], axis=0).astype(jnp.float32)
        conv_sum = jnp.zeros((half_rows, rows_in.shape[1]), jnp.float32)
        for offset in range(KERNEL):
            conv_sum = conv_sum + taps[offset][None, :] * padded[offset : offset + half_rows]
        return jax.nn.silu(conv_sum).astype(jnp.bfloat16)

    def local_block(lead_rows, inner_in, proj_in, block_step):
        inner_out = conv(lead_rows[0], inner_in, conv_inner)
        proj_out = conv(lead_rows[1], proj_in, conv_proj)
        inner_conv = inner_out.reshape(half_rows, head_count, HEAD_SIZE)
        b_rows = lax.dynamic_slice_in_dim(proj_out, my_group * STATE, STATE, 1)
        c_rows = lax.dynamic_slice_in_dim(proj_out, (group_count + my_group) * STATE, STATE, 1)
        log_cum = jnp.cumsum(-block_step * decay_rate[None, :], axis=0)
        score_grid = jnp.dot(c_rows, b_rows.T, preferred_element_type=jnp.float32)
        log_gap = log_cum.T[:, :, None] - log_cum.T[:, None, :]
        decay_grid = jnp.where(causal[None], jnp.exp(jnp.where(causal[None], log_gap, 0.0)), 0.0)
        weights = (score_grid[None] * decay_grid * block_step.T[:, None, :]).astype(jnp.bfloat16)
        intra_out = jnp.einsum(
            "hts,shp->thp", weights, inner_conv, preferred_element_type=jnp.float32
        )
        tail_decay = jnp.exp(log_cum[-1][None, :] - log_cum) * block_step
        x_weighted = (inner_conv.astype(jnp.float32) * tail_decay[:, :, None]).astype(jnp.bfloat16)
        local_state = jnp.einsum(
            "shp,sn->hpn", x_weighted, b_rows, preferred_element_type=jnp.float32
        )
        partial_out = intra_out + skip_gain[None, :, None] * inner_conv.astype(jnp.float32)
        return (partial_out, log_cum, c_rows, (jnp.exp(log_cum[-1]), local_state))

    def finish_block(partial_out, log_cum, c_rows, state_in):
        inter_out = jnp.einsum(
            "tn,hpn->thp", c_rows.astype(jnp.float32), state_in, precision=lax.Precision.HIGHEST
        )
        total_out = partial_out + jnp.exp(log_cum)[:, :, None] * inter_out
        return total_out.reshape(half_rows, inner_width)

    first_out, first_cum, first_c, first_elem = local_block(
        lead_first, inner_rows[:half_rows], input_proj[:half_rows], step_size[:half_rows]
    )
    second_out, second_cum, second_c, second_elem = local_block(
        lead_second, inner_rows[half_rows:], input_proj[half_rows:], step_size[half_rows:]
    )
    first_in, second_in = block_states(
        first_elem[1], second_elem[1], first_cum[-1], second_cum[-1], seq_pos, seq_count
    )
    ssm_out = jnp.concatenate(
        [
            finish_block(first_out, first_cum, first_c, first_in),
            finish_block(second_out, second_cum, second_c, second_in),
        ],
        axis=0,
    )
    gated = ssm_out * jax.nn.silu(gate_rows.astype(jnp.float32))
    partial_sq = jnp.sum(gated * gated, axis=1)
    other_sq = partner(partial_sq, "head", 0)
    mean_sq = (partial_sq + other_sq) / (GROUP_HEADS * HEAD_SIZE)
    normed = gated * lax.rsqrt(mean_sq + 1e-05)[:, None] * norm_gain[None, :]
    return normed.astype(jnp.bfloat16)


def solution(mesh):
    in_specs = (
        P("seq", "head"),
        P("seq", "head"),
        P("seq", None),
        P("seq", "head"),
        P("head"),
        P("head"),
        P(None, "head"),
        P(),
        P("head"),
    )
    out_specs = P("seq", "head")
    return jax.shard_map(
        on_device, mesh=mesh, in_specs=in_specs, out_specs=out_specs, check_vma=False
    )
```

```python
import jax
import jax.numpy as jnp
from jax import lax
from jax.sharding import PartitionSpec as P

HEAD_SIZE = 64
STATE = 128
GROUP_HEADS = 32
KERNEL = 4


def exchange_rims(tails, heads, axis):
    count = lax.axis_size(axis)
    pos = lax.axis_index(axis)
    forward = [(i, (i + 1) % count) for i in range(count)]
    backward = [(target, source) for source, target in forward]
    tails, heads = lax.optimization_barrier((tails, heads))
    low = lax.ppermute(tails, axis, forward)
    high = lax.ppermute(heads, axis, backward)
    low = tuple(jnp.where(pos == 0, jnp.zeros_like(x), x) for x in low)
    return low, high


def partner(array, axis, stride):
    return lax.ppermute(array, axis, [(i, i ^ 1 << stride) for i in range(lax.axis_size(axis))])


LINK = jnp.bfloat16


def pack(maps, decays, kind):
    flat = [m.reshape(-1, m.shape[-1]) for m in maps]
    lanes = flat[0].shape[1]
    rows = jnp.stack(decays)
    high = rows.astype(kind)
    low = (rows - high.astype(jnp.float32)).astype(kind)
    tail = jnp.concatenate([high, low], axis=0)
    tail = jnp.pad(tail, ((0, 8 - tail.shape[0]), (0, lanes - tail.shape[1])))
    return jnp.concatenate([f.astype(kind) for f in flat] + [tail], axis=0)


def unpack(message, count, shape):
    rows = shape[0] * shape[1]
    maps = [
        message[i * rows : (i + 1) * rows].astype(jnp.float32).reshape(shape) for i in range(count)
    ]
    tail = message[count * rows :].astype(jnp.float32)
    decays = [tail[i, : shape[0]] + tail[count + i, : shape[0]] for i in range(count)]
    return maps, decays


def col(v):
    return v[:, None, None]


def to_link(x, rows):
    high = x.astype(LINK)
    low = (x - high.astype(jnp.float32)).astype(LINK)
    row = lax.broadcasted_iota(jnp.int32, x.shape, x.ndim - 2)
    return jnp.where(row == rows + 1, low, high)


def from_link(m, rows):
    x = m.astype(jnp.float32)
    return x, x[..., rows : rows + 1, :] + x[..., rows + 1 : rows + 2, :]


def butterfly_states(sub_f, sub_g, e_f, e_g, index, count, stride, seq_count):
    levels = count.bit_length() - 1
    assert 1 << levels == count
    heads, rows, lanes = sub_f.shape
    if levels == 0:
        return jnp.zeros_like(sub_f), sub_f
    shape = (heads, rows + 8, lanes)

    def with_decay(x, e):
        return jnp.concatenate([x, jnp.broadcast_to(e[:, None, None], (heads, 8, lanes))], axis=1)

    is_map = lax.broadcasted_iota(jnp.int32, shape, 1) < rows

    def decay(x):
        return x[:, rows : rows + 1, :]

    ones = jnp.ones((heads,), jnp.float32)
    zeros = jnp.zeros((heads,), jnp.float32)
    big_f, big_g = with_decay(sub_f, e_f), with_decay(sub_g, e_g)
    prefix = with_decay(jnp.zeros_like(sub_f), ones)
    above = with_decay(jnp.zeros_like(sub_f), ones)

    def last_message(f, g, lower):
        ef, eg = decay(f), decay(g)
        body = jnp.where(lower, f, eg * f + g)
        return jnp.where(is_map, body, jnp.where(lower, ef, ef * eg))

    first_lower = index % 2 == 0
    if levels == 1:
        msg = to_link(last_message(big_f, big_g, first_lower)[None], rows)
    else:
        msg = to_link(jnp.stack([big_f, big_g]), rows)
    for level in range(levels):
        size = 1 << level
        lower = (index // size) % 2 == 0
        pairs = [(i, i ^ (size * stride)) for i in range(seq_count)]
        got, got_e = from_link(lax.ppermute(msg, "seq", pairs), rows)
        e_f, e_g, e_pre, e_abv = decay(big_f), decay(big_g), decay(prefix), decay(above)
        if level < levels - 1:
            got_f, got_g = got[0], got[1]
            p_f, p_g = got_e[0], got_e[1]
            new_f = jnp.where(
                is_map,
                jnp.where(lower, p_f * big_f + got_f, big_f + e_f * got_f),
                e_f * p_f,
            )
            new_g = jnp.where(
                is_map,
                jnp.where(lower, big_g + e_g * got_g, p_g * big_g + got_g),
                e_g * p_g,
            )
            above = jnp.where(
                is_map,
                jnp.where(lower, above + e_abv * got_g, above),
                jnp.where(lower, e_abv * p_g, e_abv),
            )
            prefix = jnp.where(
                is_map,
                jnp.where(lower, prefix, prefix + e_pre * got_f),
                jnp.where(lower, e_pre, e_pre * p_f),
            )
            big_f, big_g = new_f, new_g
            next_lower = (index // (2 * size)) % 2 == 0
            if level + 1 == levels - 1:
                msg = to_link(last_message(big_f, big_g, next_lower)[None], rows)
            else:
                msg = to_link(jnp.stack([big_f, big_g]), rows)
        else:
            got_w, p_w = got[0], got_e[0]
            first_in = jnp.where(lower, prefix, prefix + e_pre * got_w)
            second_in = jnp.where(
                lower,
                above + e_abv * p_w * big_f + e_abv * got_w,
                above + e_abv * big_f + e_abv * e_f * got_w,
            )
    return first_in[:, :rows], second_in[:, :rows]


def block_states(first_loc, second_loc, first_log, second_log, seq_pos, seq_count):
    heads = first_loc.shape[0]
    e1, e2 = jnp.exp(first_log), jnp.exp(second_log)
    if seq_count % 2 or heads % 2:
        return butterfly_states(first_loc, second_loc, e1, e2, seq_pos, seq_count, 1, seq_count)
    half = heads // 2
    core = seq_pos % 2
    upper = core == 1
    pairs = [(i, i ^ 1) for i in range(seq_count)]

    def part(x, which):
        return lax.dynamic_slice_in_dim(x, which * half, half, 0)

    theirs = 1 - core
    sent = pack(
        (part(first_loc, theirs), part(second_loc, theirs)), (part(e1, theirs), part(e2, theirs)), jnp.float32
    )
    got = lax.ppermute(sent, "seq", pairs)
    (p1, p2), (q1, q2) = unpack(got, 2, (half, *first_loc.shape[1:]))
    l1, l2, e1h, e2h = part(first_loc, core), part(second_loc, core), part(e1, core), part(e2, core)
    ones = jnp.ones((half,), jnp.float32)
    pair_f = col(jnp.where(upper, ones, q1)) * l1 + col(jnp.where(upper, e1h, ones)) * p1
    pair_g = col(jnp.where(upper, q2, ones)) * l2 + col(jnp.where(upper, ones, e2h)) * p2
    low_f = jnp.where(upper, p1, l1)
    low_fe = jnp.where(upper, q1, e1h)
    high_g = jnp.where(upper, l2, p2)
    high_ge = jnp.where(upper, e2h, q2)

    prefix, wrapped = butterfly_states(
        pair_f, pair_g, e1h * q1, e2h * q2, seq_pos // 2, seq_count // 2, 2, seq_count
    )
    after_low = col(low_fe) * prefix + low_f
    before_high = col(high_ge) * wrapped + high_g
    own = (jnp.where(upper, after_low, prefix), jnp.where(upper, wrapped, before_high))
    other = jnp.stack([jnp.where(upper, prefix, after_low), jnp.where(upper, before_high, wrapped)])
    got_1, got_2 = lax.ppermute(other, "seq", pairs)

    def whole(own_half, got_half):
        return jnp.where(
            upper,
            jnp.concatenate([got_half, own_half], axis=0),
            jnp.concatenate([own_half, got_half], axis=0),
        )

    return whole(own[0], got_1), whole(own[1], got_2)


def on_device(
    inner_rows,
    gate_rows,
    input_proj,
    step_raw,
    decay_rate,
    skip_gain,
    conv_inner,
    conv_proj,
    norm_gain,
):
    tokens = inner_rows.shape[0]
    half_rows = tokens // 2
    head_count = step_raw.shape[1]
    inner_width = inner_rows.shape[1]
    group_count = input_proj.shape[1] // (2 * STATE)
    rim_rows = KERNEL - 1
    seq_count = lax.axis_size("seq")
    seq_pos = lax.axis_index("seq")
    is_last = seq_pos == seq_count - 1
    my_group = lax.axis_index("head") * head_count // GROUP_HEADS

    tails = (inner_rows[half_rows - rim_rows : half_rows], input_proj[half_rows - rim_rows : half_rows])
    heads = (inner_rows[tokens - rim_rows :], input_proj[tokens - rim_rows :])
    lead_first, high = exchange_rims(tails, heads, "seq")
    lead_second = tuple(jnp.where(is_last, t, h) for t, h in zip(tails, high))
    step_size = jax.nn.softplus(step_raw)
    causal = jnp.arange(half_rows)[:, None] >= jnp.arange(half_rows)[None, :]

    def conv(leads, rows_in, taps):
        width = rows_in.shape[1]
        blocks = rows_in.reshape(2, half_rows, width)
        padded = jnp.concatenate([jnp.stack(leads), blocks], axis=1).astype(jnp.float32)
        conv_sum = jnp.zeros((2, half_rows, width), jnp.float32)
        for offset in range(KERNEL):
            conv_sum = conv_sum + taps[offset][None, None, :] * padded[:, offset : offset + half_rows]
        return jax.nn.silu(conv_sum).astype(jnp.bfloat16)

    inner_all = conv((lead_first[0], lead_second[0]), inner_rows, conv_inner)
    proj_all = conv((lead_first[1], lead_second[1]), input_proj, conv_proj)

    def local_block(inner_out, proj_out, block_step):
        inner_conv = inner_out.reshape(half_rows, head_count, HEAD_SIZE)
        b_rows = lax.dynamic_slice_in_dim(proj_out, my_group * STATE, STATE, 1)
        c_rows = lax.dynamic_slice_in_dim(proj_out, (group_count + my_group) * STATE, STATE, 1)
        log_cum = jnp.cumsum(-block_step * decay_rate[None, :], axis=0)
        score_grid = jnp.dot(c_rows, b_rows.T, preferred_element_type=jnp.float32)
        log_gap = log_cum.T[:, :, None] - log_cum.T[:, None, :]
        decay_grid = jnp.where(causal[None], jnp.exp(jnp.where(causal[None], log_gap, 0.0)), 0.0)
        weights = (score_grid[None] * decay_grid * block_step.T[:, None, :]).astype(jnp.bfloat16)
        intra_out = jnp.einsum(
            "hts,shp->thp", weights, inner_conv, preferred_element_type=jnp.float32
        )
        tail_decay = jnp.exp(log_cum[-1][None, :] - log_cum) * block_step
        x_weighted = (inner_conv.astype(jnp.float32) * tail_decay[:, :, None]).astype(jnp.bfloat16)
        local_state = jnp.einsum(
            "shp,sn->hpn", x_weighted, b_rows, preferred_element_type=jnp.float32
        )
        partial_out = intra_out + skip_gain[None, :, None] * inner_conv.astype(jnp.float32)
        return (partial_out, log_cum, c_rows, (jnp.exp(log_cum[-1]), local_state))

    def finish_block(partial_out, log_cum, c_rows, state_in):
        inter_out = jnp.einsum(
            "tn,hpn->thp", c_rows.astype(jnp.float32), state_in, precision=lax.Precision.HIGHEST
        )
        total_out = partial_out + jnp.exp(log_cum)[:, :, None] * inter_out
        return total_out.reshape(half_rows, inner_width)

    first_out, first_cum, first_c, first_elem = local_block(
        inner_all[0], proj_all[0], step_size[:half_rows]
    )
    second_out, second_cum, second_c, second_elem = local_block(
        inner_all[1], proj_all[1], step_size[half_rows:]
    )
    first_in, second_in = block_states(
        first_elem[1], second_elem[1], first_cum[-1], second_cum[-1], seq_pos, seq_count
    )
    ssm_out = jnp.concatenate(
        [
            finish_block(first_out, first_cum, first_c, first_in),
            finish_block(second_out, second_cum, second_c, second_in),
        ],
        axis=0,
    )
    gated = ssm_out * jax.nn.silu(gate_rows.astype(jnp.float32))
    partial_sq = jnp.sum(gated * gated, axis=1)
    other_sq = partner(partial_sq, "head", 0)
    mean_sq = (partial_sq + other_sq) / (GROUP_HEADS * HEAD_SIZE)
    normed = gated * lax.rsqrt(mean_sq + 1e-05)[:, None] * norm_gain[None, :]
    return normed.astype(jnp.bfloat16)


def solution(mesh):
    in_specs = (
        P("seq", "head"),
        P("seq", "head"),
        P("seq", None),
        P("seq", "head"),
        P("head"),
        P("head"),
        P(None, "head"),
        P(),
        P("head"),
    )
    out_specs = P("seq", "head")
    return jax.shard_map(
        on_device, mesh=mesh, in_specs=in_specs, out_specs=out_specs, check_vma=False
    )
```

```python
import jax
import jax.numpy as jnp
from jax import lax
from jax.sharding import PartitionSpec as P

HEAD_SIZE = 64
STATE = 128
GROUP_HEADS = 32
KERNEL = 4


def exchange_rims(tails, heads, axis):
    count = lax.axis_size(axis)
    pos = lax.axis_index(axis)
    forward = [(i, (i + 1) % count) for i in range(count)]
    backward = [(target, source) for source, target in forward]
    tails, heads = lax.optimization_barrier((tails, heads))
    low = lax.ppermute(tails, axis, forward)
    high = lax.ppermute(heads, axis, backward)
    low = tuple(jnp.where(pos == 0, jnp.zeros_like(x), x) for x in low)
    return low, high


def partner(array, axis, stride):
    return lax.ppermute(array, axis, [(i, i ^ 1 << stride) for i in range(lax.axis_size(axis))])


LINK = jnp.bfloat16


def pack(maps, decays, kind):
    flat = [m.reshape(-1, m.shape[-1]) for m in maps]
    lanes = flat[0].shape[1]
    rows = jnp.stack(decays)
    high = rows.astype(kind)
    low = (rows - high.astype(jnp.float32)).astype(kind)
    tail = jnp.concatenate([high, low], axis=0)
    tail = jnp.pad(tail, ((0, 8 - tail.shape[0]), (0, lanes - tail.shape[1])))
    return jnp.concatenate([f.astype(kind) for f in flat] + [tail], axis=0)


def unpack(message, count, shape):
    rows = shape[0] * shape[1]
    maps = [
        message[i * rows : (i + 1) * rows].astype(jnp.float32).reshape(shape) for i in range(count)
    ]
    tail = message[count * rows :].astype(jnp.float32)
    decays = [tail[i, : shape[0]] + tail[count + i, : shape[0]] for i in range(count)]
    return maps, decays


def col(v):
    return v[:, None, None]


def to_link(x, rows):
    lanes = x.shape[-1]
    high = x.astype(LINK)
    low = (x - high.astype(jnp.float32)).astype(LINK)
    decays = jnp.concatenate([high[..., rows : rows + 1, :], low[..., rows : rows + 1, :]], axis=-2)
    return jnp.concatenate([high[..., :rows, :].reshape(-1, lanes), decays.reshape(-1, lanes)], axis=0)


def from_link(m, count, heads, rows):
    lanes = m.shape[-1]
    size = count * heads * rows
    maps = m[:size].astype(jnp.float32).reshape(count, heads, rows, lanes)
    decays = m[size:].astype(jnp.float32).reshape(count, heads, 2, lanes)
    e = decays[..., 0:1, :] + decays[..., 1:2, :]
    full = jnp.concatenate([maps, jnp.broadcast_to(e, (count, heads, 8, lanes))], axis=-2)
    return full, e


def butterfly_states(sub_f, sub_g, e_f, e_g, index, count, stride, seq_count):
    levels = count.bit_length() - 1
    assert 1 << levels == count
    heads, rows, lanes = sub_f.shape
    if levels == 0:
        return jnp.zeros_like(sub_f), sub_f
    shape = (heads, rows + 8, lanes)

    def with_decay(x, e):
        return jnp.concatenate([x, jnp.broadcast_to(e[:, None, None], (heads, 8, lanes))], axis=1)

    is_map = lax.broadcasted_iota(jnp.int32, shape, 1) < rows

    def decay(x):
        return x[:, rows : rows + 1, :]

    ones = jnp.ones((heads,), jnp.float32)
    zeros = jnp.zeros((heads,), jnp.float32)
    big_f, big_g = with_decay(sub_f, e_f), with_decay(sub_g, e_g)
    prefix = with_decay(jnp.zeros_like(sub_f), ones)
    above = with_decay(jnp.zeros_like(sub_f), ones)

    def last_message(f, g, lower):
        ef, eg = decay(f), decay(g)
        body = jnp.where(lower, f, eg * f + g)
        return jnp.where(is_map, body, jnp.where(lower, ef, ef * eg))

    first_lower = index % 2 == 0
    if levels == 1:
        msg = to_link(last_message(big_f, big_g, first_lower)[None], rows)
    else:
        msg = to_link(jnp.stack([big_f, big_g]), rows)
    for level in range(levels):
        size = 1 << level
        lower = (index // size) % 2 == 0
        pairs = [(i, i ^ (size * stride)) for i in range(seq_count)]
        got, got_e = from_link(
            lax.ppermute(msg, "seq", pairs), 1 if level == levels - 1 else 2, heads, rows
        )
        e_f, e_g, e_pre, e_abv = decay(big_f), decay(big_g), decay(prefix), decay(above)
        if level < levels - 1:
            got_f, got_g = got[0], got[1]
            p_f, p_g = got_e[0], got_e[1]
            new_f = jnp.where(
                is_map,
                jnp.where(lower, p_f * big_f + got_f, big_f + e_f * got_f),
                e_f * p_f,
            )
            new_g = jnp.where(
                is_map,
                jnp.where(lower, big_g + e_g * got_g, p_g * big_g + got_g),
                e_g * p_g,
            )
            above = jnp.where(
                is_map,
                jnp.where(lower, above + e_abv * got_g, above),
                jnp.where(lower, e_abv * p_g, e_abv),
            )
            prefix = jnp.where(
                is_map,
                jnp.where(lower, prefix, prefix + e_pre * got_f),
                jnp.where(lower, e_pre, e_pre * p_f),
            )
            big_f, big_g = new_f, new_g
            next_lower = (index // (2 * size)) % 2 == 0
            if level + 1 == levels - 1:
                msg = to_link(last_message(big_f, big_g, next_lower)[None], rows)
            else:
                msg = to_link(jnp.stack([big_f, big_g]), rows)
        else:
            got_w, p_w = got[0], got_e[0]
            first_in = jnp.where(lower, prefix, prefix + e_pre * got_w)
            second_in = jnp.where(
                lower,
                above + e_abv * p_w * big_f + e_abv * got_w,
                above + e_abv * big_f + e_abv * e_f * got_w,
            )
    return first_in[:, :rows], second_in[:, :rows]


def block_states(first_loc, second_loc, first_log, second_log, seq_pos, seq_count):
    heads = first_loc.shape[0]
    e1, e2 = jnp.exp(first_log), jnp.exp(second_log)
    if seq_count % 2 or heads % 2:
        return butterfly_states(first_loc, second_loc, e1, e2, seq_pos, seq_count, 1, seq_count)
    half = heads // 2
    core = seq_pos % 2
    upper = core == 1
    pairs = [(i, i ^ 1) for i in range(seq_count)]

    def part(x, which):
        return lax.dynamic_slice_in_dim(x, which * half, half, 0)

    theirs = 1 - core
    sent = pack(
        (part(first_loc, theirs), part(second_loc, theirs)), (part(e1, theirs), part(e2, theirs)), jnp.float32
    )
    got = lax.ppermute(sent, "seq", pairs)
    (p1, p2), (q1, q2) = unpack(got, 2, (half, *first_loc.shape[1:]))
    l1, l2, e1h, e2h = part(first_loc, core), part(second_loc, core), part(e1, core), part(e2, core)
    ones = jnp.ones((half,), jnp.float32)
    pair_f = col(jnp.where(upper, ones, q1)) * l1 + col(jnp.where(upper, e1h, ones)) * p1
    pair_g = col(jnp.where(upper, q2, ones)) * l2 + col(jnp.where(upper, ones, e2h)) * p2
    low_f = jnp.where(upper, p1, l1)
    low_fe = jnp.where(upper, q1, e1h)
    high_g = jnp.where(upper, l2, p2)
    high_ge = jnp.where(upper, e2h, q2)

    prefix, wrapped = butterfly_states(
        pair_f, pair_g, e1h * q1, e2h * q2, seq_pos // 2, seq_count // 2, 2, seq_count
    )
    after_low = col(low_fe) * prefix + low_f
    before_high = col(high_ge) * wrapped + high_g
    own = (jnp.where(upper, after_low, prefix), jnp.where(upper, wrapped, before_high))
    other = jnp.stack([jnp.where(upper, prefix, after_low), jnp.where(upper, before_high, wrapped)])
    got_1, got_2 = lax.ppermute(other, "seq", pairs)

    def whole(own_half, got_half):
        return jnp.where(
            upper,
            jnp.concatenate([got_half, own_half], axis=0),
            jnp.concatenate([own_half, got_half], axis=0),
        )

    return whole(own[0], got_1), whole(own[1], got_2)


def on_device(
    inner_rows,
    gate_rows,
    input_proj,
    step_raw,
    decay_rate,
    skip_gain,
    conv_inner,
    conv_proj,
    norm_gain,
):
    tokens = inner_rows.shape[0]
    half_rows = tokens // 2
    head_count = step_raw.shape[1]
    inner_width = inner_rows.shape[1]
    group_count = input_proj.shape[1] // (2 * STATE)
    rim_rows = KERNEL - 1
    seq_count = lax.axis_size("seq")
    seq_pos = lax.axis_index("seq")
    is_last = seq_pos == seq_count - 1
    my_group = lax.axis_index("head") * head_count // GROUP_HEADS

    tails = (inner_rows[half_rows - rim_rows : half_rows], input_proj[half_rows - rim_rows : half_rows])
    heads = (inner_rows[tokens - rim_rows :], input_proj[tokens - rim_rows :])
    lead_first, high = exchange_rims(tails, heads, "seq")
    lead_second = tuple(jnp.where(is_last, t, h) for t, h in zip(tails, high))
    step_size = jax.nn.softplus(step_raw)
    causal = jnp.arange(half_rows)[:, None] >= jnp.arange(half_rows)[None, :]

    def conv(lead_rows, rows_in, taps):
        padded = jnp.concatenate([lead_rows, rows_in], axis=0).astype(jnp.float32)
        conv_sum = jnp.zeros((half_rows, rows_in.shape[1]), jnp.float32)
        for offset in range(KERNEL):
            conv_sum = conv_sum + taps[offset][None, :] * padded[offset : offset + half_rows]
        return jax.nn.silu(conv_sum).astype(jnp.bfloat16)

    def local_block(lead_rows, inner_in, proj_in, block_step):
        inner_out = conv(lead_rows[0], inner_in, conv_inner)
        proj_out = conv(lead_rows[1], proj_in, conv_proj)
        inner_conv = inner_out.reshape(half_rows, head_count, HEAD_SIZE)
        b_rows = lax.dynamic_slice_in_dim(proj_out, my_group * STATE, STATE, 1)
        c_rows = lax.dynamic_slice_in_dim(proj_out, (group_count + my_group) * STATE, STATE, 1)
        log_cum = jnp.cumsum(-block_step * decay_rate[None, :], axis=0)
        score_grid = jnp.dot(c_rows, b_rows.T, preferred_element_type=jnp.float32)
        log_gap = log_cum.T[:, :, None] - log_cum.T[:, None, :]
        decay_grid = jnp.where(causal[None], jnp.exp(jnp.where(causal[None], log_gap, 0.0)), 0.0)
        weights = (score_grid[None] * decay_grid * block_step.T[:, None, :]).astype(jnp.bfloat16)
        intra_out = jnp.einsum(
            "hts,shp->thp", weights, inner_conv, preferred_element_type=jnp.float32
        )
        tail_decay = jnp.exp(log_cum[-1][None, :] - log_cum) * block_step
        x_weighted = (inner_conv.astype(jnp.float32) * tail_decay[:, :, None]).astype(jnp.bfloat16)
        local_state = jnp.einsum(
            "shp,sn->hpn", x_weighted, b_rows, preferred_element_type=jnp.float32
        )
        partial_out = intra_out + skip_gain[None, :, None] * inner_conv.astype(jnp.float32)
        return (partial_out, log_cum, c_rows, (jnp.exp(log_cum[-1]), local_state))

    def finish_block(partial_out, log_cum, c_rows, state_in):
        inter_out = jnp.einsum(
            "tn,hpn->thp", c_rows.astype(jnp.float32), state_in, precision=lax.Precision.HIGHEST
        )
        total_out = partial_out + jnp.exp(log_cum)[:, :, None] * inter_out
        return total_out.reshape(half_rows, inner_width)

    first_out, first_cum, first_c, first_elem = local_block(
        lead_first, inner_rows[:half_rows], input_proj[:half_rows], step_size[:half_rows]
    )
    second_out, second_cum, second_c, second_elem = local_block(
        lead_second, inner_rows[half_rows:], input_proj[half_rows:], step_size[half_rows:]
    )
    first_in, second_in = block_states(
        first_elem[1], second_elem[1], first_cum[-1], second_cum[-1], seq_pos, seq_count
    )
    ssm_out = jnp.concatenate(
        [
            finish_block(first_out, first_cum, first_c, first_in),
            finish_block(second_out, second_cum, second_c, second_in),
        ],
        axis=0,
    )
    gated = ssm_out * jax.nn.silu(gate_rows.astype(jnp.float32))
    partial_sq = jnp.sum(gated * gated, axis=1)
    other_sq = partner(partial_sq, "head", 0)
    mean_sq = (partial_sq + other_sq) / (GROUP_HEADS * HEAD_SIZE)
    normed = gated * lax.rsqrt(mean_sq + 1e-05)[:, None] * norm_gain[None, :]
    return normed.astype(jnp.bfloat16)


def solution(mesh):
    in_specs = (
        P("seq", "head"),
        P("seq", "head"),
        P("seq", None),
        P("seq", "head"),
        P("head"),
        P("head"),
        P(None, "head"),
        P(),
        P("head"),
    )
    out_specs = P("seq", "head")
    return jax.shard_map(
        on_device, mesh=mesh, in_specs=in_specs, out_specs=out_specs, check_vma=False
    )
```

```python
import jax
import jax.numpy as jnp
from jax import lax
from jax.sharding import PartitionSpec as P

HEAD_SIZE = 64
STATE = 128
GROUP_HEADS = 32
KERNEL = 4


def exchange_rims(tails, heads, axis):
    count = lax.axis_size(axis)
    pos = lax.axis_index(axis)
    forward = [(i, (i + 1) % count) for i in range(count)]
    backward = [(target, source) for source, target in forward]
    tails, heads = lax.optimization_barrier((tails, heads))
    low = lax.ppermute(tails, axis, forward)
    high = lax.ppermute(heads, axis, backward)
    low = tuple(jnp.where(pos == 0, jnp.zeros_like(x), x) for x in low)
    return low, high


def partner(array, axis, stride):
    return lax.ppermute(array, axis, [(i, i ^ 1 << stride) for i in range(lax.axis_size(axis))])


LINK = jnp.bfloat16


def pack(maps, decays, kind):
    flat = [m.reshape(-1, m.shape[-1]) for m in maps]
    lanes = flat[0].shape[1]
    rows = jnp.stack(decays)
    high = rows.astype(kind)
    low = (rows - high.astype(jnp.float32)).astype(kind)
    tail = jnp.concatenate([high, low], axis=0)
    tail = jnp.pad(tail, ((0, 8 - tail.shape[0]), (0, lanes - tail.shape[1])))
    return jnp.concatenate([f.astype(kind) for f in flat] + [tail], axis=0)


def unpack(message, count, shape):
    rows = shape[0] * shape[1]
    maps = [
        message[i * rows : (i + 1) * rows].astype(jnp.float32).reshape(shape) for i in range(count)
    ]
    tail = message[count * rows :].astype(jnp.float32)
    decays = [tail[i, : shape[0]] + tail[count + i, : shape[0]] for i in range(count)]
    return maps, decays


def col(v):
    return v[:, None, None]


def to_link(x, rows):
    high = x.astype(LINK)
    low = (x - high.astype(jnp.float32)).astype(LINK)
    row = lax.broadcasted_iota(jnp.int32, x.shape, x.ndim - 2)
    return jnp.where(row == rows + 1, low, high)


def from_link(m, rows):
    x = m.astype(jnp.float32)
    return x, x[..., rows : rows + 1, :] + x[..., rows + 1 : rows + 2, :]


def butterfly_states(sub_f, sub_g, e_f, e_g, index, count, stride, seq_count):
    levels = count.bit_length() - 1
    assert 1 << levels == count
    heads, rows, lanes = sub_f.shape
    if levels == 0:
        return jnp.zeros_like(sub_f), sub_f
    shape = (heads, rows + 8, lanes)

    def with_decay(x, e):
        return jnp.concatenate([x, jnp.broadcast_to(e[:, None, None], (heads, 8, lanes))], axis=1)

    is_map = lax.broadcasted_iota(jnp.int32, shape, 1) < rows

    def decay(x):
        return x[:, rows : rows + 1, :]

    ones = jnp.ones((heads,), jnp.float32)
    zeros = jnp.zeros((heads,), jnp.float32)
    big_f, big_g = with_decay(sub_f, e_f), with_decay(sub_g, e_g)
    prefix = with_decay(jnp.zeros_like(sub_f), ones)
    above = with_decay(jnp.zeros_like(sub_f), ones)

    def last_message(f, g, lower):
        ef, eg = decay(f), decay(g)
        body = jnp.where(lower, f, eg * f + g)
        return jnp.where(is_map, body, jnp.where(lower, ef, ef * eg))

    first_lower = index % 2 == 0
    if levels == 1:
        msg = to_link(last_message(big_f, big_g, first_lower)[None], rows)
    else:
        msg = to_link(jnp.stack([big_f, big_g]), rows)
    for level in range(levels):
        size = 1 << level
        lower = (index // size) % 2 == 0
        pairs = [(i, i ^ (size * stride)) for i in range(seq_count)]
        got, got_e = from_link(lax.ppermute(msg, "seq", pairs), rows)
        e_f, e_g, e_pre, e_abv = decay(big_f), decay(big_g), decay(prefix), decay(above)
        if level < levels - 1:
            got_f, got_g = got[0], got[1]
            p_f, p_g = got_e[0], got_e[1]
            new_f = jnp.where(
                is_map,
                jnp.where(lower, p_f * big_f + got_f, big_f + e_f * got_f),
                e_f * p_f,
            )
            new_g = jnp.where(
                is_map,
                jnp.where(lower, big_g + e_g * got_g, p_g * big_g + got_g),
                e_g * p_g,
            )
            above = jnp.where(
                is_map,
                jnp.where(lower, above + e_abv * got_g, above),
                jnp.where(lower, e_abv * p_g, e_abv),
            )
            prefix = jnp.where(
                is_map,
                jnp.where(lower, prefix, prefix + e_pre * got_f),
                jnp.where(lower, e_pre, e_pre * p_f),
            )
            big_f, big_g = new_f, new_g
            next_lower = (index // (2 * size)) % 2 == 0
            if level + 1 == levels - 1:
                msg = to_link(last_message(big_f, big_g, next_lower)[None], rows)
            else:
                msg = to_link(jnp.stack([big_f, big_g]), rows)
        else:
            got_w, p_w = got[0], got_e[0]
            first_in = jnp.where(lower, prefix, prefix + e_pre * got_w)
            second_in = jnp.where(
                lower,
                above + e_abv * p_w * big_f + e_abv * got_w,
                above + e_abv * big_f + e_abv * e_f * got_w,
            )
    return first_in[:, :rows], second_in[:, :rows]


def block_states(first_loc, second_loc, first_log, second_log, seq_pos, seq_count):
    heads = first_loc.shape[0]
    e1, e2 = jnp.exp(first_log), jnp.exp(second_log)
    if seq_count % 2 or heads % 2:
        return butterfly_states(first_loc, second_loc, e1, e2, seq_pos, seq_count, 1, seq_count)
    half = heads // 2
    core = seq_pos % 2
    upper = core == 1
    pairs = [(i, i ^ 1) for i in range(seq_count)]

    def part(x, which):
        return lax.dynamic_slice_in_dim(x, which * half, half, 0)

    theirs = 1 - core
    sent = pack(
        (part(first_loc, theirs), part(second_loc, theirs)), (part(e1, theirs), part(e2, theirs)), LINK
    )
    got = lax.ppermute(sent, "seq", pairs)
    (p1, p2), (q1, q2) = unpack(got, 2, (half, *first_loc.shape[1:]))
    l1, l2, e1h, e2h = part(first_loc, core), part(second_loc, core), part(e1, core), part(e2, core)
    ones = jnp.ones((half,), jnp.float32)
    pair_f = col(jnp.where(upper, ones, q1)) * l1 + col(jnp.where(upper, e1h, ones)) * p1
    pair_g = col(jnp.where(upper, q2, ones)) * l2 + col(jnp.where(upper, ones, e2h)) * p2
    low_f = jnp.where(upper, p1, l1)
    low_fe = jnp.where(upper, q1, e1h)
    high_g = jnp.where(upper, l2, p2)
    high_ge = jnp.where(upper, e2h, q2)

    prefix, wrapped = butterfly_states(
        pair_f, pair_g, e1h * q1, e2h * q2, seq_pos // 2, seq_count // 2, 2, seq_count
    )
    after_low = col(low_fe) * prefix + low_f
    before_high = col(high_ge) * wrapped + high_g
    own = (jnp.where(upper, after_low, prefix), jnp.where(upper, wrapped, before_high))
    other = jnp.stack([jnp.where(upper, prefix, after_low), jnp.where(upper, before_high, wrapped)])
    got_1, got_2 = lax.ppermute(other, "seq", pairs)

    def whole(own_half, got_half):
        return jnp.where(
            upper,
            jnp.concatenate([got_half, own_half], axis=0),
            jnp.concatenate([own_half, got_half], axis=0),
        )

    return whole(own[0], got_1), whole(own[1], got_2)


def on_device(
    inner_rows,
    gate_rows,
    input_proj,
    step_raw,
    decay_rate,
    skip_gain,
    conv_inner,
    conv_proj,
    norm_gain,
):
    tokens = inner_rows.shape[0]
    half_rows = tokens // 2
    head_count = step_raw.shape[1]
    inner_width = inner_rows.shape[1]
    group_count = input_proj.shape[1] // (2 * STATE)
    rim_rows = KERNEL - 1
    seq_count = lax.axis_size("seq")
    seq_pos = lax.axis_index("seq")
    is_last = seq_pos == seq_count - 1
    my_group = lax.axis_index("head") * head_count // GROUP_HEADS

    tails = (inner_rows[half_rows - rim_rows : half_rows], input_proj[half_rows - rim_rows : half_rows])
    heads = (inner_rows[tokens - rim_rows :], input_proj[tokens - rim_rows :])
    lead_first, high = exchange_rims(tails, heads, "seq")
    lead_second = tuple(jnp.where(is_last, t, h) for t, h in zip(tails, high))
    step_size = jax.nn.softplus(step_raw)
    causal = jnp.arange(half_rows)[:, None] >= jnp.arange(half_rows)[None, :]

    def conv(lead_rows, rows_in, taps):
        padded = jnp.concatenate([lead_rows, rows_in], axis=0).astype(jnp.float32)
        conv_sum = jnp.zeros((half_rows, rows_in.shape[1]), jnp.float32)
        for offset in range(KERNEL):
            conv_sum = conv_sum + taps[offset][None, :] * padded[offset : offset + half_rows]
        return jax.nn.silu(conv_sum).astype(jnp.bfloat16)

    def local_block(lead_rows, inner_in, proj_in, block_step):
        inner_out = conv(lead_rows[0], inner_in, conv_inner)
        proj_out = conv(lead_rows[1], proj_in, conv_proj)
        inner_conv = inner_out.reshape(half_rows, head_count, HEAD_SIZE)
        b_rows = lax.dynamic_slice_in_dim(proj_out, my_group * STATE, STATE, 1)
        c_rows = lax.dynamic_slice_in_dim(proj_out, (group_count + my_group) * STATE, STATE, 1)
        log_cum = jnp.cumsum(-block_step * decay_rate[None, :], axis=0)
        score_grid = jnp.dot(c_rows, b_rows.T, preferred_element_type=jnp.float32)
        log_gap = log_cum.T[:, :, None] - log_cum.T[:, None, :]
        decay_grid = jnp.where(causal[None], jnp.exp(jnp.where(causal[None], log_gap, 0.0)), 0.0)
        weights = (score_grid[None] * decay_grid * block_step.T[:, None, :]).astype(jnp.bfloat16)
        intra_out = jnp.einsum(
            "hts,shp->thp", weights, inner_conv, preferred_element_type=jnp.float32
        )
        tail_decay = jnp.exp(log_cum[-1][None, :] - log_cum) * block_step
        x_weighted = (inner_conv.astype(jnp.float32) * tail_decay[:, :, None]).astype(jnp.bfloat16)
        local_state = jnp.einsum(
            "shp,sn->hpn", x_weighted, b_rows, preferred_element_type=jnp.float32
        )
        partial_out = intra_out + skip_gain[None, :, None] * inner_conv.astype(jnp.float32)
        return (partial_out, log_cum, c_rows, (jnp.exp(log_cum[-1]), local_state))

    def finish_block(partial_out, log_cum, c_rows, state_in):
        inter_out = jnp.einsum(
            "tn,hpn->thp", c_rows.astype(jnp.float32), state_in, precision=lax.Precision.HIGHEST
        )
        total_out = partial_out + jnp.exp(log_cum)[:, :, None] * inter_out
        return total_out.reshape(half_rows, inner_width)

    first_out, first_cum, first_c, first_elem = local_block(
        lead_first, inner_rows[:half_rows], input_proj[:half_rows], step_size[:half_rows]
    )
    second_out, second_cum, second_c, second_elem = local_block(
        lead_second, inner_rows[half_rows:], input_proj[half_rows:], step_size[half_rows:]
    )
    first_in, second_in = block_states(
        first_elem[1], second_elem[1], first_cum[-1], second_cum[-1], seq_pos, seq_count
    )
    ssm_out = jnp.concatenate(
        [
            finish_block(first_out, first_cum, first_c, first_in),
            finish_block(second_out, second_cum, second_c, second_in),
        ],
        axis=0,
    )
    gated = ssm_out * jax.nn.silu(gate_rows.astype(jnp.float32))
    partial_sq = jnp.sum(gated * gated, axis=1)
    other_sq = partner(partial_sq, "head", 0)
    mean_sq = (partial_sq + other_sq) / (GROUP_HEADS * HEAD_SIZE)
    normed = gated * lax.rsqrt(mean_sq + 1e-05)[:, None] * norm_gain[None, :]
    return normed.astype(jnp.bfloat16)


def solution(mesh):
    in_specs = (
        P("seq", "head"),
        P("seq", "head"),
        P("seq", None),
        P("seq", "head"),
        P("head"),
        P("head"),
        P(None, "head"),
        P(),
        P("head"),
    )
    out_specs = P("seq", "head")
    return jax.shard_map(
        on_device, mesh=mesh, in_specs=in_specs, out_specs=out_specs, check_vma=False
    )
```
